32 devices in a mesh: scan: 8 (over y, x, core), head: 4 (over z).
Axes of the slice: x: 2, y: 2, z: 4, core: 2. Of those that a mesh axis runs over, the one named last changes fastest.
Arguments:
- stream: bfloat16 [8192, 1536], P('scan', 'head'), may hold values from -6 to 6
- w_xz: bfloat16 [2, 1536, 512], P(None, None, 'head'), may hold values from -0.15625 to 0.15625
- w_bc: bfloat16 [2, 1536, 256], replicated, may hold values from -0.15625 to 0.15625
- w_dt: bfloat16 [2, 1536, 4], P(None, None, 'head'), may hold values from -0.3125 to 0.3125
- dt_bias: float32 [2, 4], P(None, 'head'), may hold values from -2 to 0.5
- decay_rate: float32 [2, 4], P(None, 'head'), may hold values from 1.2207031e-06 to 0.04
- conv_x: float32 [2, 4, 256], P(None, None, 'head'), may hold values from -3 to 3
- conv_bc: float32 [2, 4, 256], replicated, may hold values from -3 to 3
- w_out: bfloat16 [2, 256, 1536], P(None, None, 'head'), may hold values from -0.375 to 0.375
Outputs:
- result: bfloat16 [8192, 1536], P('scan', 'head')
The draws below stay inside these ranges and needn't reach their ends.
All inputs are finite; a program needn't handle non-finite values.
Results may differ from the reference program's by a relative error of at most 0.015.
Values may be sent and summed in bfloat16 or wider, within the bound.
No kernel may reach another device: no remote copies, remote signals or barrier semaphores. Data moves between devices by JAX's collectives and lax.ppermute only.
A program may use at most 64 MiB of HBM per device.

```python
import math
import jax
import jax.numpy as jnp
from jax import lax

D = 1536
HEAD_DIM = 64
STATE = 128
CONV = 4
BLOCK = 256
TOK_DEV = 1024
HEADS = 4
INNER = 256
FRAMES = 8
SEQ = 8192


def draw_stream(key, part):
    key_mean = jax.random.fold_in(key, 11)
    key_noise = jax.random.fold_in(key, 12)
    frame_mean = jnp.clip(jax.random.normal(key_mean, (FRAMES, 1, D), jnp.float32), -2.5, 2.5)
    noise = jnp.clip(jax.random.normal(key_noise, (FRAMES, TOK_DEV, D), jnp.float32), -3.0, 3.0)
    values = frame_mean + noise
    return values.reshape(SEQ, D).astype(jnp.bfloat16)


def block_scale(stream_key, extent, cuts, low, top_value):
    def one(dim, blocks):
        draws = jax.random.uniform(jax.random.fold_in(jax.random.fold_in(stream_key, 6), dim), (blocks,), jnp.float32, low / len(cuts), top_value / len(cuts))
        return jnp.repeat(jnp.exp(draws), extent[dim] // blocks).reshape((-1,) + (1,) * (len(extent) - dim - 1))

    factor_of = one(*cuts[0])
    for cut in cuts[1:]:
        factor_of = factor_of * one(*cut)
    return factor_of


def normal_values(stream_key, dims, scale, limit, cuts=(), kind=jnp.bfloat16):
    array = jax.random.normal(stream_key, dims, jnp.float32) * scale
    if len(cuts) > 0:
        array = block_scale(stream_key, dims, cuts, -0.22, 0.18) * array
    return jnp.clip(array, min=-limit, max=limit).astype(kind)


def setup_inputs(seed: int = 0) -> dict:
    keys = jax.random.split(jax.random.key(seed), 10)
    return {
        "stream": draw_stream(jax.random.fold_in(keys[9], 71), 0),
        "w_xz": normal_values(keys[1], (2, D, 2 * INNER), D ** -0.5, 0.15625, ((2, 4),)),
        "w_bc": normal_values(keys[2], (2, D, 2 * STATE), D ** -0.5, 0.15625),
        "w_dt": normal_values(keys[3], (2, D, HEADS), (D // 4) ** -0.5, 0.3125, ((2, 4),)),
        "dt_bias": jnp.clip(-2.0 + 2.5 * jax.random.uniform(keys[4], (2, HEADS), jnp.float32) ** block_scale(keys[4], (2, HEADS), ((1, 4),), -0.2, 0.2), -2.0, 0.5),
        "decay_rate": jnp.clip(jnp.exp(math.log(0.04) - 10.3972077 * jax.random.uniform(keys[5], (2, HEADS), jnp.float32) ** block_scale(keys[5], (2, HEADS), ((1, 4),), -0.2, 0.2)), 1.220703097715159e-06, 0.04),
        "conv_x": normal_values(keys[6], (2, CONV, INNER), 0.5, 3.0, ((2, 4),), jnp.float32),
        "conv_bc": normal_values(keys[7], (2, CONV, 2 * STATE), 0.5, 3.0, (), jnp.float32),
        "w_out": normal_values(keys[8], (2, INNER, D), INNER ** -0.5, 0.375, ((2, 4),)),
    }


EPSILON = 1e-05

def causal_conv(pre_conv, kernel):
    padded = jnp.concatenate([jnp.zeros((CONV - 1, pre_conv.shape[1]), pre_conv.dtype), pre_conv], axis=0).astype(jnp.float32)
    length = pre_conv.shape[0]
    summed = jnp.zeros(pre_conv.shape, jnp.float32)
    for offset in range(CONV):
        summed = summed + kernel[offset] * padded[offset:offset + length]
    return jax.nn.silu(summed).astype(jnp.bfloat16)

def head_scan(gram_mat, c_blocks, b_blocks, x_head, cum_head, dt_head):
    positions = jnp.arange(BLOCK)
    causal = positions[:, None] >= positions[None, :]
    spread = cum_head[:, :, None] - cum_head[:, None, :]
    weights = (gram_mat * jnp.exp(jnp.where(causal[None], spread, -jnp.inf)) * dt_head[:, None, :]).astype(jnp.bfloat16)
    inside = jnp.einsum('kqs,ksp->kqp', weights.astype(jnp.float32), x_head.astype(jnp.float32))
    to_end = jnp.exp(cum_head[:, -1:] - cum_head) * dt_head
    scaled = (x_head.astype(jnp.float32) * to_end[:, :, None]).astype(jnp.bfloat16)
    block_ends = jnp.einsum('ksp,ksn->kpn', scaled.astype(jnp.float32), b_blocks)

    def advance(running, inputs):
        block_decay, block_end = inputs
        return (jnp.exp(block_decay) * running + block_end, running)
    _, starts = lax.scan(advance, jnp.zeros((HEAD_DIM, STATE), jnp.float32), (cum_head[:, -1], block_ends))
    carried = jnp.einsum('kqn,kpn->kqp', c_blocks, starts, precision=lax.Precision.HIGHEST)
    return inside + jnp.exp(cum_head)[:, :, None] * carried

def mix_layer(stream, w_xz, w_bc, w_dt, dt_bias, decay_rate, conv_x, conv_bc, w_out):
    wide_in = stream.astype(jnp.float32)
    row_scale = lax.rsqrt(lax.optimization_barrier(jnp.mean(wide_in * wide_in, axis=1, keepdims=True)) + EPSILON)
    proj_xz = (jnp.dot(stream, w_xz, preferred_element_type=jnp.float32) * row_scale).astype(jnp.bfloat16)
    proj_bc = (jnp.dot(stream, w_bc, preferred_element_type=jnp.float32) * row_scale).astype(jnp.bfloat16)
    dt_raw = jnp.dot(stream, w_dt, preferred_element_type=jnp.float32) * row_scale
    split_xz = proj_xz.reshape(SEQ, HEADS, 2, HEAD_DIM)
    inputs_x = causal_conv(split_xz[:, :, 0, :].reshape(SEQ, INNER), conv_x)
    gate_vals = split_xz[:, :, 1, :].astype(jnp.float32)
    conv_out = causal_conv(proj_bc, conv_bc)
    block_count = SEQ // BLOCK
    b_blocks = conv_out[:, :STATE].astype(jnp.float32).reshape(block_count, BLOCK, STATE)
    c_blocks = conv_out[:, STATE:].astype(jnp.float32).reshape(block_count, BLOCK, STATE)
    gram_mat = jnp.einsum('kqn,ksn->kqs', c_blocks, b_blocks)
    step_dt = jax.nn.softplus(dt_raw + dt_bias)
    cum_decay = jnp.cumsum((-step_dt * decay_rate).reshape(block_count, BLOCK, HEADS), axis=1)
    x_heads = jnp.moveaxis(inputs_x.reshape(block_count, BLOCK, HEADS, HEAD_DIM), 2, 0)
    cum_heads = jnp.moveaxis(cum_decay, 2, 0)
    dt_heads = jnp.moveaxis(step_dt.reshape(block_count, BLOCK, HEADS), 2, 0)

    def per_head(packed):
        return head_scan(gram_mat, c_blocks, b_blocks, packed[0], packed[1], packed[2])
    outputs = lax.map(per_head, (x_heads, cum_heads, dt_heads))
    mixed_out = jnp.moveaxis(outputs, 0, 2).reshape(SEQ, HEADS, HEAD_DIM)
    gated_out = mixed_out * jax.nn.silu(gate_vals)
    normed = (gated_out * lax.rsqrt(lax.optimization_barrier(jnp.mean(gated_out * gated_out, axis=2, keepdims=True)) + EPSILON)).astype(jnp.bfloat16).reshape(SEQ, INNER)
    return (wide_in + jnp.dot(normed, w_out, preferred_element_type=jnp.float32)).astype(jnp.bfloat16)

def reference(stream, w_xz, w_bc, w_dt, dt_bias, decay_rate, conv_x, conv_bc, w_out):
    raster_out = mix_layer(stream, w_xz[0], w_bc[0], w_dt[0], dt_bias[0], decay_rate[0], conv_x[0], conv_bc[0], w_out[0])
    reordered = jnp.transpose(raster_out.reshape(FRAMES, TOK_DEV, D), (1, 0, 2)).reshape(SEQ, D)
    return mix_layer(reordered, w_xz[1], w_bc[1], w_dt[1], dt_bias[1], decay_rate[1], conv_x[1], conv_bc[1], w_out[1])
```

```python
import jax
import jax.numpy as jnp
from jax import lax
from jax.sharding import PartitionSpec as P

BLOCK = 256


EPSILON = 1e-05


def from_behind(shard, axis, by):
    devices = lax.axis_size(axis)
    pairs = [(i, i + by) for i in range(devices) if 0 <= i + by < devices]
    return lax.ppermute(shard, axis, pairs)


def carried_in(decay, state, axis):
    place = lax.axis_index(axis)
    members = lax.axis_size(axis)
    heads, rows, cols = state.shape
    decay_row = jnp.zeros((1, cols), jnp.float32).at[0, :heads].set(decay)
    packed = jnp.concatenate([state.reshape(heads * rows, cols), decay_row], axis=0)
    gathered = lax.all_gather(packed.astype(jnp.bfloat16), axis).astype(jnp.float32)
    states = gathered[:, : heads * rows].reshape(members, heads, rows, cols)
    decays = gathered[:, heads * rows, :heads]
    order = jnp.arange(members)
    between = (order[:, None] < order[None, :]) & (order[None, :] < place)
    span = jnp.sum(jnp.where(between[:, :, None], decays[None, :, :], 0.0), axis=1)
    scale = jnp.where((order < place)[:, None], jnp.exp(span), 0.0)
    return jnp.sum(scale[:, :, None, None] * states, axis=0)


def causal_conv(rim_rows, pre_conv, kernel):
    padded = jnp.concatenate([rim_rows, pre_conv], axis=0).astype(jnp.float32)
    length = pre_conv.shape[0]
    summed = jnp.zeros(pre_conv.shape, jnp.float32)
    for offset in range(kernel.shape[0]):
        summed = summed + kernel[offset] * padded[offset : offset + length]
    return jax.nn.silu(summed).astype(jnp.bfloat16)


def mix_layer(stream, w_xz, w_bc, w_dt, dt_bias, decay_rate, conv_x, conv_bc, w_out):
    length = stream.shape[0]
    feature_count = stream.shape[1] * lax.axis_size("head")
    heads_here = w_dt.shape[1]
    head_dim = w_xz.shape[1] // (2 * heads_here)
    state_dim = w_bc.shape[1] // 2
    taps = conv_x.shape[0]
    portion = lax.all_gather(stream, "head", axis=1, tiled=True)

    def project(weight):
        return jnp.dot(portion, weight, preferred_element_type=jnp.float32)

    wide_piece = portion.astype(jnp.float32)
    row_scale = lax.rsqrt(jnp.sum(wide_piece * wide_piece, axis=1) / feature_count + EPSILON)[
        :, None
    ]
    proj_xz = (
        (project(w_xz) * row_scale).astype(jnp.bfloat16).reshape(length, heads_here, 2, head_dim)
    )
    proj_bc = (project(w_bc) * row_scale).astype(jnp.bfloat16)
    dt_raw = project(w_dt) * row_scale
    pre_x = proj_xz[:, :, 0, :].reshape(length, heads_here * head_dim)
    gate_vals = proj_xz[:, :, 1, :].astype(jnp.float32)
    rim_x, rim_bc = from_behind(
        (pre_x[length - taps + 1 :], proj_bc[length - taps + 1 :]), "scan", 1
    )
    inputs_x = causal_conv(rim_x, pre_x, conv_x)
    conv_out = causal_conv(rim_bc, proj_bc, conv_bc)
    block_count = length // BLOCK
    b_blocks = conv_out[:, :state_dim].reshape(block_count, BLOCK, state_dim)
    c_blocks = conv_out[:, state_dim:].reshape(block_count, BLOCK, state_dim)
    gram_mat = jnp.einsum("kqn,ksn->kqs", c_blocks, b_blocks, preferred_element_type=jnp.float32)
    step_dt = jax.nn.softplus(dt_raw + dt_bias)
    cum_decay = jnp.cumsum((-step_dt * decay_rate).reshape(block_count, BLOCK, heads_here), axis=1)
    dt_blocks = step_dt.reshape(block_count, BLOCK, heads_here)
    x_blocks = inputs_x.reshape(block_count, BLOCK, heads_here, head_dim)
    positions = jnp.arange(BLOCK)
    causal = positions[:, None] >= positions[None, :]
    cum_heads = jnp.moveaxis(cum_decay, 2, 1)
    dt_heads = jnp.moveaxis(dt_blocks, 2, 1)
    spread = cum_heads[:, :, :, None] - cum_heads[:, :, None, :]
    weights = (
        gram_mat[:, None]
        * jnp.exp(jnp.where(causal[None, None], spread, -jnp.inf))
        * dt_heads[:, :, None, :]
    ).astype(jnp.bfloat16)
    inside = jnp.einsum("khqs,kshp->kqhp", weights, x_blocks, preferred_element_type=jnp.float32)
    to_end = jnp.exp(cum_decay[:, -1:, :] - cum_decay) * dt_blocks
    scaled = (x_blocks.astype(jnp.float32) * to_end[:, :, :, None]).astype(jnp.bfloat16)
    block_ends = jnp.einsum("kqhp,kqn->khpn", scaled, b_blocks, preferred_element_type=jnp.float32)
    block_decay = cum_decay[:, -1, :]

    def advance(running, inputs):
        return (jnp.exp(inputs[0])[:, None, None] * running + inputs[1], running)

    local_end, starts_local = lax.scan(
        advance,
        jnp.zeros((heads_here, head_dim, state_dim), jnp.float32),
        (block_decay, block_ends),
    )
    device_decay = jnp.sum(block_decay, axis=0)
    incoming = carried_in(device_decay, local_end, "scan")
    prior_decay = jnp.concatenate(
        [jnp.zeros((1, heads_here), jnp.float32), jnp.cumsum(block_decay, axis=0)[:-1]], axis=0
    )
    starts = jnp.exp(prior_decay)[:, :, None, None] * incoming[None] + starts_local
    carried = jnp.einsum(
        "kqn,khpn->kqhp", c_blocks.astype(jnp.float32), starts, precision=lax.Precision.HIGHEST
    )
    mixed_out = inside + jnp.exp(cum_decay)[:, :, :, None] * carried
    gated_out = mixed_out.reshape(length, heads_here, head_dim) * jax.nn.silu(gate_vals)
    normed = (
        (gated_out * lax.rsqrt(jnp.mean(gated_out * gated_out, axis=2, keepdims=True) + EPSILON))
        .astype(jnp.bfloat16)
        .reshape(length, heads_here * head_dim)
    )
    summed_out = jnp.dot(
        lax.all_gather(normed, "head", axis=1, tiled=True),
        w_out,
        preferred_element_type=jnp.float32,
    )
    return (stream.astype(jnp.float32) + summed_out).astype(jnp.bfloat16)


def local(stream, w_xz, w_bc, w_dt, dt_bias, decay_rate, conv_x, conv_bc, w_out):
    raster_out = mix_layer(
        stream,
        w_xz[0],
        w_bc[0],
        w_dt[0],
        dt_bias[0],
        decay_rate[0],
        conv_x[0],
        conv_bc[0],
        w_out[0],
    )
    members = lax.axis_size("scan")
    length = raster_out.shape[0]
    columns = raster_out.shape[1]
    grouped = raster_out.reshape(members, length // members, 1, columns)
    exchanged = lax.all_to_all(grouped, "scan", split_axis=0, concat_axis=2, tiled=True)
    reordered = exchanged.reshape(length, columns)
    return mix_layer(
        reordered,
        w_xz[1],
        w_bc[1],
        w_dt[1],
        dt_bias[1],
        decay_rate[1],
        conv_x[1],
        conv_bc[1],
        w_out[1],
    )


def solution(mesh):
    placed = (
        P("scan", "head"),
        P(None, None, "head"),
        P(),
        P(None, None, "head"),
        P(None, "head"),
        P(None, "head"),
        P(None, None, "head"),
        P(),
        P(None, None, "head"),
    )
    return jax.shard_map(
        local, mesh=mesh, in_specs=placed, out_specs=P("scan", "head"), check_vma=False
    )
```

```python
import jax
import jax.numpy as jnp
from jax import lax
from jax.sharding import PartitionSpec as P

BLOCK = 256


EPSILON = 1e-05


def from_behind(shard, axis, by):
    devices = lax.axis_size(axis)
    pairs = [(i, i + by) for i in range(devices) if 0 <= i + by < devices]
    return lax.ppermute(shard, axis, pairs)


def weighted_prefix(states, decays, place):
    order = jnp.arange(states.shape[0])
    between = (order[:, None] < order[None, :]) & (order[None, :] < place)
    span = jnp.sum(jnp.where(between[:, :, None], decays[None, :, :], 0.0), axis=1)
    scale = jnp.where((order < place)[:, None], jnp.exp(span), 0.0)
    return jnp.sum(scale[:, :, None, None] * states, axis=0)


def pack_state(decay, state, kind):
    heads, rows, cols = state.shape
    decay_row = jnp.zeros((1, cols), jnp.float32).at[0, :heads].set(decay)
    return jnp.concatenate([state.reshape(heads * rows, cols), decay_row], axis=0).astype(kind)


def unpack_state(gathered, heads, rows):
    members, _, cols = gathered.shape
    gathered = gathered.astype(jnp.float32)
    states = gathered[:, : heads * rows].reshape(members, heads, rows, cols)
    return states, gathered[:, heads * rows, :heads]


def carried_in(decay, state, axis):
    heads, rows, _ = state.shape
    gathered = lax.all_gather(pack_state(decay, state, jnp.bfloat16), axis)
    states, decays = unpack_state(gathered, heads, rows)
    return weighted_prefix(states, decays, lax.axis_index(axis))


def carried_in_two_level(decay, state):
    heads, rows, _ = state.shape
    inner = lax.axis_size("head")
    spot = lax.axis_index("head")
    states, decays = unpack_state(
        lax.all_gather(pack_state(decay, state, jnp.float32), "head"), heads, rows
    )
    before_here = weighted_prefix(states, decays, spot)
    group_total = weighted_prefix(states, decays, inner)
    group_decay = jnp.sum(decays, axis=0)
    group_states, group_decays = unpack_state(
        lax.all_gather(pack_state(group_decay, group_total, jnp.float32), "scan"), heads, rows
    )
    entering_group = weighted_prefix(group_states, group_decays, lax.axis_index("scan"))
    lead = jnp.sum(jnp.where((jnp.arange(inner) < spot)[:, None], decays, 0.0), axis=0)
    return jnp.exp(lead)[:, None, None] * entering_group + before_here


def causal_conv(rim_rows, pre_conv, kernel):
    padded = jnp.concatenate([rim_rows, pre_conv], axis=0).astype(jnp.float32)
    length = pre_conv.shape[0]
    summed = jnp.zeros(pre_conv.shape, jnp.float32)
    for offset in range(kernel.shape[0]):
        summed = summed + kernel[offset] * padded[offset : offset + length]
    return jax.nn.silu(summed).astype(jnp.bfloat16)


def mix_core(portion, w_xz, w_bc, w_dt, dt_bias, decay_rate, conv_x, conv_bc, rim_of, carry_of):
    length = portion.shape[0]
    feature_count = portion.shape[1]
    heads_here = w_dt.shape[1]
    head_dim = w_xz.shape[1] // (2 * heads_here)
    state_dim = w_bc.shape[1] // 2
    taps = conv_x.shape[0]

    def project(weight):
        return jnp.dot(portion, weight, preferred_element_type=jnp.float32)

    wide_piece = portion.astype(jnp.float32)
    row_scale = lax.rsqrt(jnp.sum(wide_piece * wide_piece, axis=1) / feature_count + EPSILON)[
        :, None
    ]
    proj_xz = (
        (project(w_xz) * row_scale).astype(jnp.bfloat16).reshape(length, heads_here, 2, head_dim)
    )
    proj_bc = (project(w_bc) * row_scale).astype(jnp.bfloat16)
    dt_raw = project(w_dt) * row_scale
    pre_x = proj_xz[:, :, 0, :].reshape(length, heads_here * head_dim)
    gate_vals = proj_xz[:, :, 1, :].astype(jnp.float32)
    rim_x, rim_bc = rim_of((pre_x[length - taps + 1 :], proj_bc[length - taps + 1 :]))
    inputs_x = causal_conv(rim_x, pre_x, conv_x)
    conv_out = causal_conv(rim_bc, proj_bc, conv_bc)
    block_count = length // BLOCK
    b_blocks = conv_out[:, :state_dim].reshape(block_count, BLOCK, state_dim)
    c_blocks = conv_out[:, state_dim:].reshape(block_count, BLOCK, state_dim)
    gram_mat = jnp.einsum("kqn,ksn->kqs", c_blocks, b_blocks, preferred_element_type=jnp.float32)
    step_dt = jax.nn.softplus(dt_raw + dt_bias)
    cum_decay = jnp.cumsum((-step_dt * decay_rate).reshape(block_count, BLOCK, heads_here), axis=1)
    dt_blocks = step_dt.reshape(block_count, BLOCK, heads_here)
    x_blocks = inputs_x.reshape(block_count, BLOCK, heads_here, head_dim)
    positions = jnp.arange(BLOCK)
    causal = positions[:, None] >= positions[None, :]
    cum_heads = jnp.moveaxis(cum_decay, 2, 1)
    dt_heads = jnp.moveaxis(dt_blocks, 2, 1)
    spread = cum_heads[:, :, :, None] - cum_heads[:, :, None, :]
    weights = (
        gram_mat[:, None]
        * jnp.exp(jnp.where(causal[None, None], spread, -jnp.inf))
        * dt_heads[:, :, None, :]
    ).astype(jnp.bfloat16)
    inside = jnp.einsum("khqs,kshp->kqhp", weights, x_blocks, preferred_element_type=jnp.float32)
    to_end = jnp.exp(cum_decay[:, -1:, :] - cum_decay) * dt_blocks
    scaled = (x_blocks.astype(jnp.float32) * to_end[:, :, :, None]).astype(jnp.bfloat16)
    block_ends = jnp.einsum("kqhp,kqn->khpn", scaled, b_blocks, preferred_element_type=jnp.float32)
    block_decay = cum_decay[:, -1, :]

    def advance(running, inputs):
        return (jnp.exp(inputs[0])[:, None, None] * running + inputs[1], running)

    local_end, starts_local = lax.scan(
        advance,
        jnp.zeros((heads_here, head_dim, state_dim), jnp.float32),
        (block_decay, block_ends),
    )
    device_decay = jnp.sum(block_decay, axis=0)
    incoming = carry_of(device_decay, local_end)
    prior_decay = jnp.concatenate(
        [jnp.zeros((1, heads_here), jnp.float32), jnp.cumsum(block_decay, axis=0)[:-1]], axis=0
    )
    starts = jnp.exp(prior_decay)[:, :, None, None] * incoming[None] + starts_local
    carried = jnp.einsum(
        "kqn,khpn->kqhp", c_blocks.astype(jnp.float32), starts, precision=lax.Precision.HIGHEST
    )
    mixed_out = inside + jnp.exp(cum_decay)[:, :, :, None] * carried
    gated_out = mixed_out.reshape(length, heads_here, head_dim) * jax.nn.silu(gate_vals)
    return (
        (gated_out * lax.rsqrt(jnp.mean(gated_out * gated_out, axis=2, keepdims=True) + EPSILON))
        .astype(jnp.bfloat16)
        .reshape(length, heads_here * head_dim)
    )


def mix_layer(stream, w_xz, w_bc, w_dt, dt_bias, decay_rate, conv_x, conv_bc, w_out):
    portion = lax.all_gather(stream, "head", axis=1, tiled=True)
    normed = mix_core(
        portion,
        w_xz,
        w_bc,
        w_dt,
        dt_bias,
        decay_rate,
        conv_x,
        conv_bc,
        lambda rims: from_behind(rims, "scan", 1),
        lambda decay, state: carried_in(decay, state, "scan"),
    )
    summed_out = jnp.dot(
        lax.all_gather(normed, "head", axis=1, tiled=True),
        w_out,
        preferred_element_type=jnp.float32,
    )
    return (stream.astype(jnp.float32) + summed_out).astype(jnp.bfloat16)


def split_local(stream, w_xz, w_bc, w_dt, dt_bias, decay_rate, conv_x, conv_bc, w_out):
    layer = lambda u, l: mix_layer(
        u, w_xz[l], w_bc[l], w_dt[l], dt_bias[l], decay_rate[l], conv_x[l], conv_bc[l], w_out[l]
    )
    raster_out = layer(stream, 0)
    members = lax.axis_size("scan")
    length = raster_out.shape[0]
    columns = raster_out.shape[1]
    grouped = raster_out.reshape(members, length // members, 1, columns)
    exchanged = lax.all_to_all(grouped, "scan", split_axis=0, concat_axis=2, tiled=True)
    return layer(exchanged.reshape(length, columns), 1)


def chained_rims(rims):
    count = lax.axis_size("scan") * lax.axis_size("head")
    pairs = [(i, i + 1) for i in range(count - 1)]
    return lax.ppermute(rims, ("scan", "head"), pairs)


def gather_weights(w_xz, w_dt, w_out, layer):
    inner = lax.axis_size("head")
    features = w_xz.shape[1]
    xz_cols = w_xz.shape[2]
    dt_cols = w_dt.shape[2]
    rows_out, cols_out = w_out.shape[1], w_out.shape[2]
    out_as_rows = w_out[layer].reshape(features, rows_out * cols_out // features)
    packed = jnp.concatenate([w_xz[layer], w_dt[layer], out_as_rows], axis=1)
    gathered = lax.all_gather(packed, "head")
    xz_full = jnp.moveaxis(gathered[:, :, :xz_cols], 0, 1).reshape(features, inner * xz_cols)
    dt_full = jnp.moveaxis(gathered[:, :, xz_cols : xz_cols + dt_cols], 0, 1).reshape(
        features, inner * dt_cols
    )
    out_pieces = gathered[:, :, xz_cols + dt_cols :].reshape(inner, rows_out, cols_out)
    out_full = jnp.moveaxis(out_pieces, 0, 1).reshape(rows_out, inner * cols_out)
    return xz_full, dt_full, out_full


def gather_small(dt_bias, decay_rate, conv_x):
    inner = lax.axis_size("head")
    layers, taps, width = conv_x.shape
    heads = dt_bias.shape[1]
    rows = jnp.zeros((layers, 2, width), jnp.float32)
    rows = rows.at[:, 0, :heads].set(dt_bias).at[:, 1, :heads].set(decay_rate)
    gathered = lax.all_gather(jnp.concatenate([conv_x, rows], axis=1), "head")
    conv_full = jnp.moveaxis(gathered[:, :, :taps], 0, 2).reshape(layers, taps, inner * width)
    bias_full = jnp.moveaxis(gathered[:, :, taps, :heads], 0, 1).reshape(layers, inner * heads)
    rate_full = jnp.moveaxis(gathered[:, :, taps + 1, :heads], 0, 1).reshape(layers, inner * heads)
    return bias_full, rate_full, conv_full


def block_layer(u, weights, w_bc, conv_bc, dt_bias, decay_rate, conv_x):
    xz_full, dt_full, out_full = weights
    normed = mix_core(
        u, xz_full, w_bc, dt_full, dt_bias, decay_rate, conv_x, conv_bc, chained_rims,
        carried_in_two_level,
    )
    summed_out = jnp.dot(normed, out_full, preferred_element_type=jnp.float32)
    return (u.astype(jnp.float32) + summed_out).astype(jnp.bfloat16)


def block_local(stream, w_xz, w_bc, w_dt, dt_bias, decay_rate, conv_x, conv_bc, w_out):
    inner = lax.axis_size("head")
    frames = lax.axis_size("scan")
    length, piece = stream.shape
    chunk = length // inner
    span = chunk // frames
    bias_full, rate_full, conv_full = gather_small(dt_bias, decay_rate, conv_x)
    first = gather_weights(w_xz, w_dt, w_out, 0)
    second = gather_weights(w_xz, w_dt, w_out, 1)
    spread = lax.all_to_all(stream.reshape(inner, chunk, piece), "head", 0, 0)
    u0 = jnp.moveaxis(spread, 0, 1).reshape(chunk, inner * piece)
    v0 = block_layer(u0, first, w_bc[0], conv_bc[0], bias_full[0], rate_full[0], conv_full[0])
    columns = v0.shape[1]
    step = lax.all_to_all(v0.reshape(frames // inner, inner, span, columns), "head", 1, 1)
    by_scan = jnp.moveaxis(step, 0, 1).reshape(frames, span, columns)
    landed = lax.all_to_all(by_scan, "scan", 0, 0)
    u1 = jnp.moveaxis(landed, 0, 1).reshape(chunk, columns)
    v1 = block_layer(u1, second, w_bc[1], conv_bc[1], bias_full[1], rate_full[1], conv_full[1])
    back = lax.all_to_all(v1.reshape(chunk, inner, piece), "head", 1, 0)
    return back.reshape(length, piece)


def fits_blocks(mesh, stream_rows):
    inner = mesh.shape["head"]
    frames = mesh.shape["scan"]
    length = stream_rows // frames
    chunk = length // inner
    return (
        length % inner == 0
        and chunk % BLOCK == 0
        and chunk % frames == 0
        and frames % inner == 0
    )


def solution(mesh):
    placed = (
        P("scan", "head"),
        P(None, None, "head"),
        P(),
        P(None, None, "head"),
        P(None, "head"),
        P(None, "head"),
        P(None, None, "head"),
        P(),
        P(None, None, "head"),
    )

    def run(stream, *rest):
        local = block_local if fits_blocks(mesh, stream.shape[0]) else split_local
        inner = jax.shard_map(
            local, mesh=mesh, in_specs=placed, out_specs=P("scan", "head"), check_vma=False
        )
        return inner(stream, *rest)

    return run
```

```python
import jax
import jax.numpy as jnp
from jax import lax
from jax.sharding import PartitionSpec as P

BLOCK = 256


EPSILON = 1e-05


def from_behind(shard, axis, by):
    devices = lax.axis_size(axis)
    pairs = [(i, i + by) for i in range(devices) if 0 <= i + by < devices]
    return lax.ppermute(shard, axis, pairs)


def carried_in(decay, state, axis):
    place = lax.axis_index(axis)
    members = lax.axis_size(axis)
    heads, rows, cols = state.shape
    decay_row = jnp.zeros((1, cols), jnp.float32).at[0, :heads].set(decay)
    packed = jnp.concatenate([state.reshape(heads * rows, cols), decay_row], axis=0)
    gathered = lax.all_gather(packed.astype(jnp.bfloat16), axis).astype(jnp.float32)
    states = gathered[:, : heads * rows].reshape(members, heads, rows, cols)
    decays = gathered[:, heads * rows, :heads]
    order = jnp.arange(members)
    between = (order[:, None] < order[None, :]) & (order[None, :] < place)
    span = jnp.sum(jnp.where(between[:, :, None], decays[None, :, :], 0.0), axis=1)
    scale = jnp.where((order < place)[:, None], jnp.exp(span), 0.0)
    return jnp.sum(scale[:, :, None, None] * states, axis=0)


def causal_conv(rim_rows, pre_conv, kernel):
    padded = jnp.concatenate([rim_rows, pre_conv], axis=0).astype(jnp.float32)
    length = pre_conv.shape[0]
    summed = jnp.zeros(pre_conv.shape, jnp.float32)
    for offset in range(kernel.shape[0]):
        summed = summed + kernel[offset] * padded[offset : offset + length]
    return jax.nn.silu(summed).astype(jnp.bfloat16)


def split_pair(values):
    high = values.astype(jnp.bfloat16)
    low = (values - high.astype(jnp.float32)).astype(jnp.bfloat16)
    return high, low


def regroup(w_xz, w_dt):
    inner = lax.axis_size("head")
    layers, features, _ = w_xz.shape
    packed = jnp.concatenate([w_xz, w_dt], axis=2)
    split = packed.reshape(layers, inner, features // inner, packed.shape[2])
    return lax.all_to_all(split, "head", 1, 1)


def mix_layer(stream, regrouped, xz_cols, w_bc, dt_bias, decay_rate, conv_x, conv_bc, w_out):
    length, piece = stream.shape
    inner = lax.axis_size("head")
    spot = lax.axis_index("head")
    feature_count = piece * inner
    heads_here = regrouped.shape[2] - xz_cols
    head_dim = xz_cols // (2 * heads_here)
    state_dim = w_bc.shape[1] // 2
    taps = conv_x.shape[0]
    partial = jnp.einsum("tf,gfc->tgc", stream, regrouped, preferred_element_type=jnp.float32)
    rows_bc = lax.dynamic_slice_in_dim(w_bc, spot * piece, piece, 0)
    partial_bc = jnp.dot(stream, rows_bc, preferred_element_type=jnp.float32)
    wide_piece = stream.astype(jnp.float32)
    exact = jnp.concatenate(
        [
            jnp.sum(wide_piece * wide_piece, axis=1, keepdims=True),
            partial[:, :, xz_cols:].reshape(length, inner * heads_here),
        ],
        axis=1,
    )
    high, low = split_pair(exact)
    slots = jnp.zeros((length, inner, 2, exact.shape[1]), jnp.bfloat16)
    slots = lax.dynamic_update_slice_in_dim(
        slots, jnp.stack([high, low], axis=1)[:, None], spot, 1
    )
    summed_xz = lax.psum_scatter(
        partial[:, :, :xz_cols].astype(jnp.bfloat16), "head", scatter_dimension=1
    )
    reduced = lax.psum(
        jnp.concatenate([partial_bc.astype(jnp.bfloat16), slots.reshape(length, -1)], axis=1),
        "head",
    )
    summed_bc = reduced[:, : 2 * state_dim].astype(jnp.float32)
    totals = jnp.sum(
        reduced[:, 2 * state_dim :].astype(jnp.float32).reshape(length, inner * 2, -1), axis=1
    )
    row_scale = lax.rsqrt(totals[:, :1] / feature_count + EPSILON)
    dt_sum = lax.dynamic_index_in_dim(
        totals[:, 1:].reshape(length, inner, heads_here), spot, 1, keepdims=False
    )
    proj_xz = (
        (summed_xz.astype(jnp.float32) * row_scale)
        .astype(jnp.bfloat16)
        .reshape(length, heads_here, 2, head_dim)
    )
    proj_bc = (summed_bc * row_scale).astype(jnp.bfloat16)
    dt_raw = dt_sum * row_scale
    pre_x = proj_xz[:, :, 0, :].reshape(length, heads_here * head_dim)
    gate_vals = proj_xz[:, :, 1, :].astype(jnp.float32)
    rim_x, rim_bc = from_behind(
        (pre_x[length - taps + 1 :], proj_bc[length - taps + 1 :]), "scan", 1
    )
    inputs_x = causal_conv(rim_x, pre_x, conv_x)
    conv_out = causal_conv(rim_bc, proj_bc, conv_bc)
    block_count = length // BLOCK
    b_blocks = conv_out[:, :state_dim].reshape(block_count, BLOCK, state_dim)
    c_blocks = conv_out[:, state_dim:].reshape(block_count, BLOCK, state_dim)
    gram_mat = jnp.einsum("kqn,ksn->kqs", c_blocks, b_blocks, preferred_element_type=jnp.float32)
    step_dt = jax.nn.softplus(dt_raw + dt_bias)
    cum_decay = jnp.cumsum((-step_dt * decay_rate).reshape(block_count, BLOCK, heads_here), axis=1)
    dt_blocks = step_dt.reshape(block_count, BLOCK, heads_here)
    x_blocks = inputs_x.reshape(block_count, BLOCK, heads_here, head_dim)
    positions = jnp.arange(BLOCK)
    causal = positions[:, None] >= positions[None, :]
    cum_heads = jnp.moveaxis(cum_decay, 2, 1)
    dt_heads = jnp.moveaxis(dt_blocks, 2, 1)
    spread = cum_heads[:, :, :, None] - cum_heads[:, :, None, :]
    weights = (
        gram_mat[:, None]
        * jnp.exp(jnp.where(causal[None, None], spread, -jnp.inf))
        * dt_heads[:, :, None, :]
    ).astype(jnp.bfloat16)
    inside = jnp.einsum("khqs,kshp->kqhp", weights, x_blocks, preferred_element_type=jnp.float32)
    to_end = jnp.exp(cum_decay[:, -1:, :] - cum_decay) * dt_blocks
    scaled = (x_blocks.astype(jnp.float32) * to_end[:, :, :, None]).astype(jnp.bfloat16)
    block_ends = jnp.einsum("kqhp,kqn->khpn", scaled, b_blocks, preferred_element_type=jnp.float32)
    block_decay = cum_decay[:, -1, :]

    def advance(running, inputs):
        return (jnp.exp(inputs[0])[:, None, None] * running + inputs[1], running)

    local_end, starts_local = lax.scan(
        advance,
        jnp.zeros((heads_here, head_dim, state_dim), jnp.float32),
        (block_decay, block_ends),
    )
    device_decay = jnp.sum(block_decay, axis=0)
    incoming = carried_in(device_decay, local_end, "scan")
    prior_decay = jnp.concatenate(
        [jnp.zeros((1, heads_here), jnp.float32), jnp.cumsum(block_decay, axis=0)[:-1]], axis=0
    )
    starts = jnp.exp(prior_decay)[:, :, None, None] * incoming[None] + starts_local
    carried = jnp.einsum(
        "kqn,khpn->kqhp", c_blocks.astype(jnp.float32), starts, precision=lax.Precision.HIGHEST
    )
    mixed_out = inside + jnp.exp(cum_decay)[:, :, :, None] * carried
    gated_out = mixed_out.reshape(length, heads_here, head_dim) * jax.nn.silu(gate_vals)
    normed = (
        (gated_out * lax.rsqrt(jnp.mean(gated_out * gated_out, axis=2, keepdims=True) + EPSILON))
        .astype(jnp.bfloat16)
        .reshape(length, heads_here * head_dim)
    )
    summed_out = jnp.dot(
        lax.all_gather(normed, "head", axis=1, tiled=True),
        w_out,
        preferred_element_type=jnp.float32,
    )
    return (stream.astype(jnp.float32) + summed_out).astype(jnp.bfloat16)


def local(stream, w_xz, w_bc, w_dt, dt_bias, decay_rate, conv_x, conv_bc, w_out):
    regrouped = regroup(w_xz, w_dt)
    xz_cols = w_xz.shape[2]
    layer = lambda u, l: mix_layer(
        u, regrouped[l], xz_cols, w_bc[l], dt_bias[l], decay_rate[l], conv_x[l], conv_bc[l], w_out[l]
    )
    raster_out = layer(stream, 0)
    members = lax.axis_size("scan")
    length = raster_out.shape[0]
    columns = raster_out.shape[1]
    grouped = raster_out.reshape(members, length // members, 1, columns)
    exchanged = lax.all_to_all(grouped, "scan", split_axis=0, concat_axis=2, tiled=True)
    return layer(exchanged.reshape(length, columns), 1)


def solution(mesh):
    placed = (
        P("scan", "head"),
        P(None, None, "head"),
        P(),
        P(None, None, "head"),
        P(None, "head"),
        P(None, "head"),
        P(None, None, "head"),
        P(),
        P(None, None, "head"),
    )
    return jax.shard_map(
        local, mesh=mesh, in_specs=placed, out_specs=P("scan", "head"), check_vma=False
    )
```

```python
import jax
import jax.numpy as jnp
from jax import lax
from jax.sharding import PartitionSpec as P

BLOCK = 256


EPSILON = 1e-05


def from_behind(shard, axis, by):
    devices = lax.axis_size(axis)
    pairs = [(i, i + by) for i in range(devices) if 0 <= i + by < devices]
    return lax.ppermute(shard, axis, pairs)


def weighted_prefix(states, decays, place):
    order = jnp.arange(states.shape[0])
    between = (order[:, None] < order[None, :]) & (order[None, :] < place)
    span = jnp.sum(jnp.where(between[:, :, None], decays[None, :, :], 0.0), axis=1)
    scale = jnp.where((order < place)[:, None], jnp.exp(span), 0.0)
    return jnp.sum(scale[:, :, None, None] * states, axis=0)


def carried_in(decay, state, axis):
    members = lax.axis_size(axis)
    heads, rows, cols = state.shape
    decay_row = jnp.zeros((1, cols), jnp.float32).at[0, :heads].set(decay)
    packed = jnp.concatenate([state.reshape(heads * rows, cols), decay_row], axis=0)
    gathered = lax.all_gather(packed.astype(jnp.bfloat16), axis).astype(jnp.float32)
    states = gathered[:, : heads * rows].reshape(members, heads, rows, cols)
    decays = gathered[:, heads * rows, :heads]
    return weighted_prefix(states, decays, lax.axis_index(axis))


def causal_conv(rim_rows, pre_conv, kernel):
    padded = jnp.concatenate([rim_rows, pre_conv], axis=0).astype(jnp.float32)
    length = pre_conv.shape[0]
    summed = jnp.zeros(pre_conv.shape, jnp.float32)
    for offset in range(kernel.shape[0]):
        summed = summed + kernel[offset] * padded[offset : offset + length]
    return jax.nn.silu(summed).astype(jnp.bfloat16)


def split_pair(values):
    high = values.astype(jnp.bfloat16)
    low = (values - high.astype(jnp.float32)).astype(jnp.bfloat16)
    return high, low


def regroup(w_xz, w_dt):
    inner = lax.axis_size("head")
    layers, features, _ = w_xz.shape
    packed = jnp.concatenate([w_xz, w_dt], axis=2)
    split = packed.reshape(layers, inner, features // inner, packed.shape[2])
    return lax.all_to_all(split, "head", 1, 1)


def mix_layer(stream, regrouped, xz_cols, w_bc, dt_bias, decay_rate, conv_x, conv_bc, w_out):
    length, piece = stream.shape
    inner = lax.axis_size("head")
    spot = lax.axis_index("head")
    feature_count = piece * inner
    heads_here = regrouped.shape[2] - xz_cols
    head_dim = xz_cols // (2 * heads_here)
    state_dim = w_bc.shape[1] // 2
    taps = conv_x.shape[0]
    partial = jnp.einsum("tf,gfc->tgc", stream, regrouped, preferred_element_type=jnp.float32)
    rows_bc = lax.dynamic_slice_in_dim(w_bc, spot * piece, piece, 0)
    partial_bc = jnp.dot(stream, rows_bc, preferred_element_type=jnp.float32)
    wide_piece = stream.astype(jnp.float32)
    square_high, square_low = split_pair(jnp.sum(wide_piece * wide_piece, axis=1))
    square_slots = jnp.zeros((length, inner, 2), jnp.bfloat16)
    square_slots = lax.dynamic_update_slice_in_dim(
        square_slots, jnp.stack([square_high, square_low], axis=1)[:, None], spot, 1
    )
    reduced = lax.psum(
        jnp.concatenate(
            [partial_bc.astype(jnp.bfloat16), square_slots.reshape(length, 2 * inner)], axis=1
        ),
        "head",
    )
    step_high, step_low = split_pair(partial[:, :, xz_cols:])
    step_slots = jnp.zeros((length, inner, inner, 2, heads_here), jnp.bfloat16)
    step_slots = lax.dynamic_update_slice_in_dim(
        step_slots, jnp.stack([step_high, step_low], axis=2)[:, :, None], spot, 2
    )
    scattered = lax.psum_scatter(
        jnp.concatenate(
            [
                partial[:, :, :xz_cols].astype(jnp.bfloat16),
                step_slots.reshape(length, inner, inner * 2 * heads_here),
            ],
            axis=2,
        ),
        "head",
        scatter_dimension=1,
    )
    summed_xz = scattered[:, :xz_cols]
    dt_sum = jnp.sum(
        scattered[:, xz_cols:].astype(jnp.float32).reshape(length, inner * 2, heads_here), axis=1
    )
    summed_bc = reduced[:, : 2 * state_dim].astype(jnp.float32)
    square_sum = jnp.sum(reduced[:, 2 * state_dim :].astype(jnp.float32), axis=1, keepdims=True)
    row_scale = lax.rsqrt(square_sum / feature_count + EPSILON)
    proj_xz = (
        (summed_xz.astype(jnp.float32) * row_scale)
        .astype(jnp.bfloat16)
        .reshape(length, heads_here, 2, head_dim)
    )
    proj_bc = (summed_bc * row_scale).astype(jnp.bfloat16)
    dt_raw = dt_sum * row_scale
    pre_x = proj_xz[:, :, 0, :].reshape(length, heads_here * head_dim)
    gate_vals = proj_xz[:, :, 1, :].astype(jnp.float32)
    rim_x, rim_bc = from_behind(
        (pre_x[length - taps + 1 :], proj_bc[length - taps + 1 :]), "scan", 1
    )
    inputs_x = causal_conv(rim_x, pre_x, conv_x)
    conv_out = causal_conv(rim_bc, proj_bc, conv_bc)
    block_count = length // BLOCK
    b_blocks = conv_out[:, :state_dim].reshape(block_count, BLOCK, state_dim)
    c_blocks = conv_out[:, state_dim:].reshape(block_count, BLOCK, state_dim)
    gram_mat = jnp.einsum("kqn,ksn->kqs", c_blocks, b_blocks, preferred_element_type=jnp.float32)
    step_dt = jax.nn.softplus(dt_raw + dt_bias)
    cum_decay = jnp.cumsum((-step_dt * decay_rate).reshape(block_count, BLOCK, heads_here), axis=1)
    dt_blocks = step_dt.reshape(block_count, BLOCK, heads_here)
    x_blocks = inputs_x.reshape(block_count, BLOCK, heads_here, head_dim)
    positions = jnp.arange(BLOCK)
    causal = positions[:, None] >= positions[None, :]
    cum_heads = jnp.moveaxis(cum_decay, 2, 1)
    dt_heads = jnp.moveaxis(dt_blocks, 2, 1)
    spread = cum_heads[:, :, :, None] - cum_heads[:, :, None, :]
    weights = (
        gram_mat[:, None]
        * jnp.exp(jnp.where(causal[None, None], spread, -jnp.inf))
        * dt_heads[:, :, None, :]
    ).astype(jnp.bfloat16)
    inside = jnp.einsum("khqs,kshp->kqhp", weights, x_blocks, preferred_element_type=jnp.float32)
    to_end = jnp.exp(cum_decay[:, -1:, :] - cum_decay) * dt_blocks
    scaled = (x_blocks.astype(jnp.float32) * to_end[:, :, :, None]).astype(jnp.bfloat16)
    block_ends = jnp.einsum("kqhp,kqn->khpn", scaled, b_blocks, preferred_element_type=jnp.float32)
    block_decay = cum_decay[:, -1, :]

    starts_local = jnp.stack(
        [weighted_prefix(block_ends, block_decay, k) for k in range(block_count)]
    )
    local_end = weighted_prefix(block_ends, block_decay, block_count)
    device_decay = jnp.sum(block_decay, axis=0)
    incoming = carried_in(device_decay, local_end, "scan")
    prior_decay = jnp.concatenate(
        [jnp.zeros((1, heads_here), jnp.float32), jnp.cumsum(block_decay, axis=0)[:-1]], axis=0
    )
    starts = jnp.exp(prior_decay)[:, :, None, None] * incoming[None] + starts_local
    carried = jnp.einsum(
        "kqn,khpn->kqhp", c_blocks.astype(jnp.float32), starts, precision=lax.Precision.HIGHEST
    )
    mixed_out = inside + jnp.exp(cum_decay)[:, :, :, None] * carried
    gated_out = mixed_out.reshape(length, heads_here, head_dim) * jax.nn.silu(gate_vals)
    normed = (
        (gated_out * lax.rsqrt(jnp.mean(gated_out * gated_out, axis=2, keepdims=True) + EPSILON))
        .astype(jnp.bfloat16)
        .reshape(length, heads_here * head_dim)
    )
    summed_out = jnp.dot(
        lax.all_gather(normed, "head", axis=1, tiled=True),
        w_out,
        preferred_element_type=jnp.float32,
    )
    return (stream.astype(jnp.float32) + summed_out).astype(jnp.bfloat16)


def local(stream, w_xz, w_bc, w_dt, dt_bias, decay_rate, conv_x, conv_bc, w_out):
    regrouped = regroup(w_xz, w_dt)
    xz_cols = w_xz.shape[2]
    layer = lambda u, l: mix_layer(
        u, regrouped[l], xz_cols, w_bc[l], dt_bias[l], decay_rate[l], conv_x[l], conv_bc[l], w_out[l]
    )
    raster_out = layer(stream, 0)
    members = lax.axis_size("scan")
    length = raster_out.shape[0]
    columns = raster_out.shape[1]
    grouped = raster_out.reshape(members, length // members, 1, columns)
    exchanged = lax.all_to_all(grouped, "scan", split_axis=0, concat_axis=2, tiled=True)
    return layer(exchanged.reshape(length, columns), 1)


def solution(mesh):
    placed = (
        P("scan", "head"),
        P(None, None, "head"),
        P(),
        P(None, None, "head"),
        P(None, "head"),
        P(None, "head"),
        P(None, None, "head"),
        P(),
        P(None, None, "head"),
    )
    return jax.shard_map(
        local, mesh=mesh, in_specs=placed, out_specs=P("scan", "head"), check_vma=False
    )
```

```python
import jax
import jax.numpy as jnp
from jax import lax
from jax.sharding import PartitionSpec as P

BLOCK = 256


EPSILON = 1e-05


def from_behind(shard, axis, by):
    devices = lax.axis_size(axis)
    pairs = [(i, i + by) for i in range(devices) if 0 <= i + by < devices]
    return lax.ppermute(shard, axis, pairs)


def weighted_prefix(states, decays, place):
    order = jnp.arange(states.shape[0])
    between = (order[:, None] < order[None, :]) & (order[None, :] < place)
    span = jnp.sum(jnp.where(between[:, :, None], decays[None, :, :], 0.0), axis=1)
    scale = jnp.where((order < place)[:, None], jnp.exp(span), 0.0)
    return jnp.sum(scale[:, :, None, None] * states, axis=0)


def carried_in(decay, state, axis):
    members = lax.axis_size(axis)
    heads, rows, cols = state.shape
    decay_row = jnp.zeros((1, cols), jnp.float32).at[0, :heads].set(decay)
    packed = jnp.concatenate([state.reshape(heads * rows, cols), decay_row], axis=0)
    gathered = lax.all_gather(packed.astype(jnp.bfloat16), axis).astype(jnp.float32)
    states = gathered[:, : heads * rows].reshape(members, heads, rows, cols)
    decays = gathered[:, heads * rows, :heads]
    return weighted_prefix(states, decays, lax.axis_index(axis))


def causal_conv(rim_rows, pre_conv, kernel):
    padded = jnp.concatenate([rim_rows, pre_conv], axis=0).astype(jnp.float32)
    length = pre_conv.shape[0]
    summed = jnp.zeros(pre_conv.shape, jnp.float32)
    for offset in range(kernel.shape[0]):
        summed = summed + kernel[offset] * padded[offset : offset + length]
    return jax.nn.silu(summed).astype(jnp.bfloat16)


def split_pair(values):
    high = values.astype(jnp.bfloat16)
    low = (values - high.astype(jnp.float32)).astype(jnp.bfloat16)
    return high, low


def regroup(w_xz, w_dt):
    inner = lax.axis_size("head")
    layers, features, _ = w_xz.shape
    packed = jnp.concatenate([w_xz, w_dt], axis=2)
    split = packed.reshape(layers, inner, features // inner, packed.shape[2])
    return lax.all_to_all(split, "head", 1, 1)


def mix_layer(stream, regrouped, xz_cols, w_bc, dt_bias, decay_rate, conv_x, conv_bc, w_out):
    length, piece = stream.shape
    inner = lax.axis_size("head")
    spot = lax.axis_index("head")
    feature_count = piece * inner
    heads_here = regrouped.shape[2] - xz_cols
    head_dim = xz_cols // (2 * heads_here)
    state_dim = w_bc.shape[1] // 2
    taps = conv_x.shape[0]
    partial = jnp.einsum("tf,gfc->tgc", stream, regrouped, preferred_element_type=jnp.float32)
    rows_bc = lax.dynamic_slice_in_dim(w_bc, spot * piece, piece, 0)
    partial_bc = jnp.dot(stream, rows_bc, preferred_element_type=jnp.float32)
    wide_piece = stream.astype(jnp.float32)
    square_high, square_low = split_pair(jnp.sum(wide_piece * wide_piece, axis=1))
    square_slots = jnp.zeros((length, inner, 2), jnp.bfloat16)
    square_slots = lax.dynamic_update_slice_in_dim(
        square_slots, jnp.stack([square_high, square_low], axis=1)[:, None], spot, 1
    )
    reduced = lax.psum(
        jnp.concatenate(
            [partial_bc.astype(jnp.bfloat16), square_slots.reshape(length, 2 * inner)], axis=1
        ),
        "head",
    )
    step_high, step_low = split_pair(partial[:, :, xz_cols:])
    outgoing = jnp.concatenate(
        [partial[:, :, :xz_cols].astype(jnp.bfloat16), step_high, step_low], axis=2
    )
    arrived = lax.all_to_all(jnp.moveaxis(outgoing, 1, 0), "head", 0, 0).astype(jnp.float32)
    summed_xz = jnp.sum(arrived[:, :, :xz_cols], axis=0)
    dt_sum = jnp.sum(
        arrived[:, :, xz_cols : xz_cols + heads_here] + arrived[:, :, xz_cols + heads_here :],
        axis=0,
    )
    summed_bc = reduced[:, : 2 * state_dim].astype(jnp.float32)
    square_sum = jnp.sum(reduced[:, 2 * state_dim :].astype(jnp.float32), axis=1, keepdims=True)
    row_scale = lax.rsqrt(square_sum / feature_count + EPSILON)
    proj_xz = (
        (summed_xz.astype(jnp.float32) * row_scale)
        .astype(jnp.bfloat16)
        .reshape(length, heads_here, 2, head_dim)
    )
    proj_bc = (summed_bc * row_scale).astype(jnp.bfloat16)
    dt_raw = dt_sum * row_scale
    pre_x = proj_xz[:, :, 0, :].reshape(length, heads_here * head_dim)
    gate_vals = proj_xz[:, :, 1, :].astype(jnp.float32)
    rim_x, rim_bc = from_behind(
        (pre_x[length - taps + 1 :], proj_bc[length - taps + 1 :]), "scan", 1
    )
    inputs_x = causal_conv(rim_x, pre_x, conv_x)
    conv_out = causal_conv(rim_bc, proj_bc, conv_bc)
    block_count = length // BLOCK
    b_blocks = conv_out[:, :state_dim].reshape(block_count, BLOCK, state_dim)
    c_blocks = conv_out[:, state_dim:].reshape(block_count, BLOCK, state_dim)
    gram_mat = jnp.einsum("kqn,ksn->kqs", c_blocks, b_blocks, preferred_element_type=jnp.float32)
    step_dt = jax.nn.softplus(dt_raw + dt_bias)
    cum_decay = jnp.cumsum((-step_dt * decay_rate).reshape(block_count, BLOCK, heads_here), axis=1)
    dt_blocks = step_dt.reshape(block_count, BLOCK, heads_here)
    x_blocks = inputs_x.reshape(block_count, BLOCK, heads_here, head_dim)
    positions = jnp.arange(BLOCK)
    causal = positions[:, None] >= positions[None, :]
    cum_heads = jnp.moveaxis(cum_decay, 2, 1)
    dt_heads = jnp.moveaxis(dt_blocks, 2, 1)
    spread = cum_heads[:, :, :, None] - cum_heads[:, :, None, :]
    weights = (
        gram_mat[:, None]
        * jnp.exp(jnp.where(causal[None, None], spread, -jnp.inf))
        * dt_heads[:, :, None, :]
    ).astype(jnp.bfloat16)
    inside = jnp.einsum("khqs,kshp->kqhp", weights, x_blocks, preferred_element_type=jnp.float32)
    to_end = jnp.exp(cum_decay[:, -1:, :] - cum_decay) * dt_blocks
    scaled = (x_blocks.astype(jnp.float32) * to_end[:, :, :, None]).astype(jnp.bfloat16)
    block_ends = jnp.einsum("kqhp,kqn->khpn", scaled, b_blocks, preferred_element_type=jnp.float32)
    block_decay = cum_decay[:, -1, :]

    starts_local = jnp.stack(
        [weighted_prefix(block_ends, block_decay, k) for k in range(block_count)]
    )
    local_end = weighted_prefix(block_ends, block_decay, block_count)
    device_decay = jnp.sum(block_decay, axis=0)
    incoming = carried_in(device_decay, local_end, "scan")
    prior_decay = jnp.concatenate(
        [jnp.zeros((1, heads_here), jnp.float32), jnp.cumsum(block_decay, axis=0)[:-1]], axis=0
    )
    starts = jnp.exp(prior_decay)[:, :, None, None] * incoming[None] + starts_local
    carried = jnp.einsum(
        "kqn,khpn->kqhp", c_blocks.astype(jnp.float32), starts, precision=lax.Precision.HIGHEST
    )
    mixed_out = inside + jnp.exp(cum_decay)[:, :, :, None] * carried
    gated_out = mixed_out.reshape(length, heads_here, head_dim) * jax.nn.silu(gate_vals)
    normed = (
        (gated_out * lax.rsqrt(jnp.mean(gated_out * gated_out, axis=2, keepdims=True) + EPSILON))
        .astype(jnp.bfloat16)
        .reshape(length, heads_here * head_dim)
    )
    summed_out = jnp.dot(
        lax.all_gather(normed, "head", axis=1, tiled=True),
        w_out,
        preferred_element_type=jnp.float32,
    )
    return (stream.astype(jnp.float32) + summed_out).astype(jnp.bfloat16)


def local(stream, w_xz, w_bc, w_dt, dt_bias, decay_rate, conv_x, conv_bc, w_out):
    regrouped = regroup(w_xz, w_dt)
    xz_cols = w_xz.shape[2]
    layer = lambda u, l: mix_layer(
        u, regrouped[l], xz_cols, w_bc[l], dt_bias[l], decay_rate[l], conv_x[l], conv_bc[l], w_out[l]
    )
    raster_out = layer(stream, 0)
    members = lax.axis_size("scan")
    length = raster_out.shape[0]
    columns = raster_out.shape[1]
    grouped = raster_out.reshape(members, length // members, 1, columns)
    exchanged = lax.all_to_all(grouped, "scan", split_axis=0, concat_axis=2, tiled=True)
    return layer(exchanged.reshape(length, columns), 1)


def solution(mesh):
    placed = (
        P("scan", "head"),
        P(None, None, "head"),
        P(),
        P(None, None, "head"),
        P(None, "head"),
        P(None, "head"),
        P(None, None, "head"),
        P(),
        P(None, None, "head"),
    )
    return jax.shard_map(
        local, mesh=mesh, in_specs=placed, out_specs=P("scan", "head"), check_vma=False
    )
```

```python
import jax
import jax.numpy as jnp
from jax import lax
from jax.sharding import PartitionSpec as P

BLOCK = 256


EPSILON = 1e-05


def from_behind(shard, axis, by):
    devices = lax.axis_size(axis)
    pairs = [(i, i + by) for i in range(devices) if 0 <= i + by < devices]
    return lax.ppermute(shard, axis, pairs)


def weighted_prefix(states, decays, place):
    order = jnp.arange(states.shape[0])
    between = (order[:, None] < order[None, :]) & (order[None, :] < place)
    span = jnp.sum(jnp.where(between[:, :, None], decays[None, :, :], 0.0), axis=1)
    scale = jnp.where((order < place)[:, None], jnp.exp(span), 0.0)
    return jnp.sum(scale[:, :, None, None] * states, axis=0)


def carried_in(decay, state, axis):
    members = lax.axis_size(axis)
    heads, rows, cols = state.shape
    decay_row = jnp.zeros((1, cols), jnp.float32).at[0, :heads].set(decay)
    packed = jnp.concatenate([state.reshape(heads * rows, cols), decay_row], axis=0)
    gathered = lax.all_gather(packed.astype(jnp.bfloat16), axis).astype(jnp.float32)
    states = gathered[:, : heads * rows].reshape(members, heads, rows, cols)
    decays = gathered[:, heads * rows, :heads]
    return weighted_prefix(states, decays, lax.axis_index(axis))


def causal_conv(rim_rows, pre_conv, kernel):
    padded = jnp.concatenate([rim_rows, pre_conv], axis=0).astype(jnp.float32)
    length = pre_conv.shape[0]
    summed = jnp.zeros(pre_conv.shape, jnp.float32)
    for offset in range(kernel.shape[0]):
        summed = summed + kernel[offset] * padded[offset : offset + length]
    return jax.nn.silu(summed).astype(jnp.bfloat16)


def split_pair(values):
    high = values.astype(jnp.bfloat16)
    low = (values - high.astype(jnp.float32)).astype(jnp.bfloat16)
    return high, low


def regroup(w_xz, w_dt):
    inner = lax.axis_size("head")
    layers, features, _ = w_xz.shape
    packed = jnp.concatenate([w_xz, w_dt], axis=2)
    split = packed.reshape(layers, inner, features // inner, packed.shape[2])
    return lax.all_to_all(split, "head", 1, 1)


def mix_layer(stream, regrouped, xz_cols, w_bc, dt_bias, decay_rate, conv_x, conv_bc, w_out):
    length, piece = stream.shape
    inner = lax.axis_size("head")
    spot = lax.axis_index("head")
    feature_count = piece * inner
    heads_here = regrouped.shape[2] - xz_cols
    head_dim = xz_cols // (2 * heads_here)
    state_dim = w_bc.shape[1] // 2
    taps = conv_x.shape[0]
    partial = jnp.einsum("tf,gfc->tgc", stream, regrouped, preferred_element_type=jnp.float32)
    rows_bc = lax.dynamic_slice_in_dim(w_bc, spot * piece, piece, 0)
    slice_bc = 2 * state_dim // inner
    partial_bc = jnp.dot(stream, rows_bc, preferred_element_type=jnp.float32).reshape(
        length, inner, slice_bc
    )
    wide_piece = stream.astype(jnp.float32)
    square_high, square_low = split_pair(jnp.sum(wide_piece * wide_piece, axis=1))
    squares = jnp.broadcast_to(
        jnp.stack([square_high, square_low], axis=1)[:, None], (length, inner, 2)
    )
    step_high, step_low = split_pair(partial[:, :, xz_cols:])
    outgoing = jnp.concatenate(
        [
            partial[:, :, :xz_cols].astype(jnp.bfloat16),
            partial_bc.astype(jnp.bfloat16),
            step_high,
            step_low,
            squares,
        ],
        axis=2,
    )
    arrived = lax.all_to_all(jnp.moveaxis(outgoing, 1, 0), "head", 0, 0).astype(jnp.float32)
    summed = jnp.sum(arrived, axis=0)
    summed_xz = summed[:, :xz_cols]
    summed_bc = summed[:, xz_cols : xz_cols + slice_bc]
    at = xz_cols + slice_bc
    dt_sum = summed[:, at : at + heads_here] + summed[:, at + heads_here : at + 2 * heads_here]
    square_sum = summed[:, at + 2 * heads_here :].sum(axis=1, keepdims=True)
    row_scale = lax.rsqrt(square_sum / feature_count + EPSILON)
    proj_xz = (
        (summed_xz.astype(jnp.float32) * row_scale)
        .astype(jnp.bfloat16)
        .reshape(length, heads_here, 2, head_dim)
    )
    proj_bc = (summed_bc * row_scale).astype(jnp.bfloat16)
    dt_raw = dt_sum * row_scale
    pre_x = proj_xz[:, :, 0, :].reshape(length, heads_here * head_dim)
    gate_vals = proj_xz[:, :, 1, :].astype(jnp.float32)
    rim_x, rim_bc = from_behind(
        (pre_x[length - taps + 1 :], proj_bc[length - taps + 1 :]), "scan", 1
    )
    inputs_x = causal_conv(rim_x, pre_x, conv_x)
    taps_bc = lax.dynamic_slice_in_dim(conv_bc, spot * slice_bc, slice_bc, 1)
    conv_slice = causal_conv(rim_bc, proj_bc, taps_bc)
    conv_out = jnp.moveaxis(lax.all_gather(conv_slice, "head"), 0, 1).reshape(length, 2 * state_dim)
    block_count = length // BLOCK
    b_blocks = conv_out[:, :state_dim].reshape(block_count, BLOCK, state_dim)
    c_blocks = conv_out[:, state_dim:].reshape(block_count, BLOCK, state_dim)
    gram_mat = jnp.einsum("kqn,ksn->kqs", c_blocks, b_blocks, preferred_element_type=jnp.float32)
    step_dt = jax.nn.softplus(dt_raw + dt_bias)
    cum_decay = jnp.cumsum((-step_dt * decay_rate).reshape(block_count, BLOCK, heads_here), axis=1)
    dt_blocks = step_dt.reshape(block_count, BLOCK, heads_here)
    x_blocks = inputs_x.reshape(block_count, BLOCK, heads_here, head_dim)
    positions = jnp.arange(BLOCK)
    causal = positions[:, None] >= positions[None, :]
    cum_heads = jnp.moveaxis(cum_decay, 2, 1)
    dt_heads = jnp.moveaxis(dt_blocks, 2, 1)
    spread = cum_heads[:, :, :, None] - cum_heads[:, :, None, :]
    weights = (
        gram_mat[:, None]
        * jnp.exp(jnp.where(causal[None, None], spread, -jnp.inf))
        * dt_heads[:, :, None, :]
    ).astype(jnp.bfloat16)
    inside = jnp.einsum("khqs,kshp->kqhp", weights, x_blocks, preferred_element_type=jnp.float32)
    to_end = jnp.exp(cum_decay[:, -1:, :] - cum_decay) * dt_blocks
    scaled = (x_blocks.astype(jnp.float32) * to_end[:, :, :, None]).astype(jnp.bfloat16)
    block_ends = jnp.einsum("kqhp,kqn->khpn", scaled, b_blocks, preferred_element_type=jnp.float32)
    block_decay = cum_decay[:, -1, :]

    starts_local = jnp.stack(
        [weighted_prefix(block_ends, block_decay, k) for k in range(block_count)]
    )
    local_end = weighted_prefix(block_ends, block_decay, block_count)
    device_decay = jnp.sum(block_decay, axis=0)
    incoming = carried_in(device_decay, local_end, "scan")
    prior_decay = jnp.concatenate(
        [jnp.zeros((1, heads_here), jnp.float32), jnp.cumsum(block_decay, axis=0)[:-1]], axis=0
    )
    starts = jnp.exp(prior_decay)[:, :, None, None] * incoming[None] + starts_local
    carried = jnp.einsum(
        "kqn,khpn->kqhp", c_blocks.astype(jnp.float32), starts, precision=lax.Precision.HIGHEST
    )
    mixed_out = inside + jnp.exp(cum_decay)[:, :, :, None] * carried
    gated_out = mixed_out.reshape(length, heads_here, head_dim) * jax.nn.silu(gate_vals)
    normed = (
        (gated_out * lax.rsqrt(jnp.mean(gated_out * gated_out, axis=2, keepdims=True) + EPSILON))
        .astype(jnp.bfloat16)
        .reshape(length, heads_here * head_dim)
    )
    summed_out = jnp.dot(
        lax.all_gather(normed, "head", axis=1, tiled=True),
        w_out,
        preferred_element_type=jnp.float32,
    )
    return (stream.astype(jnp.float32) + summed_out).astype(jnp.bfloat16)


def local(stream, w_xz, w_bc, w_dt, dt_bias, decay_rate, conv_x, conv_bc, w_out):
    regrouped = regroup(w_xz, w_dt)
    xz_cols = w_xz.shape[2]
    layer = lambda u, l: mix_layer(
        u, regrouped[l], xz_cols, w_bc[l], dt_bias[l], decay_rate[l], conv_x[l], conv_bc[l], w_out[l]
    )
    raster_out = layer(stream, 0)
    members = lax.axis_size("scan")
    length = raster_out.shape[0]
    columns = raster_out.shape[1]
    grouped = raster_out.reshape(members, length // members, 1, columns)
    exchanged = lax.all_to_all(grouped, "scan", split_axis=0, concat_axis=2, tiled=True)
    return layer(exchanged.reshape(length, columns), 1)


def solution(mesh):
    placed = (
        P("scan", "head"),
        P(None, None, "head"),
        P(),
        P(None, None, "head"),
        P(None, "head"),
        P(None, "head"),
        P(None, None, "head"),
        P(),
        P(None, None, "head"),
    )
    return jax.shard_map(
        local, mesh=mesh, in_specs=placed, out_specs=P("scan", "head"), check_vma=False
    )
```

```python
import jax
import jax.numpy as jnp
from jax import lax
from jax.sharding import PartitionSpec as P

BLOCK = 256


EPSILON = 1e-05


def from_behind(shard, axis, by):
    devices = lax.axis_size(axis)
    pairs = [(i, i + by) for i in range(devices) if 0 <= i + by < devices]
    return lax.ppermute(shard, axis, pairs)


def weighted_prefix(states, decays, place):
    order = jnp.arange(states.shape[0])
    between = (order[:, None] < order[None, :]) & (order[None, :] < place)
    span = jnp.sum(jnp.where(between[:, :, None], decays[None, :, :], 0.0), axis=1)
    scale = jnp.where((order < place)[:, None], jnp.exp(span), 0.0)
    return jnp.sum(scale[:, :, None, None] * states, axis=0)


def carried_in(decay, state, axis):
    members = lax.axis_size(axis)
    heads, rows, cols = state.shape
    decay_row = jnp.zeros((1, cols), jnp.float32).at[0, :heads].set(decay)
    packed = jnp.concatenate([state.reshape(heads * rows, cols), decay_row], axis=0)
    gathered = lax.all_gather(packed.astype(jnp.bfloat16), axis).astype(jnp.float32)
    states = gathered[:, : heads * rows].reshape(members, heads, rows, cols)
    decays = gathered[:, heads * rows, :heads]
    return weighted_prefix(states, decays, lax.axis_index(axis))


def causal_conv(rim_rows, pre_conv, kernel):
    padded = jnp.concatenate([rim_rows, pre_conv], axis=0).astype(jnp.float32)
    length = pre_conv.shape[0]
    summed = jnp.zeros(pre_conv.shape, jnp.float32)
    for offset in range(kernel.shape[0]):
        summed = summed + kernel[offset] * padded[offset : offset + length]
    return jax.nn.silu(summed).astype(jnp.bfloat16)


def split_pair(values):
    high = values.astype(jnp.bfloat16)
    low = (values - high.astype(jnp.float32)).astype(jnp.bfloat16)
    return high, low


def regroup(w_xz, w_dt):
    inner = lax.axis_size("head")
    layers, features, _ = w_xz.shape
    packed = jnp.concatenate([w_xz, w_dt], axis=2)
    split = packed.reshape(layers, inner, features // inner, packed.shape[2])
    return lax.all_to_all(split, "head", 1, 1)


def gather_heads(values):
    inner = lax.axis_size("head")
    return lax.all_to_all(jnp.broadcast_to(values[None], (inner,) + values.shape), "head", 0, 0)


def mix_layer(stream, regrouped, xz_cols, w_bc, dt_bias, decay_rate, conv_x, conv_bc, w_out):
    length, piece = stream.shape
    inner = lax.axis_size("head")
    spot = lax.axis_index("head")
    feature_count = piece * inner
    heads_here = regrouped.shape[2] - xz_cols
    head_dim = xz_cols // (2 * heads_here)
    state_dim = w_bc.shape[1] // 2
    taps = conv_x.shape[0]
    partial = jnp.einsum("tf,gfc->tgc", stream, regrouped, preferred_element_type=jnp.float32)
    rows_bc = lax.dynamic_slice_in_dim(w_bc, spot * piece, piece, 0)
    slice_bc = 2 * state_dim // inner
    partial_bc = jnp.dot(stream, rows_bc, preferred_element_type=jnp.float32).reshape(
        length, inner, slice_bc
    )
    wide_piece = stream.astype(jnp.float32)
    square_high, square_low = split_pair(jnp.sum(wide_piece * wide_piece, axis=1))
    squares = jnp.broadcast_to(
        jnp.stack([square_high, square_low], axis=1)[:, None], (length, inner, 2)
    )
    step_high, step_low = split_pair(partial[:, :, xz_cols:])
    outgoing = jnp.concatenate(
        [
            partial[:, :, :xz_cols].astype(jnp.bfloat16),
            partial_bc.astype(jnp.bfloat16),
            step_high,
            step_low,
            squares,
        ],
        axis=2,
    )
    arrived = lax.all_to_all(jnp.moveaxis(outgoing, 1, 0), "head", 0, 0).astype(jnp.float32)
    summed = jnp.sum(arrived, axis=0)
    summed_xz = summed[:, :xz_cols]
    summed_bc = summed[:, xz_cols : xz_cols + slice_bc]
    at = xz_cols + slice_bc
    dt_sum = summed[:, at : at + heads_here] + summed[:, at + heads_here : at + 2 * heads_here]
    square_sum = summed[:, at + 2 * heads_here :].sum(axis=1, keepdims=True)
    row_scale = lax.rsqrt(square_sum / feature_count + EPSILON)
    proj_xz = (
        (summed_xz.astype(jnp.float32) * row_scale)
        .astype(jnp.bfloat16)
        .reshape(length, heads_here, 2, head_dim)
    )
    proj_bc = (summed_bc * row_scale).astype(jnp.bfloat16)
    dt_raw = dt_sum * row_scale
    pre_x = proj_xz[:, :, 0, :].reshape(length, heads_here * head_dim)
    gate_vals = proj_xz[:, :, 1, :].astype(jnp.float32)
    rim_x, rim_bc = from_behind(
        (pre_x[length - taps + 1 :], proj_bc[length - taps + 1 :]), "scan", 1
    )
    inputs_x = causal_conv(rim_x, pre_x, conv_x)
    taps_bc = lax.dynamic_slice_in_dim(conv_bc, spot * slice_bc, slice_bc, 1)
    conv_slice = causal_conv(rim_bc, proj_bc, taps_bc)
    conv_out = jnp.moveaxis(gather_heads(conv_slice), 0, 1).reshape(length, 2 * state_dim)
    block_count = length // BLOCK
    b_blocks = conv_out[:, :state_dim].reshape(block_count, BLOCK, state_dim)
    c_blocks = conv_out[:, state_dim:].reshape(block_count, BLOCK, state_dim)
    gram_mat = jnp.einsum("kqn,ksn->kqs", c_blocks, b_blocks, preferred_element_type=jnp.float32)
    step_dt = jax.nn.softplus(dt_raw + dt_bias)
    cum_decay = jnp.cumsum((-step_dt * decay_rate).reshape(block_count, BLOCK, heads_here), axis=1)
    dt_blocks = step_dt.reshape(block_count, BLOCK, heads_here)
    x_blocks = inputs_x.reshape(block_count, BLOCK, heads_here, head_dim)
    positions = jnp.arange(BLOCK)
    causal = positions[:, None] >= positions[None, :]
    cum_heads = jnp.moveaxis(cum_decay, 2, 1)
    dt_heads = jnp.moveaxis(dt_blocks, 2, 1)
    spread = cum_heads[:, :, :, None] - cum_heads[:, :, None, :]
    weights = (
        gram_mat[:, None]
        * jnp.exp(jnp.where(causal[None, None], spread, -jnp.inf))
        * dt_heads[:, :, None, :]
    ).astype(jnp.bfloat16)
    inside = jnp.einsum("khqs,kshp->kqhp", weights, x_blocks, preferred_element_type=jnp.float32)
    to_end = jnp.exp(cum_decay[:, -1:, :] - cum_decay) * dt_blocks
    scaled = (x_blocks.astype(jnp.float32) * to_end[:, :, :, None]).astype(jnp.bfloat16)
    block_ends = jnp.einsum("kqhp,kqn->khpn", scaled, b_blocks, preferred_element_type=jnp.float32)
    block_decay = cum_decay[:, -1, :]

    starts_local = jnp.stack(
        [weighted_prefix(block_ends, block_decay, k) for k in range(block_count)]
    )
    local_end = weighted_prefix(block_ends, block_decay, block_count)
    device_decay = jnp.sum(block_decay, axis=0)
    incoming = carried_in(device_decay, local_end, "scan")
    prior_decay = jnp.concatenate(
        [jnp.zeros((1, heads_here), jnp.float32), jnp.cumsum(block_decay, axis=0)[:-1]], axis=0
    )
    starts = jnp.exp(prior_decay)[:, :, None, None] * incoming[None] + starts_local
    carried = jnp.einsum(
        "kqn,khpn->kqhp", c_blocks.astype(jnp.float32), starts, precision=lax.Precision.HIGHEST
    )
    mixed_out = inside + jnp.exp(cum_decay)[:, :, :, None] * carried
    gated_out = mixed_out.reshape(length, heads_here, head_dim) * jax.nn.silu(gate_vals)
    normed = (
        (gated_out * lax.rsqrt(jnp.mean(gated_out * gated_out, axis=2, keepdims=True) + EPSILON))
        .astype(jnp.bfloat16)
        .reshape(length, heads_here * head_dim)
    )
    summed_out = jnp.dot(
        jnp.moveaxis(gather_heads(normed), 0, 1).reshape(length, inner * normed.shape[1]),
        w_out,
        preferred_element_type=jnp.float32,
    )
    return (stream.astype(jnp.float32) + summed_out).astype(jnp.bfloat16)


def local(stream, w_xz, w_bc, w_dt, dt_bias, decay_rate, conv_x, conv_bc, w_out):
    xz_cols = w_xz.shape[2]
    layer = lambda u, l: mix_layer(
        u, regroup(w_xz[l : l + 1], w_dt[l : l + 1])[0], xz_cols, w_bc[l], dt_bias[l], decay_rate[l], conv_x[l], conv_bc[l], w_out[l]
    )
    raster_out = layer(stream, 0)
    members = lax.axis_size("scan")
    length = raster_out.shape[0]
    columns = raster_out.shape[1]
    grouped = raster_out.reshape(members, length // members, 1, columns)
    exchanged = lax.all_to_all(grouped, "scan", split_axis=0, concat_axis=2, tiled=True)
    return layer(exchanged.reshape(length, columns), 1)


def solution(mesh):
    placed = (
        P("scan", "head"),
        P(None, None, "head"),
        P(),
        P(None, None, "head"),
        P(None, "head"),
        P(None, "head"),
        P(None, None, "head"),
        P(),
        P(None, None, "head"),
    )
    return jax.shard_map(
        local, mesh=mesh, in_specs=placed, out_specs=P("scan", "head"), check_vma=False
    )
```

```python
import jax
import jax.numpy as jnp
from jax import lax
from jax.sharding import PartitionSpec as P

BLOCK = 256


EPSILON = 1e-05


def from_behind(shard, axis, by):
    devices = lax.axis_size(axis)
    pairs = [(i, i + by) for i in range(devices) if 0 <= i + by < devices]
    return lax.ppermute(shard, axis, pairs)


def weighted_prefix(states, decays, place):
    order = jnp.arange(states.shape[0])
    between = (order[:, None] < order[None, :]) & (order[None, :] < place)
    span = jnp.sum(jnp.where(between[:, :, None], decays[None, :, :], 0.0), axis=1)
    scale = jnp.where((order < place)[:, None], jnp.exp(span), 0.0)
    return jnp.sum(scale[:, :, None, None] * states, axis=0)


def carried_in(decay, state, axis):
    members = lax.axis_size(axis)
    heads, rows, cols = state.shape
    decay_row = jnp.zeros((1, cols), jnp.float32).at[0, :heads].set(decay)
    packed = jnp.concatenate([state.reshape(heads * rows, cols), decay_row], axis=0)
    gathered = lax.all_gather(packed.astype(jnp.bfloat16), axis).astype(jnp.float32)
    states = gathered[:, : heads * rows].reshape(members, heads, rows, cols)
    decays = gathered[:, heads * rows, :heads]
    return weighted_prefix(states, decays, lax.axis_index(axis))


def causal_conv(rim_rows, pre_conv, kernel):
    padded = jnp.concatenate([rim_rows, pre_conv], axis=0).astype(jnp.float32)
    length = pre_conv.shape[0]
    summed = jnp.zeros(pre_conv.shape, jnp.float32)
    for offset in range(kernel.shape[0]):
        summed = summed + kernel[offset] * padded[offset : offset + length]
    return jax.nn.silu(summed).astype(jnp.bfloat16)


def split_pair(values):
    high = values.astype(jnp.bfloat16)
    low = (values - high.astype(jnp.float32)).astype(jnp.bfloat16)
    return high, low


def regroup(w_xz, w_dt):
    inner = lax.axis_size("head")
    layers, features, _ = w_xz.shape
    packed = jnp.concatenate([w_xz, w_dt], axis=2)
    split = packed.reshape(layers, inner, features // inner, packed.shape[2])
    return lax.all_to_all(split, "head", 1, 1)


def regroup_by_gather(w_xz, w_dt):
    inner = lax.axis_size("head")
    features = w_xz.shape[0]
    piece = features // inner
    gathered = lax.all_gather(jnp.concatenate([w_xz, w_dt], axis=1), "head")
    return lax.dynamic_slice_in_dim(gathered, lax.axis_index("head") * piece, piece, 1)


def mix_layer(stream, regrouped, xz_cols, w_bc, dt_bias, decay_rate, conv_x, conv_bc, w_out):
    length, piece = stream.shape
    inner = lax.axis_size("head")
    spot = lax.axis_index("head")
    feature_count = piece * inner
    heads_here = regrouped.shape[2] - xz_cols
    head_dim = xz_cols // (2 * heads_here)
    state_dim = w_bc.shape[1] // 2
    taps = conv_x.shape[0]
    partial = jnp.einsum("tf,gfc->tgc", stream, regrouped, preferred_element_type=jnp.float32)
    rows_bc = lax.dynamic_slice_in_dim(w_bc, spot * piece, piece, 0)
    slice_bc = 2 * state_dim // inner
    partial_bc = jnp.dot(stream, rows_bc, preferred_element_type=jnp.float32).reshape(
        length, inner, slice_bc
    )
    wide_piece = stream.astype(jnp.float32)
    square_high, square_low = split_pair(jnp.sum(wide_piece * wide_piece, axis=1))
    squares = jnp.broadcast_to(
        jnp.stack([square_high, square_low], axis=1)[:, None], (length, inner, 2)
    )
    step_high, step_low = split_pair(partial[:, :, xz_cols:])
    outgoing = jnp.concatenate(
        [
            partial[:, :, :xz_cols].astype(jnp.bfloat16),
            partial_bc.astype(jnp.bfloat16),
            step_high,
            step_low,
            squares,
        ],
        axis=2,
    )
    arrived = lax.all_to_all(jnp.moveaxis(outgoing, 1, 0), "head", 0, 0).astype(jnp.float32)
    summed = jnp.sum(arrived, axis=0)
    summed_xz = summed[:, :xz_cols]
    summed_bc = summed[:, xz_cols : xz_cols + slice_bc]
    at = xz_cols + slice_bc
    dt_sum = summed[:, at : at + heads_here] + summed[:, at + heads_here : at + 2 * heads_here]
    square_sum = summed[:, at + 2 * heads_here :].sum(axis=1, keepdims=True)
    row_scale = lax.rsqrt(square_sum / feature_count + EPSILON)
    proj_xz = (
        (summed_xz.astype(jnp.float32) * row_scale)
        .astype(jnp.bfloat16)
        .reshape(length, heads_here, 2, head_dim)
    )
    proj_bc = (summed_bc * row_scale).astype(jnp.bfloat16)
    dt_raw = dt_sum * row_scale
    pre_x = proj_xz[:, :, 0, :].reshape(length, heads_here * head_dim)
    gate_vals = proj_xz[:, :, 1, :].astype(jnp.float32)
    rim_x, rim_bc = from_behind(
        (pre_x[length - taps + 1 :], proj_bc[length - taps + 1 :]), "scan", 1
    )
    inputs_x = causal_conv(rim_x, pre_x, conv_x)
    taps_bc = lax.dynamic_slice_in_dim(conv_bc, spot * slice_bc, slice_bc, 1)
    conv_slice = causal_conv(rim_bc, proj_bc, taps_bc)
    conv_out = jnp.moveaxis(lax.all_gather(conv_slice, "head"), 0, 1).reshape(length, 2 * state_dim)
    block_count = length // BLOCK
    b_blocks = conv_out[:, :state_dim].reshape(block_count, BLOCK, state_dim)
    c_blocks = conv_out[:, state_dim:].reshape(block_count, BLOCK, state_dim)
    gram_mat = jnp.einsum("kqn,ksn->kqs", c_blocks, b_blocks, preferred_element_type=jnp.float32)
    step_dt = jax.nn.softplus(dt_raw + dt_bias)
    cum_decay = jnp.cumsum((-step_dt * decay_rate).reshape(block_count, BLOCK, heads_here), axis=1)
    dt_blocks = step_dt.reshape(block_count, BLOCK, heads_here)
    x_blocks = inputs_x.reshape(block_count, BLOCK, heads_here, head_dim)
    positions = jnp.arange(BLOCK)
    causal = positions[:, None] >= positions[None, :]
    cum_heads = jnp.moveaxis(cum_decay, 2, 1)
    dt_heads = jnp.moveaxis(dt_blocks, 2, 1)
    spread = cum_heads[:, :, :, None] - cum_heads[:, :, None, :]
    weights = (
        gram_mat[:, None]
        * jnp.exp(jnp.where(causal[None, None], spread, -jnp.inf))
        * dt_heads[:, :, None, :]
    ).astype(jnp.bfloat16)
    inside = jnp.einsum("khqs,kshp->kqhp", weights, x_blocks, preferred_element_type=jnp.float32)
    to_end = jnp.exp(cum_decay[:, -1:, :] - cum_decay) * dt_blocks
    scaled = (x_blocks.astype(jnp.float32) * to_end[:, :, :, None]).astype(jnp.bfloat16)
    block_ends = jnp.einsum("kqhp,kqn->khpn", scaled, b_blocks, preferred_element_type=jnp.float32)
    block_decay = cum_decay[:, -1, :]

    starts_local = jnp.stack(
        [weighted_prefix(block_ends, block_decay, k) for k in range(block_count)]
    )
    local_end = weighted_prefix(block_ends, block_decay, block_count)
    device_decay = jnp.sum(block_decay, axis=0)
    incoming = carried_in(device_decay, local_end, "scan")
    prior_decay = jnp.concatenate(
        [jnp.zeros((1, heads_here), jnp.float32), jnp.cumsum(block_decay, axis=0)[:-1]], axis=0
    )
    starts = jnp.exp(prior_decay)[:, :, None, None] * incoming[None] + starts_local
    carried = jnp.einsum(
        "kqn,khpn->kqhp", c_blocks.astype(jnp.float32), starts, precision=lax.Precision.HIGHEST
    )
    mixed_out = inside + jnp.exp(cum_decay)[:, :, :, None] * carried
    gated_out = mixed_out.reshape(length, heads_here, head_dim) * jax.nn.silu(gate_vals)
    normed = (
        (gated_out * lax.rsqrt(jnp.mean(gated_out * gated_out, axis=2, keepdims=True) + EPSILON))
        .astype(jnp.bfloat16)
        .reshape(length, heads_here * head_dim)
    )
    summed_out = jnp.dot(
        lax.all_gather(normed, "head", axis=1, tiled=True),
        w_out,
        preferred_element_type=jnp.float32,
    )
    return (stream.astype(jnp.float32) + summed_out).astype(jnp.bfloat16)


def local(stream, w_xz, w_bc, w_dt, dt_bias, decay_rate, conv_x, conv_bc, w_out):
    xz_cols = w_xz.shape[2]
    first = regroup(w_xz[:1], w_dt[:1])[0]
    second = regroup_by_gather(w_xz[1], w_dt[1])
    layer = lambda u, l, weights: mix_layer(
        u, weights, xz_cols, w_bc[l], dt_bias[l], decay_rate[l], conv_x[l], conv_bc[l], w_out[l]
    )
    raster_out = layer(stream, 0, first)
    members = lax.axis_size("scan")
    length = raster_out.shape[0]
    columns = raster_out.shape[1]
    grouped = raster_out.reshape(members, length // members, 1, columns)
    exchanged = lax.all_to_all(grouped, "scan", split_axis=0, concat_axis=2, tiled=True)
    return layer(exchanged.reshape(length, columns), 1, second)


def solution(mesh):
    placed = (
        P("scan", "head"),
        P(None, None, "head"),
        P(),
        P(None, None, "head"),
        P(None, "head"),
        P(None, "head"),
        P(None, None, "head"),
        P(),
        P(None, None, "head"),
    )
    return jax.shard_map(
        local, mesh=mesh, in_specs=placed, out_specs=P("scan", "head"), check_vma=False
    )
```

```python
import jax
import jax.numpy as jnp
from jax import lax
from jax.sharding import PartitionSpec as P

BLOCK = 256


EPSILON = 1e-05


def from_behind(shard, axis, by):
    devices = lax.axis_size(axis)
    pairs = [(i, i + by) for i in range(devices) if 0 <= i + by < devices]
    return lax.ppermute(shard, axis, pairs)


def weighted_prefix(states, decays, place):
    order = jnp.arange(states.shape[0])
    between = (order[:, None] < order[None, :]) & (order[None, :] < place)
    span = jnp.sum(jnp.where(between[:, :, None], decays[None, :, :], 0.0), axis=1)
    scale = jnp.where((order < place)[:, None], jnp.exp(span), 0.0)
    return jnp.sum(scale[:, :, None, None] * states, axis=0)


def carried_in(decay, state, axis):
    members = lax.axis_size(axis)
    heads, rows, cols = state.shape
    decay_row = jnp.zeros((1, cols), jnp.float32).at[0, :heads].set(decay)
    packed = jnp.concatenate([state.reshape(heads * rows, cols), decay_row], axis=0)
    gathered = lax.all_gather(packed.astype(jnp.bfloat16), axis).astype(jnp.float32)
    states = gathered[:, : heads * rows].reshape(members, heads, rows, cols)
    decays = gathered[:, heads * rows, :heads]
    return weighted_prefix(states, decays, lax.axis_index(axis))


def causal_conv(rim_rows, pre_conv, kernel):
    padded = jnp.concatenate([rim_rows, pre_conv], axis=0).astype(jnp.float32)
    length = pre_conv.shape[0]
    summed = jnp.zeros(pre_conv.shape, jnp.float32)
    for offset in range(kernel.shape[0]):
        summed = summed + kernel[offset] * padded[offset : offset + length]
    return jax.nn.silu(summed).astype(jnp.bfloat16)


def split_pair(values):
    high = values.astype(jnp.bfloat16)
    low = (values - high.astype(jnp.float32)).astype(jnp.bfloat16)
    return high, low


def regroup(w_xz, w_dt):
    inner = lax.axis_size("head")
    layers, features, _ = w_xz.shape
    packed = jnp.concatenate([w_xz, w_dt], axis=2)
    split = packed.reshape(layers, inner, features // inner, packed.shape[2])
    return lax.all_to_all(split, "head", 1, 1)


def regroup_shared(w_xz, w_dt):
    members = lax.axis_size("scan")
    core = lax.axis_index("scan") % 2
    own = regroup(
        jnp.where(core == 0, w_xz[:1], w_xz[1:2]), jnp.where(core == 0, w_dt[:1], w_dt[1:2])
    )[0]
    pairs = [(i, i ^ 1) for i in range(members)]
    other = lax.ppermute(own, "scan", pairs)
    return jnp.where(core == 0, own, other), jnp.where(core == 0, other, own)


def mix_layer(stream, regrouped, xz_cols, w_bc, dt_bias, decay_rate, conv_x, conv_bc, w_out):
    length, piece = stream.shape
    inner = lax.axis_size("head")
    spot = lax.axis_index("head")
    feature_count = piece * inner
    heads_here = regrouped.shape[2] - xz_cols
    head_dim = xz_cols // (2 * heads_here)
    state_dim = w_bc.shape[1] // 2
    taps = conv_x.shape[0]
    partial = jnp.einsum("tf,gfc->tgc", stream, regrouped, preferred_element_type=jnp.float32)
    rows_bc = lax.dynamic_slice_in_dim(w_bc, spot * piece, piece, 0)
    slice_bc = 2 * state_dim // inner
    partial_bc = jnp.dot(stream, rows_bc, preferred_element_type=jnp.float32).reshape(
        length, inner, slice_bc
    )
    wide_piece = stream.astype(jnp.float32)
    square_high, square_low = split_pair(jnp.sum(wide_piece * wide_piece, axis=1))
    squares = jnp.broadcast_to(
        jnp.stack([square_high, square_low], axis=1)[:, None], (length, inner, 2)
    )
    step_high, step_low = split_pair(partial[:, :, xz_cols:])
    outgoing = jnp.concatenate(
        [
            partial[:, :, :xz_cols].astype(jnp.bfloat16),
            partial_bc.astype(jnp.bfloat16),
            step_high,
            step_low,
            squares,
        ],
        axis=2,
    )
    arrived = lax.all_to_all(jnp.moveaxis(outgoing, 1, 0), "head", 0, 0).astype(jnp.float32)
    summed = jnp.sum(arrived, axis=0)
    summed_xz = summed[:, :xz_cols]
    summed_bc = summed[:, xz_cols : xz_cols + slice_bc]
    at = xz_cols + slice_bc
    dt_sum = summed[:, at : at + heads_here] + summed[:, at + heads_here : at + 2 * heads_here]
    square_sum = summed[:, at + 2 * heads_here :].sum(axis=1, keepdims=True)
    row_scale = lax.rsqrt(square_sum / feature_count + EPSILON)
    proj_xz = (
        (summed_xz.astype(jnp.float32) * row_scale)
        .astype(jnp.bfloat16)
        .reshape(length, heads_here, 2, head_dim)
    )
    proj_bc = (summed_bc * row_scale).astype(jnp.bfloat16)
    dt_raw = dt_sum * row_scale
    pre_x = proj_xz[:, :, 0, :].reshape(length, heads_here * head_dim)
    gate_vals = proj_xz[:, :, 1, :].astype(jnp.float32)
    rim_x, rim_bc = from_behind(
        (pre_x[length - taps + 1 :], proj_bc[length - taps + 1 :]), "scan", 1
    )
    inputs_x = causal_conv(rim_x, pre_x, conv_x)
    taps_bc = lax.dynamic_slice_in_dim(conv_bc, spot * slice_bc, slice_bc, 1)
    conv_slice = causal_conv(rim_bc, proj_bc, taps_bc)
    conv_out = jnp.moveaxis(lax.all_gather(conv_slice, "head"), 0, 1).reshape(length, 2 * state_dim)
    block_count = length // BLOCK
    b_blocks = conv_out[:, :state_dim].reshape(block_count, BLOCK, state_dim)
    c_blocks = conv_out[:, state_dim:].reshape(block_count, BLOCK, state_dim)
    gram_mat = jnp.einsum("kqn,ksn->kqs", c_blocks, b_blocks, preferred_element_type=jnp.float32)
    step_dt = jax.nn.softplus(dt_raw + dt_bias)
    cum_decay = jnp.cumsum((-step_dt * decay_rate).reshape(block_count, BLOCK, heads_here), axis=1)
    dt_blocks = step_dt.reshape(block_count, BLOCK, heads_here)
    x_blocks = inputs_x.reshape(block_count, BLOCK, heads_here, head_dim)
    positions = jnp.arange(BLOCK)
    causal = positions[:, None] >= positions[None, :]
    cum_heads = jnp.moveaxis(cum_decay, 2, 1)
    dt_heads = jnp.moveaxis(dt_blocks, 2, 1)
    spread = cum_heads[:, :, :, None] - cum_heads[:, :, None, :]
    weights = (
        gram_mat[:, None]
        * jnp.exp(jnp.where(causal[None, None], spread, -jnp.inf))
        * dt_heads[:, :, None, :]
    ).astype(jnp.bfloat16)
    inside = jnp.einsum("khqs,kshp->kqhp", weights, x_blocks, preferred_element_type=jnp.float32)
    to_end = jnp.exp(cum_decay[:, -1:, :] - cum_decay) * dt_blocks
    scaled = (x_blocks.astype(jnp.float32) * to_end[:, :, :, None]).astype(jnp.bfloat16)
    block_ends = jnp.einsum("kqhp,kqn->khpn", scaled, b_blocks, preferred_element_type=jnp.float32)
    block_decay = cum_decay[:, -1, :]

    starts_local = jnp.stack(
        [weighted_prefix(block_ends, block_decay, k) for k in range(block_count)]
    )
    local_end = weighted_prefix(block_ends, block_decay, block_count)
    device_decay = jnp.sum(block_decay, axis=0)
    incoming = carried_in(device_decay, local_end, "scan")
    prior_decay = jnp.concatenate(
        [jnp.zeros((1, heads_here), jnp.float32), jnp.cumsum(block_decay, axis=0)[:-1]], axis=0
    )
    starts = jnp.exp(prior_decay)[:, :, None, None] * incoming[None] + starts_local
    carried = jnp.einsum(
        "kqn,khpn->kqhp", c_blocks.astype(jnp.float32), starts, precision=lax.Precision.HIGHEST
    )
    mixed_out = inside + jnp.exp(cum_decay)[:, :, :, None] * carried
    gated_out = mixed_out.reshape(length, heads_here, head_dim) * jax.nn.silu(gate_vals)
    normed = (
        (gated_out * lax.rsqrt(jnp.mean(gated_out * gated_out, axis=2, keepdims=True) + EPSILON))
        .astype(jnp.bfloat16)
        .reshape(length, heads_here * head_dim)
    )
    summed_out = jnp.dot(
        lax.all_gather(normed, "head", axis=1, tiled=True),
        w_out,
        preferred_element_type=jnp.float32,
    )
    return (stream.astype(jnp.float32) + summed_out).astype(jnp.bfloat16)


def local(stream, w_xz, w_bc, w_dt, dt_bias, decay_rate, conv_x, conv_bc, w_out):
    xz_cols = w_xz.shape[2]
    first, second = regroup_shared(w_xz, w_dt)
    layer = lambda u, l, weights: mix_layer(
        u, weights, xz_cols, w_bc[l], dt_bias[l], decay_rate[l], conv_x[l], conv_bc[l], w_out[l]
    )
    raster_out = layer(stream, 0, first)
    members = lax.axis_size("scan")
    length = raster_out.shape[0]
    columns = raster_out.shape[1]
    grouped = raster_out.reshape(members, length // members, 1, columns)
    exchanged = lax.all_to_all(grouped, "scan", split_axis=0, concat_axis=2, tiled=True)
    return layer(exchanged.reshape(length, columns), 1, second)


def solution(mesh):
    placed = (
        P("scan", "head"),
        P(None, None, "head"),
        P(),
        P(None, None, "head"),
        P(None, "head"),
        P(None, "head"),
        P(None, None, "head"),
        P(),
        P(None, None, "head"),
    )
    return jax.shard_map(
        local, mesh=mesh, in_specs=placed, out_specs=P("scan", "head"), check_vma=False
    )
```

```python
import jax
import jax.numpy as jnp
from jax import lax
from jax.sharding import PartitionSpec as P

BLOCK = 256


EPSILON = 1e-05


def from_behind(shard, axis, by):
    devices = lax.axis_size(axis)
    pairs = [(i, i + by) for i in range(devices) if 0 <= i + by < devices]
    return lax.ppermute(shard, axis, pairs)


def weighted_prefix(states, decays, place):
    order = jnp.arange(states.shape[0])
    between = (order[:, None] < order[None, :]) & (order[None, :] < place)
    span = jnp.sum(jnp.where(between[:, :, None], decays[None, :, :], 0.0), axis=1)
    scale = jnp.where((order < place)[:, None], jnp.exp(span), 0.0)
    return jnp.sum(scale[:, :, None, None] * states, axis=0)


def carried_in(decay, state, axis):
    members = lax.axis_size(axis)
    heads, rows, cols = state.shape
    decay_row = jnp.zeros((1, cols), jnp.float32).at[0, :heads].set(decay)
    packed = jnp.concatenate([state.reshape(heads * rows, cols), decay_row], axis=0)
    gathered = lax.all_gather(packed.astype(jnp.bfloat16), axis).astype(jnp.float32)
    states = gathered[:, : heads * rows].reshape(members, heads, rows, cols)
    decays = gathered[:, heads * rows, :heads]
    return weighted_prefix(states, decays, lax.axis_index(axis))


def causal_conv(rim_rows, pre_conv, kernel):
    padded = jnp.concatenate([rim_rows, pre_conv], axis=0).astype(jnp.float32)
    length = pre_conv.shape[0]
    summed = jnp.zeros(pre_conv.shape, jnp.float32)
    for offset in range(kernel.shape[0]):
        summed = summed + kernel[offset] * padded[offset : offset + length]
    return jax.nn.silu(summed).astype(jnp.bfloat16)


def split_pair(values):
    high = values.astype(jnp.bfloat16)
    low = (values - high.astype(jnp.float32)).astype(jnp.bfloat16)
    return high, low


def regroup(w_xz, w_dt):
    inner = lax.axis_size("head")
    layers, features, _ = w_xz.shape
    packed = jnp.concatenate([w_xz, w_dt], axis=2)
    split = packed.reshape(layers, inner, features // inner, packed.shape[2])
    return lax.all_to_all(split, "head", 1, 1)


def regroup_shared(w_xz, w_dt):
    members = lax.axis_size("scan")
    core = lax.axis_index("scan") % 2
    own = regroup(
        jnp.where(core == 0, w_xz[:1], w_xz[1:2]), jnp.where(core == 0, w_dt[:1], w_dt[1:2])
    )[0]
    pairs = [(i, i ^ 1) for i in range(members)]
    other = lax.ppermute(own, "scan", pairs)
    return jnp.where(core == 0, own, other), jnp.where(core == 0, other, own)


def gather_heads(values):
    inner = lax.axis_size("head")
    me = lax.axis_index("head")
    pieces = [values] + [
        lax.ppermute(values, "head", [(i, (i + shift) % inner) for i in range(inner)])
        for shift in range(1, inner)
    ]
    flipped = jnp.stack(pieces[::-1])
    doubled = jnp.concatenate([flipped, flipped], axis=0)
    return lax.dynamic_slice_in_dim(doubled, inner - 1 - me, inner, 0)


def mix_layer(stream, regrouped, xz_cols, w_bc, dt_bias, decay_rate, conv_x, conv_bc, w_out):
    length, piece = stream.shape
    inner = lax.axis_size("head")
    spot = lax.axis_index("head")
    feature_count = piece * inner
    heads_here = regrouped.shape[2] - xz_cols
    head_dim = xz_cols // (2 * heads_here)
    state_dim = w_bc.shape[1] // 2
    taps = conv_x.shape[0]
    partial = jnp.einsum("tf,gfc->tgc", stream, regrouped, preferred_element_type=jnp.float32)
    rows_bc = lax.dynamic_slice_in_dim(w_bc, spot * piece, piece, 0)
    slice_bc = 2 * state_dim // inner
    partial_bc = jnp.dot(stream, rows_bc, preferred_element_type=jnp.float32).reshape(
        length, inner, slice_bc
    )
    wide_piece = stream.astype(jnp.float32)
    square_high, square_low = split_pair(jnp.sum(wide_piece * wide_piece, axis=1))
    squares = jnp.broadcast_to(
        jnp.stack([square_high, square_low], axis=1)[:, None], (length, inner, 2)
    )
    step_high, step_low = split_pair(partial[:, :, xz_cols:])
    outgoing = jnp.concatenate(
        [
            partial[:, :, :xz_cols].astype(jnp.bfloat16),
            partial_bc.astype(jnp.bfloat16),
            step_high,
            step_low,
            squares,
        ],
        axis=2,
    )
    arrived = lax.all_to_all(jnp.moveaxis(outgoing, 1, 0), "head", 0, 0).astype(jnp.float32)
    summed = jnp.sum(arrived, axis=0)
    summed_xz = summed[:, :xz_cols]
    summed_bc = summed[:, xz_cols : xz_cols + slice_bc]
    at = xz_cols + slice_bc
    dt_sum = summed[:, at : at + heads_here] + summed[:, at + heads_here : at + 2 * heads_here]
    square_sum = summed[:, at + 2 * heads_here :].sum(axis=1, keepdims=True)
    row_scale = lax.rsqrt(square_sum / feature_count + EPSILON)
    proj_xz = (
        (summed_xz.astype(jnp.float32) * row_scale)
        .astype(jnp.bfloat16)
        .reshape(length, heads_here, 2, head_dim)
    )
    proj_bc = (summed_bc * row_scale).astype(jnp.bfloat16)
    dt_raw = dt_sum * row_scale
    pre_x = proj_xz[:, :, 0, :].reshape(length, heads_here * head_dim)
    gate_vals = proj_xz[:, :, 1, :].astype(jnp.float32)
    rim_x, rim_bc = from_behind(
        (pre_x[length - taps + 1 :], proj_bc[length - taps + 1 :]), "scan", 1
    )
    inputs_x = causal_conv(rim_x, pre_x, conv_x)
    taps_bc = lax.dynamic_slice_in_dim(conv_bc, spot * slice_bc, slice_bc, 1)
    conv_slice = causal_conv(rim_bc, proj_bc, taps_bc)
    conv_out = jnp.moveaxis(gather_heads(conv_slice), 0, 1).reshape(length, 2 * state_dim)
    block_count = length // BLOCK
    b_blocks = conv_out[:, :state_dim].reshape(block_count, BLOCK, state_dim)
    c_blocks = conv_out[:, state_dim:].reshape(block_count, BLOCK, state_dim)
    gram_mat = jnp.einsum("kqn,ksn->kqs", c_blocks, b_blocks, preferred_element_type=jnp.float32)
    step_dt = jax.nn.softplus(dt_raw + dt_bias)
    cum_decay = jnp.cumsum((-step_dt * decay_rate).reshape(block_count, BLOCK, heads_here), axis=1)
    dt_blocks = step_dt.reshape(block_count, BLOCK, heads_here)
    x_blocks = inputs_x.reshape(block_count, BLOCK, heads_here, head_dim)
    positions = jnp.arange(BLOCK)
    causal = positions[:, None] >= positions[None, :]
    cum_heads = jnp.moveaxis(cum_decay, 2, 1)
    dt_heads = jnp.moveaxis(dt_blocks, 2, 1)
    spread = cum_heads[:, :, :, None] - cum_heads[:, :, None, :]
    weights = (
        gram_mat[:, None]
        * jnp.exp(jnp.where(causal[None, None], spread, -jnp.inf))
        * dt_heads[:, :, None, :]
    ).astype(jnp.bfloat16)
    inside = jnp.einsum("khqs,kshp->kqhp", weights, x_blocks, preferred_element_type=jnp.float32)
    to_end = jnp.exp(cum_decay[:, -1:, :] - cum_decay) * dt_blocks
    scaled = (x_blocks.astype(jnp.float32) * to_end[:, :, :, None]).astype(jnp.bfloat16)
    block_ends = jnp.einsum("kqhp,kqn->khpn", scaled, b_blocks, preferred_element_type=jnp.float32)
    block_decay = cum_decay[:, -1, :]

    starts_local = jnp.stack(
        [weighted_prefix(block_ends, block_decay, k) for k in range(block_count)]
    )
    local_end = weighted_prefix(block_ends, block_decay, block_count)
    device_decay = jnp.sum(block_decay, axis=0)
    incoming = carried_in(device_decay, local_end, "scan")
    prior_decay = jnp.concatenate(
        [jnp.zeros((1, heads_here), jnp.float32), jnp.cumsum(block_decay, axis=0)[:-1]], axis=0
    )
    starts = jnp.exp(prior_decay)[:, :, None, None] * incoming[None] + starts_local
    carried = jnp.einsum(
        "kqn,khpn->kqhp", c_blocks.astype(jnp.float32), starts, precision=lax.Precision.HIGHEST
    )
    mixed_out = inside + jnp.exp(cum_decay)[:, :, :, None] * carried
    gated_out = mixed_out.reshape(length, heads_here, head_dim) * jax.nn.silu(gate_vals)
    normed = (
        (gated_out * lax.rsqrt(jnp.mean(gated_out * gated_out, axis=2, keepdims=True) + EPSILON))
        .astype(jnp.bfloat16)
        .reshape(length, heads_here * head_dim)
    )
    summed_out = jnp.dot(
        jnp.moveaxis(gather_heads(normed), 0, 1).reshape(length, inner * normed.shape[1]),
        w_out,
        preferred_element_type=jnp.float32,
    )
    return (stream.astype(jnp.float32) + summed_out).astype(jnp.bfloat16)


def local(stream, w_xz, w_bc, w_dt, dt_bias, decay_rate, conv_x, conv_bc, w_out):
    xz_cols = w_xz.shape[2]
    first, second = regroup_shared(w_xz, w_dt)
    layer = lambda u, l, weights: mix_layer(
        u, weights, xz_cols, w_bc[l], dt_bias[l], decay_rate[l], conv_x[l], conv_bc[l], w_out[l]
    )
    raster_out = layer(stream, 0, first)
    members = lax.axis_size("scan")
    length = raster_out.shape[0]
    columns = raster_out.shape[1]
    grouped = raster_out.reshape(members, length // members, 1, columns)
    exchanged = lax.all_to_all(grouped, "scan", split_axis=0, concat_axis=2, tiled=True)
    return layer(exchanged.reshape(length, columns), 1, second)


def solution(mesh):
    placed = (
        P("scan", "head"),
        P(None, None, "head"),
        P(),
        P(None, None, "head"),
        P(None, "head"),
        P(None, "head"),
        P(None, None, "head"),
        P(),
        P(None, None, "head"),
    )
    return jax.shard_map(
        local, mesh=mesh, in_specs=placed, out_specs=P("scan", "head"), check_vma=False
    )
```

```python
import jax
import jax.numpy as jnp
from jax import lax
from jax.sharding import PartitionSpec as P

BLOCK = 256


EPSILON = 1e-05


def from_behind(shard, axis, by):
    devices = lax.axis_size(axis)
    pairs = [(i, i + by) for i in range(devices) if 0 <= i + by < devices]
    return lax.ppermute(shard, axis, pairs)


def weighted_prefix(states, decays, place):
    order = jnp.arange(states.shape[0])
    between = (order[:, None] < order[None, :]) & (order[None, :] < place)
    span = jnp.sum(jnp.where(between[:, :, None], decays[None, :, :], 0.0), axis=1)
    scale = jnp.where((order < place)[:, None], jnp.exp(span), 0.0)
    return jnp.sum(scale[:, :, None, None] * states, axis=0)


def carried_in(decay, state, axis):
    members = lax.axis_size(axis)
    heads, rows, cols = state.shape
    decay_row = jnp.zeros((1, cols), jnp.float32).at[0, :heads].set(decay)
    packed = jnp.concatenate([state.reshape(heads * rows, cols), decay_row], axis=0)
    gathered = lax.all_gather(packed.astype(jnp.bfloat16), axis).astype(jnp.float32)
    states = gathered[:, : heads * rows].reshape(members, heads, rows, cols)
    decays = gathered[:, heads * rows, :heads]
    return weighted_prefix(states, decays, lax.axis_index(axis))


def causal_conv(rim_rows, pre_conv, kernel):
    padded = jnp.concatenate([rim_rows, pre_conv], axis=0).astype(jnp.float32)
    length = pre_conv.shape[0]
    summed = jnp.zeros(pre_conv.shape, jnp.float32)
    for offset in range(kernel.shape[0]):
        summed = summed + kernel[offset] * padded[offset : offset + length]
    return jax.nn.silu(summed).astype(jnp.bfloat16)


def split_pair(values):
    high = values.astype(jnp.bfloat16)
    low = (values - high.astype(jnp.float32)).astype(jnp.bfloat16)
    return high, low


def regroup(w_xz, w_dt):
    inner = lax.axis_size("head")
    layers, features, _ = w_xz.shape
    packed = jnp.concatenate([w_xz, w_dt], axis=2)
    split = packed.reshape(layers, inner, features // inner, packed.shape[2])
    return lax.all_to_all(split, "head", 1, 1)


def regroup_shared(w_xz, w_dt):
    members = lax.axis_size("scan")
    core = lax.axis_index("scan") % 2
    own = regroup(
        jnp.where(core == 0, w_xz[:1], w_xz[1:2]), jnp.where(core == 0, w_dt[:1], w_dt[1:2])
    )[0]
    pairs = [(i, i ^ 1) for i in range(members)]
    other = lax.ppermute(own, "scan", pairs)
    return jnp.where(core == 0, own, other), jnp.where(core == 0, other, own)


def gather_heads(values):
    inner = lax.axis_size("head")
    me = lax.axis_index("head")
    pieces = [values] + [
        lax.ppermute(values, "head", [(i, (i + shift) % inner) for i in range(inner)])
        for shift in range(1, inner)
    ]
    flipped = jnp.stack(pieces[::-1])
    doubled = jnp.concatenate([flipped, flipped], axis=0)
    return lax.dynamic_slice_in_dim(doubled, inner - 1 - me, inner, 0)


def mix_layer(stream, rim_rows, regrouped, xz_cols, w_bc, dt_bias, decay_rate, conv_x, conv_bc, w_out):
    length, piece = stream.shape
    inner = lax.axis_size("head")
    spot = lax.axis_index("head")
    feature_count = piece * inner
    heads_here = regrouped.shape[2] - xz_cols
    head_dim = xz_cols // (2 * heads_here)
    state_dim = w_bc.shape[1] // 2
    taps = conv_x.shape[0]
    extended = jnp.concatenate([rim_rows, stream], axis=0)
    wide_length = extended.shape[0]
    partial = jnp.einsum("tf,gfc->tgc", extended, regrouped, preferred_element_type=jnp.float32)
    rows_bc = lax.dynamic_slice_in_dim(w_bc, spot * piece, piece, 0)
    slice_bc = 2 * state_dim // inner
    partial_bc = jnp.dot(extended, rows_bc, preferred_element_type=jnp.float32).reshape(
        wide_length, inner, slice_bc
    )
    wide_piece = extended.astype(jnp.float32)
    square_high, square_low = split_pair(jnp.sum(wide_piece * wide_piece, axis=1))
    squares = jnp.broadcast_to(
        jnp.stack([square_high, square_low], axis=1)[:, None], (wide_length, inner, 2)
    )
    step_high, step_low = split_pair(partial[:, :, xz_cols:])
    outgoing = jnp.concatenate(
        [
            partial[:, :, :xz_cols].astype(jnp.bfloat16),
            partial_bc.astype(jnp.bfloat16),
            step_high,
            step_low,
            squares,
        ],
        axis=2,
    )
    arrived = lax.all_to_all(jnp.moveaxis(outgoing, 1, 0), "head", 0, 0).astype(jnp.float32)
    summed = jnp.sum(arrived, axis=0)
    summed_xz = summed[:, :xz_cols]
    summed_bc = summed[:, xz_cols : xz_cols + slice_bc]
    at = xz_cols + slice_bc
    dt_sum = summed[:, at : at + heads_here] + summed[:, at + heads_here : at + 2 * heads_here]
    square_sum = summed[:, at + 2 * heads_here :].sum(axis=1, keepdims=True)
    row_scale = lax.rsqrt(square_sum / feature_count + EPSILON)
    proj_xz = (
        (summed_xz * row_scale)
        .astype(jnp.bfloat16)
        .reshape(wide_length, heads_here, 2, head_dim)
    )
    proj_bc_wide = (summed_bc * row_scale).astype(jnp.bfloat16)
    dt_raw = (dt_sum * row_scale)[taps - 1 :]
    pre_wide = proj_xz[:, :, 0, :].reshape(wide_length, heads_here * head_dim)
    gate_vals = proj_xz[taps - 1 :, :, 1, :].astype(jnp.float32)
    rim_x, pre_x = pre_wide[: taps - 1], pre_wide[taps - 1 :]
    rim_bc, proj_bc = proj_bc_wide[: taps - 1], proj_bc_wide[taps - 1 :]
    inputs_x = causal_conv(rim_x, pre_x, conv_x)
    taps_bc = lax.dynamic_slice_in_dim(conv_bc, spot * slice_bc, slice_bc, 1)
    conv_slice = causal_conv(rim_bc, proj_bc, taps_bc)
    conv_out = jnp.moveaxis(gather_heads(conv_slice), 0, 1).reshape(length, 2 * state_dim)
    block_count = length // BLOCK
    b_blocks = conv_out[:, :state_dim].reshape(block_count, BLOCK, state_dim)
    c_blocks = conv_out[:, state_dim:].reshape(block_count, BLOCK, state_dim)
    gram_mat = jnp.einsum("kqn,ksn->kqs", c_blocks, b_blocks, preferred_element_type=jnp.float32)
    step_dt = jax.nn.softplus(dt_raw + dt_bias)
    cum_decay = jnp.cumsum((-step_dt * decay_rate).reshape(block_count, BLOCK, heads_here), axis=1)
    dt_blocks = step_dt.reshape(block_count, BLOCK, heads_here)
    x_blocks = inputs_x.reshape(block_count, BLOCK, heads_here, head_dim)
    positions = jnp.arange(BLOCK)
    causal = positions[:, None] >= positions[None, :]
    cum_heads = jnp.moveaxis(cum_decay, 2, 1)
    dt_heads = jnp.moveaxis(dt_blocks, 2, 1)
    spread = cum_heads[:, :, :, None] - cum_heads[:, :, None, :]
    weights = (
        gram_mat[:, None]
        * jnp.exp(jnp.where(causal[None, None], spread, -jnp.inf))
        * dt_heads[:, :, None, :]
    ).astype(jnp.bfloat16)
    inside = jnp.einsum("khqs,kshp->kqhp", weights, x_blocks, preferred_element_type=jnp.float32)
    to_end = jnp.exp(cum_decay[:, -1:, :] - cum_decay) * dt_blocks
    scaled = (x_blocks.astype(jnp.float32) * to_end[:, :, :, None]).astype(jnp.bfloat16)
    block_ends = jnp.einsum("kqhp,kqn->khpn", scaled, b_blocks, preferred_element_type=jnp.float32)
    block_decay = cum_decay[:, -1, :]

    starts_local = jnp.stack(
        [weighted_prefix(block_ends, block_decay, k) for k in range(block_count)]
    )
    local_end = weighted_prefix(block_ends, block_decay, block_count)
    device_decay = jnp.sum(block_decay, axis=0)
    incoming = carried_in(device_decay, local_end, "scan")
    prior_decay = jnp.concatenate(
        [jnp.zeros((1, heads_here), jnp.float32), jnp.cumsum(block_decay, axis=0)[:-1]], axis=0
    )
    starts = jnp.exp(prior_decay)[:, :, None, None] * incoming[None] + starts_local
    carried = jnp.einsum(
        "kqn,khpn->kqhp", c_blocks.astype(jnp.float32), starts, precision=lax.Precision.HIGHEST
    )
    mixed_out = inside + jnp.exp(cum_decay)[:, :, :, None] * carried
    gated_out = mixed_out.reshape(length, heads_here, head_dim) * jax.nn.silu(gate_vals)
    normed = (
        (gated_out * lax.rsqrt(jnp.mean(gated_out * gated_out, axis=2, keepdims=True) + EPSILON))
        .astype(jnp.bfloat16)
        .reshape(length, heads_here * head_dim)
    )
    summed_out = jnp.dot(
        jnp.moveaxis(gather_heads(normed), 0, 1).reshape(length, inner * normed.shape[1]),
        w_out,
        preferred_element_type=jnp.float32,
    )
    return (stream.astype(jnp.float32) + summed_out).astype(jnp.bfloat16)


def local(stream, w_xz, w_bc, w_dt, dt_bias, decay_rate, conv_x, conv_bc, w_out):
    xz_cols = w_xz.shape[2]
    first, second = regroup_shared(w_xz, w_dt)
    layer = lambda u, rim, l, weights: mix_layer(
        u, rim, weights, xz_cols, w_bc[l], dt_bias[l], decay_rate[l], conv_x[l], conv_bc[l], w_out[l]
    )
    taps = conv_x.shape[1]
    raster_out = layer(stream, from_behind(stream[stream.shape[0] - taps + 1 :], "scan", 1), 0, first)
    members = lax.axis_size("scan")
    length = raster_out.shape[0]
    columns = raster_out.shape[1]
    span = length // members
    padded = jnp.concatenate([jnp.zeros((1, columns), raster_out.dtype), raster_out], axis=0)
    windows = jnp.stack([padded[j * span : j * span + span + 1] for j in range(members)])
    landed = lax.all_to_all(windows, "scan", 0, 0)
    reordered = jnp.moveaxis(landed[:, 1:], 0, 1).reshape(length, columns)
    rim = landed[members - taps + 1 :, 0]
    return layer(reordered, rim, 1, second)


def solution(mesh):
    placed = (
        P("scan", "head"),
        P(None, None, "head"),
        P(),
        P(None, None, "head"),
        P(None, "head"),
        P(None, "head"),
        P(None, None, "head"),
        P(),
        P(None, None, "head"),
    )
    return jax.shard_map(
        local, mesh=mesh, in_specs=placed, out_specs=P("scan", "head"), check_vma=False
    )
```

```python
import jax
import jax.numpy as jnp
from jax import lax
from jax.sharding import PartitionSpec as P

BLOCK = 256


EPSILON = 1e-05


def from_behind(shard, axis, by):
    devices = lax.axis_size(axis)
    pairs = [(i, i + by) for i in range(devices) if 0 <= i + by < devices]
    return lax.ppermute(shard, axis, pairs)


def weighted_prefix(states, decays, place):
    order = jnp.arange(states.shape[0])
    between = (order[:, None] < order[None, :]) & (order[None, :] < place)
    span = jnp.sum(jnp.where(between[:, :, None], decays[None, :, :], 0.0), axis=1)
    scale = jnp.where((order < place)[:, None], jnp.exp(span), 0.0)
    return jnp.sum(scale[:, :, None, None] * states, axis=0)


def carried_in(decay, state, axis):
    members = lax.axis_size(axis)
    heads, rows, cols = state.shape
    decay_row = jnp.zeros((1, cols), jnp.float32).at[0, :heads].set(decay)
    packed = jnp.concatenate([state.reshape(heads * rows, cols), decay_row], axis=0)
    packed = packed.astype(jnp.bfloat16)
    total = jnp.zeros(state.shape, jnp.float32)
    passed = jnp.zeros((heads,), jnp.float32)
    for shift in range(1, members):
        pairs = [(i, i + shift) for i in range(members - shift)]
        earlier = lax.ppermute(packed, axis, pairs).astype(jnp.float32)
        total = total + jnp.exp(passed)[:, None, None] * earlier[: heads * rows].reshape(state.shape)
        passed = passed + earlier[heads * rows, :heads]
    return total


def causal_conv(rim_rows, pre_conv, kernel):
    padded = jnp.concatenate([rim_rows, pre_conv], axis=0).astype(jnp.float32)
    length = pre_conv.shape[0]
    summed = jnp.zeros(pre_conv.shape, jnp.float32)
    for offset in range(kernel.shape[0]):
        summed = summed + kernel[offset] * padded[offset : offset + length]
    return jax.nn.silu(summed).astype(jnp.bfloat16)


def split_pair(values):
    high = values.astype(jnp.bfloat16)
    low = (values - high.astype(jnp.float32)).astype(jnp.bfloat16)
    return high, low


def regroup(w_xz, w_dt):
    inner = lax.axis_size("head")
    layers, features, _ = w_xz.shape
    packed = jnp.concatenate([w_xz, w_dt], axis=2)
    split = packed.reshape(layers, inner, features // inner, packed.shape[2])
    return lax.all_to_all(split, "head", 1, 1)


def regroup_shared(w_xz, w_dt):
    members = lax.axis_size("scan")
    core = lax.axis_index("scan") % 2
    own = regroup(
        jnp.where(core == 0, w_xz[:1], w_xz[1:2]), jnp.where(core == 0, w_dt[:1], w_dt[1:2])
    )[0]
    pairs = [(i, i ^ 1) for i in range(members)]
    other = lax.ppermute(own, "scan", pairs)
    return jnp.where(core == 0, own, other), jnp.where(core == 0, other, own)


def gather_heads(values):
    inner = lax.axis_size("head")
    me = lax.axis_index("head")
    pieces = [values] + [
        lax.ppermute(values, "head", [(i, (i + shift) % inner) for i in range(inner)])
        for shift in range(1, inner)
    ]
    flipped = jnp.stack(pieces[::-1])
    doubled = jnp.concatenate([flipped, flipped], axis=0)
    return lax.dynamic_slice_in_dim(doubled, inner - 1 - me, inner, 0)


def mix_layer(stream, regrouped, xz_cols, w_bc, dt_bias, decay_rate, conv_x, conv_bc, w_out):
    length, piece = stream.shape
    inner = lax.axis_size("head")
    spot = lax.axis_index("head")
    feature_count = piece * inner
    heads_here = regrouped.shape[2] - xz_cols
    head_dim = xz_cols // (2 * heads_here)
    state_dim = w_bc.shape[1] // 2
    taps = conv_x.shape[0]
    partial = jnp.einsum("tf,gfc->tgc", stream, regrouped, preferred_element_type=jnp.float32)
    rows_bc = lax.dynamic_slice_in_dim(w_bc, spot * piece, piece, 0)
    slice_bc = 2 * state_dim // inner
    partial_bc = jnp.dot(stream, rows_bc, preferred_element_type=jnp.float32).reshape(
        length, inner, slice_bc
    )
    wide_piece = stream.astype(jnp.float32)
    square_high, square_low = split_pair(jnp.sum(wide_piece * wide_piece, axis=1))
    squares = jnp.broadcast_to(
        jnp.stack([square_high, square_low], axis=1)[:, None], (length, inner, 2)
    )
    step_high, step_low = split_pair(partial[:, :, xz_cols:])
    outgoing = jnp.concatenate(
        [
            partial[:, :, :xz_cols].astype(jnp.bfloat16),
            partial_bc.astype(jnp.bfloat16),
            step_high,
            step_low,
            squares,
        ],
        axis=2,
    )
    arrived = lax.all_to_all(jnp.moveaxis(outgoing, 1, 0), "head", 0, 0).astype(jnp.float32)
    summed = jnp.sum(arrived, axis=0)
    summed_xz = summed[:, :xz_cols]
    summed_bc = summed[:, xz_cols : xz_cols + slice_bc]
    at = xz_cols + slice_bc
    dt_sum = summed[:, at : at + heads_here] + summed[:, at + heads_here : at + 2 * heads_here]
    square_sum = summed[:, at + 2 * heads_here :].sum(axis=1, keepdims=True)
    row_scale = lax.rsqrt(square_sum / feature_count + EPSILON)
    proj_xz = (
        (summed_xz.astype(jnp.float32) * row_scale)
        .astype(jnp.bfloat16)
        .reshape(length, heads_here, 2, head_dim)
    )
    proj_bc = (summed_bc * row_scale).astype(jnp.bfloat16)
    dt_raw = dt_sum * row_scale
    pre_x = proj_xz[:, :, 0, :].reshape(length, heads_here * head_dim)
    gate_vals = proj_xz[:, :, 1, :].astype(jnp.float32)
    rim_x, rim_bc = from_behind(
        (pre_x[length - taps + 1 :], proj_bc[length - taps + 1 :]), "scan", 1
    )
    inputs_x = causal_conv(rim_x, pre_x, conv_x)
    taps_bc = lax.dynamic_slice_in_dim(conv_bc, spot * slice_bc, slice_bc, 1)
    conv_slice = causal_conv(rim_bc, proj_bc, taps_bc)
    conv_out = jnp.moveaxis(gather_heads(conv_slice), 0, 1).reshape(length, 2 * state_dim)
    block_count = length // BLOCK
    b_blocks = conv_out[:, :state_dim].reshape(block_count, BLOCK, state_dim)
    c_blocks = conv_out[:, state_dim:].reshape(block_count, BLOCK, state_dim)
    gram_mat = jnp.einsum("kqn,ksn->kqs", c_blocks, b_blocks, preferred_element_type=jnp.float32)
    step_dt = jax.nn.softplus(dt_raw + dt_bias)
    cum_decay = jnp.cumsum((-step_dt * decay_rate).reshape(block_count, BLOCK, heads_here), axis=1)
    dt_blocks = step_dt.reshape(block_count, BLOCK, heads_here)
    x_blocks = inputs_x.reshape(block_count, BLOCK, heads_here, head_dim)
    positions = jnp.arange(BLOCK)
    causal = positions[:, None] >= positions[None, :]
    cum_heads = jnp.moveaxis(cum_decay, 2, 1)
    dt_heads = jnp.moveaxis(dt_blocks, 2, 1)
    spread = cum_heads[:, :, :, None] - cum_heads[:, :, None, :]
    weights = (
        gram_mat[:, None]
        * jnp.exp(jnp.where(causal[None, None], spread, -jnp.inf))
        * dt_heads[:, :, None, :]
    ).astype(jnp.bfloat16)
    inside = jnp.einsum("khqs,kshp->kqhp", weights, x_blocks, preferred_element_type=jnp.float32)
    to_end = jnp.exp(cum_decay[:, -1:, :] - cum_decay) * dt_blocks
    scaled = (x_blocks.astype(jnp.float32) * to_end[:, :, :, None]).astype(jnp.bfloat16)
    block_ends = jnp.einsum("kqhp,kqn->khpn", scaled, b_blocks, preferred_element_type=jnp.float32)
    block_decay = cum_decay[:, -1, :]

    starts_local = jnp.stack(
        [weighted_prefix(block_ends, block_decay, k) for k in range(block_count)]
    )
    local_end = weighted_prefix(block_ends, block_decay, block_count)
    device_decay = jnp.sum(block_decay, axis=0)
    incoming = carried_in(device_decay, local_end, "scan")
    prior_decay = jnp.concatenate(
        [jnp.zeros((1, heads_here), jnp.float32), jnp.cumsum(block_decay, axis=0)[:-1]], axis=0
    )
    starts = jnp.exp(prior_decay)[:, :, None, None] * incoming[None] + starts_local
    carried = jnp.einsum(
        "kqn,khpn->kqhp", c_blocks.astype(jnp.float32), starts, precision=lax.Precision.HIGHEST
    )
    mixed_out = inside + jnp.exp(cum_decay)[:, :, :, None] * carried
    gated_out = mixed_out.reshape(length, heads_here, head_dim) * jax.nn.silu(gate_vals)
    normed = (
        (gated_out * lax.rsqrt(jnp.mean(gated_out * gated_out, axis=2, keepdims=True) + EPSILON))
        .astype(jnp.bfloat16)
        .reshape(length, heads_here * head_dim)
    )
    summed_out = jnp.dot(
        jnp.moveaxis(gather_heads(normed), 0, 1).reshape(length, inner * normed.shape[1]),
        w_out,
        preferred_element_type=jnp.float32,
    )
    return (stream.astype(jnp.float32) + summed_out).astype(jnp.bfloat16)


def local(stream, w_xz, w_bc, w_dt, dt_bias, decay_rate, conv_x, conv_bc, w_out):
    xz_cols = w_xz.shape[2]
    first, second = regroup_shared(w_xz, w_dt)
    layer = lambda u, l, weights: mix_layer(
        u, weights, xz_cols, w_bc[l], dt_bias[l], decay_rate[l], conv_x[l], conv_bc[l], w_out[l]
    )
    raster_out = layer(stream, 0, first)
    members = lax.axis_size("scan")
    length = raster_out.shape[0]
    columns = raster_out.shape[1]
    grouped = raster_out.reshape(members, length // members, 1, columns)
    exchanged = lax.all_to_all(grouped, "scan", split_axis=0, concat_axis=2, tiled=True)
    return layer(exchanged.reshape(length, columns), 1, second)


def solution(mesh):
    placed = (
        P("scan", "head"),
        P(None, None, "head"),
        P(),
        P(None, None, "head"),
        P(None, "head"),
        P(None, "head"),
        P(None, None, "head"),
        P(),
        P(None, None, "head"),
    )
    return jax.shard_map(
        local, mesh=mesh, in_specs=placed, out_specs=P("scan", "head"), check_vma=False
    )
```

```python
import jax
import jax.numpy as jnp
from jax import lax
from jax.sharding import PartitionSpec as P

BLOCK = 256


EPSILON = 1e-05


def from_behind(shard, axis, by):
    devices = lax.axis_size(axis)
    pairs = [(i, i + by) for i in range(devices) if 0 <= i + by < devices]
    return lax.ppermute(shard, axis, pairs)


def weighted_prefix(states, decays, place):
    order = jnp.arange(states.shape[0])
    between = (order[:, None] < order[None, :]) & (order[None, :] < place)
    span = jnp.sum(jnp.where(between[:, :, None], decays[None, :, :], 0.0), axis=1)
    scale = jnp.where((order < place)[:, None], jnp.exp(span), 0.0)
    return jnp.sum(scale[:, :, None, None] * states, axis=0)


def carried_in(decay, state, axis):
    members = lax.axis_size(axis)
    heads, rows, cols = state.shape
    decay_row = jnp.zeros((1, cols), jnp.float32).at[0, :heads].set(decay)
    packed = jnp.concatenate([state.reshape(heads * rows, cols), decay_row], axis=0)
    copies = jnp.broadcast_to(packed.astype(jnp.bfloat16)[None], (members,) + packed.shape)
    gathered = lax.all_to_all(copies, axis, 0, 0).astype(jnp.float32)
    states = gathered[:, : heads * rows].reshape(members, heads, rows, cols)
    decays = gathered[:, heads * rows, :heads]
    return weighted_prefix(states, decays, lax.axis_index(axis))


def causal_conv(rim_rows, pre_conv, kernel):
    padded = jnp.concatenate([rim_rows, pre_conv], axis=0).astype(jnp.float32)
    length = pre_conv.shape[0]
    summed = jnp.zeros(pre_conv.shape, jnp.float32)
    for offset in range(kernel.shape[0]):
        summed = summed + kernel[offset] * padded[offset : offset + length]
    return jax.nn.silu(summed).astype(jnp.bfloat16)


def split_pair(values):
    high = values.astype(jnp.bfloat16)
    low = (values - high.astype(jnp.float32)).astype(jnp.bfloat16)
    return high, low


def regroup(w_xz, w_dt):
    inner = lax.axis_size("head")
    layers, features, _ = w_xz.shape
    packed = jnp.concatenate([w_xz, w_dt], axis=2)
    split = packed.reshape(layers, inner, features // inner, packed.shape[2])
    return lax.all_to_all(split, "head", 1, 1)


def regroup_shared(w_xz, w_dt):
    members = lax.axis_size("scan")
    core = lax.axis_index("scan") % 2
    own = regroup(
        jnp.where(core == 0, w_xz[:1], w_xz[1:2]), jnp.where(core == 0, w_dt[:1], w_dt[1:2])
    )[0]
    pairs = [(i, i ^ 1) for i in range(members)]
    other = lax.ppermute(own, "scan", pairs)
    return jnp.where(core == 0, own, other), jnp.where(core == 0, other, own)


def gather_heads(values):
    inner = lax.axis_size("head")
    me = lax.axis_index("head")
    pieces = [values] + [
        lax.ppermute(values, "head", [(i, (i + shift) % inner) for i in range(inner)])
        for shift in range(1, inner)
    ]
    flipped = jnp.stack(pieces[::-1])
    doubled = jnp.concatenate([flipped, flipped], axis=0)
    return lax.dynamic_slice_in_dim(doubled, inner - 1 - me, inner, 0)


def mix_layer(stream, regrouped, xz_cols, w_bc, dt_bias, decay_rate, conv_x, conv_bc, w_out):
    length, piece = stream.shape
    inner = lax.axis_size("head")
    spot = lax.axis_index("head")
    feature_count = piece * inner
    heads_here = regrouped.shape[2] - xz_cols
    head_dim = xz_cols // (2 * heads_here)
    state_dim = w_bc.shape[1] // 2
    taps = conv_x.shape[0]
    partial = jnp.einsum("tf,gfc->tgc", stream, regrouped, preferred_element_type=jnp.float32)
    rows_bc = lax.dynamic_slice_in_dim(w_bc, spot * piece, piece, 0)
    slice_bc = 2 * state_dim // inner
    partial_bc = jnp.dot(stream, rows_bc, preferred_element_type=jnp.float32).reshape(
        length, inner, slice_bc
    )
    wide_piece = stream.astype(jnp.float32)
    square_high, square_low = split_pair(jnp.sum(wide_piece * wide_piece, axis=1))
    squares = jnp.broadcast_to(
        jnp.stack([square_high, square_low], axis=1)[:, None], (length, inner, 2)
    )
    step_high, step_low = split_pair(partial[:, :, xz_cols:])
    outgoing = jnp.concatenate(
        [
            partial[:, :, :xz_cols].astype(jnp.bfloat16),
            partial_bc.astype(jnp.bfloat16),
            step_high,
            step_low,
            squares,
        ],
        axis=2,
    )
    arrived = lax.all_to_all(jnp.moveaxis(outgoing, 1, 0), "head", 0, 0).astype(jnp.float32)
    summed = jnp.sum(arrived, axis=0)
    summed_xz = summed[:, :xz_cols]
    summed_bc = summed[:, xz_cols : xz_cols + slice_bc]
    at = xz_cols + slice_bc
    dt_sum = summed[:, at : at + heads_here] + summed[:, at + heads_here : at + 2 * heads_here]
    square_sum = summed[:, at + 2 * heads_here :].sum(axis=1, keepdims=True)
    row_scale = lax.rsqrt(square_sum / feature_count + EPSILON)
    proj_xz = (
        (summed_xz.astype(jnp.float32) * row_scale)
        .astype(jnp.bfloat16)
        .reshape(length, heads_here, 2, head_dim)
    )
    proj_bc = (summed_bc * row_scale).astype(jnp.bfloat16)
    dt_raw = dt_sum * row_scale
    pre_x = proj_xz[:, :, 0, :].reshape(length, heads_here * head_dim)
    gate_vals = proj_xz[:, :, 1, :].astype(jnp.float32)
    rim_x, rim_bc = from_behind(
        (pre_x[length - taps + 1 :], proj_bc[length - taps + 1 :]), "scan", 1
    )
    inputs_x = causal_conv(rim_x, pre_x, conv_x)
    taps_bc = lax.dynamic_slice_in_dim(conv_bc, spot * slice_bc, slice_bc, 1)
    conv_slice = causal_conv(rim_bc, proj_bc, taps_bc)
    conv_out = jnp.moveaxis(gather_heads(conv_slice), 0, 1).reshape(length, 2 * state_dim)
    block_count = length // BLOCK
    b_blocks = conv_out[:, :state_dim].reshape(block_count, BLOCK, state_dim)
    c_blocks = conv_out[:, state_dim:].reshape(block_count, BLOCK, state_dim)
    gram_mat = jnp.einsum("kqn,ksn->kqs", c_blocks, b_blocks, preferred_element_type=jnp.float32)
    step_dt = jax.nn.softplus(dt_raw + dt_bias)
    cum_decay = jnp.cumsum((-step_dt * decay_rate).reshape(block_count, BLOCK, heads_here), axis=1)
    dt_blocks = step_dt.reshape(block_count, BLOCK, heads_here)
    x_blocks = inputs_x.reshape(block_count, BLOCK, heads_here, head_dim)
    positions = jnp.arange(BLOCK)
    causal = positions[:, None] >= positions[None, :]
    cum_heads = jnp.moveaxis(cum_decay, 2, 1)
    dt_heads = jnp.moveaxis(dt_blocks, 2, 1)
    spread = cum_heads[:, :, :, None] - cum_heads[:, :, None, :]
    weights = (
        gram_mat[:, None]
        * jnp.exp(jnp.where(causal[None, None], spread, -jnp.inf))
        * dt_heads[:, :, None, :]
    ).astype(jnp.bfloat16)
    inside = jnp.einsum("khqs,kshp->kqhp", weights, x_blocks, preferred_element_type=jnp.float32)
    to_end = jnp.exp(cum_decay[:, -1:, :] - cum_decay) * dt_blocks
    scaled = (x_blocks.astype(jnp.float32) * to_end[:, :, :, None]).astype(jnp.bfloat16)
    block_ends = jnp.einsum("kqhp,kqn->khpn", scaled, b_blocks, preferred_element_type=jnp.float32)
    block_decay = cum_decay[:, -1, :]

    starts_local = jnp.stack(
        [weighted_prefix(block_ends, block_decay, k) for k in range(block_count)]
    )
    local_end = weighted_prefix(block_ends, block_decay, block_count)
    device_decay = jnp.sum(block_decay, axis=0)
    incoming = carried_in(device_decay, local_end, "scan")
    prior_decay = jnp.concatenate(
        [jnp.zeros((1, heads_here), jnp.float32), jnp.cumsum(block_decay, axis=0)[:-1]], axis=0
    )
    starts = jnp.exp(prior_decay)[:, :, None, None] * incoming[None] + starts_local
    carried = jnp.einsum(
        "kqn,khpn->kqhp", c_blocks.astype(jnp.float32), starts, precision=lax.Precision.HIGHEST
    )
    mixed_out = inside + jnp.exp(cum_decay)[:, :, :, None] * carried
    gated_out = mixed_out.reshape(length, heads_here, head_dim) * jax.nn.silu(gate_vals)
    normed = (
        (gated_out * lax.rsqrt(jnp.mean(gated_out * gated_out, axis=2, keepdims=True) + EPSILON))
        .astype(jnp.bfloat16)
        .reshape(length, heads_here * head_dim)
    )
    summed_out = jnp.dot(
        jnp.moveaxis(gather_heads(normed), 0, 1).reshape(length, inner * normed.shape[1]),
        w_out,
        preferred_element_type=jnp.float32,
    )
    return (stream.astype(jnp.float32) + summed_out).astype(jnp.bfloat16)


def local(stream, w_xz, w_bc, w_dt, dt_bias, decay_rate, conv_x, conv_bc, w_out):
    xz_cols = w_xz.shape[2]
    first, second = regroup_shared(w_xz, w_dt)
    layer = lambda u, l, weights: mix_layer(
        u, weights, xz_cols, w_bc[l], dt_bias[l], decay_rate[l], conv_x[l], conv_bc[l], w_out[l]
    )
    raster_out = layer(stream, 0, first)
    members = lax.axis_size("scan")
    length = raster_out.shape[0]
    columns = raster_out.shape[1]
    grouped = raster_out.reshape(members, length // members, 1, columns)
    exchanged = lax.all_to_all(grouped, "scan", split_axis=0, concat_axis=2, tiled=True)
    return layer(exchanged.reshape(length, columns), 1, second)


def solution(mesh):
    placed = (
        P("scan", "head"),
        P(None, None, "head"),
        P(),
        P(None, None, "head"),
        P(None, "head"),
        P(None, "head"),
        P(None, None, "head"),
        P(),
        P(None, None, "head"),
    )
    return jax.shard_map(
        local, mesh=mesh, in_specs=placed, out_specs=P("scan", "head"), check_vma=False
    )
```

```python
import jax
import jax.numpy as jnp
from jax import lax
from jax.sharding import PartitionSpec as P

BLOCK = 256


EPSILON = 1e-05


def from_behind(shard, axis, by):
    devices = lax.axis_size(axis)
    pairs = [(i, i + by) for i in range(devices) if 0 <= i + by < devices]
    return lax.ppermute(shard, axis, pairs)


def weighted_prefix(states, decays, place):
    order = jnp.arange(states.shape[0])
    between = (order[:, None] < order[None, :]) & (order[None, :] < place)
    span = jnp.sum(jnp.where(between[:, :, None], decays[None, :, :], 0.0), axis=1)
    scale = jnp.where((order < place)[:, None], jnp.exp(span), 0.0)
    return jnp.sum(scale[:, :, None, None] * states, axis=0)


def carried_in(decay, state, axis):
    members = lax.axis_size(axis)
    heads, rows, cols = state.shape
    decay_row = jnp.zeros((1, cols), jnp.float32).at[0, :heads].set(decay)
    packed = jnp.concatenate([state.reshape(heads * rows, cols), decay_row], axis=0)
    gathered = lax.all_gather(packed.astype(jnp.bfloat16), axis).astype(jnp.float32)
    states = gathered[:, : heads * rows].reshape(members, heads, rows, cols)
    decays = gathered[:, heads * rows, :heads]
    return weighted_prefix(states, decays, lax.axis_index(axis))


def causal_conv(rim_rows, pre_conv, kernel):
    padded = jnp.concatenate([rim_rows, pre_conv], axis=0).astype(jnp.float32)
    length = pre_conv.shape[0]
    summed = jnp.zeros(pre_conv.shape, jnp.float32)
    for offset in range(kernel.shape[0]):
        summed = summed + kernel[offset] * padded[offset : offset + length]
    return jax.nn.silu(summed).astype(jnp.bfloat16)


def split_pair(values):
    high = values.astype(jnp.bfloat16)
    low = (values - high.astype(jnp.float32)).astype(jnp.bfloat16)
    return high, low


def regroup(w_xz, w_dt):
    inner = lax.axis_size("head")
    layers, features, _ = w_xz.shape
    packed = jnp.concatenate([w_xz, w_dt], axis=2)
    split = packed.reshape(layers, inner, features // inner, packed.shape[2])
    return lax.all_to_all(split, "head", 1, 1)


def regroup_shared(w_xz, w_dt):
    members = lax.axis_size("scan")
    core = lax.axis_index("scan") % 2
    own = regroup(
        jnp.where(core == 0, w_xz[:1], w_xz[1:2]), jnp.where(core == 0, w_dt[:1], w_dt[1:2])
    )[0]
    pairs = [(i, i ^ 1) for i in range(members)]
    other = lax.ppermute(own, "scan", pairs)
    return jnp.where(core == 0, own, other), jnp.where(core == 0, other, own)


def gather_heads(values):
    inner = lax.axis_size("head")
    me = lax.axis_index("head")
    pieces = [values] + [
        lax.ppermute(values, "head", [(i, (i + shift) % inner) for i in range(inner)])
        for shift in range(1, inner)
    ]
    flipped = jnp.stack(pieces[::-1])
    doubled = jnp.concatenate([flipped, flipped], axis=0)
    return lax.dynamic_slice_in_dim(doubled, inner - 1 - me, inner, 0)


def mix_layer(stream, rim_rows, regrouped, xz_cols, w_bc, dt_bias, decay_rate, conv_x, conv_bc, w_out):
    length, piece = stream.shape
    inner = lax.axis_size("head")
    spot = lax.axis_index("head")
    feature_count = piece * inner
    heads_here = regrouped.shape[2] - xz_cols
    head_dim = xz_cols // (2 * heads_here)
    state_dim = w_bc.shape[1] // 2
    taps = conv_x.shape[0]
    lead = -(-(taps - 1) // 8) * 8
    filler = jnp.zeros((lead - rim_rows.shape[0], piece), stream.dtype)
    extended = jnp.concatenate([filler, rim_rows, stream], axis=0)
    wide_length = extended.shape[0]
    partial = jnp.einsum("tf,gfc->tgc", extended, regrouped, preferred_element_type=jnp.float32)
    rows_bc = lax.dynamic_slice_in_dim(w_bc, spot * piece, piece, 0)
    slice_bc = 2 * state_dim // inner
    partial_bc = jnp.dot(extended, rows_bc, preferred_element_type=jnp.float32).reshape(
        wide_length, inner, slice_bc
    )
    wide_piece = extended.astype(jnp.float32)
    square_high, square_low = split_pair(jnp.sum(wide_piece * wide_piece, axis=1))
    squares = jnp.broadcast_to(
        jnp.stack([square_high, square_low], axis=1)[:, None], (wide_length, inner, 2)
    )
    step_high, step_low = split_pair(partial[:, :, xz_cols:])
    outgoing = jnp.concatenate(
        [
            partial[:, :, :xz_cols].astype(jnp.bfloat16),
            partial_bc.astype(jnp.bfloat16),
            step_high,
            step_low,
            squares,
        ],
        axis=2,
    )
    arrived = lax.all_to_all(jnp.moveaxis(outgoing, 1, 0), "head", 0, 0).astype(jnp.float32)
    summed = jnp.sum(arrived, axis=0)
    summed_xz = summed[:, :xz_cols]
    summed_bc = summed[:, xz_cols : xz_cols + slice_bc]
    at = xz_cols + slice_bc
    dt_sum = summed[:, at : at + heads_here] + summed[:, at + heads_here : at + 2 * heads_here]
    square_sum = summed[:, at + 2 * heads_here :].sum(axis=1, keepdims=True)
    row_scale = lax.rsqrt(square_sum / feature_count + EPSILON)
    proj_xz = (
        (summed_xz * row_scale)
        .astype(jnp.bfloat16)
        .reshape(wide_length, heads_here, 2, head_dim)
    )
    proj_bc_wide = (summed_bc * row_scale).astype(jnp.bfloat16)
    dt_raw = (dt_sum * row_scale)[lead:]
    pre_wide = proj_xz[:, :, 0, :].reshape(wide_length, heads_here * head_dim)
    gate_vals = proj_xz[lead:, :, 1, :].astype(jnp.float32)
    rim_x, pre_x = pre_wide[lead - taps + 1 : lead], pre_wide[lead:]
    rim_bc, proj_bc = proj_bc_wide[lead - taps + 1 : lead], proj_bc_wide[lead:]
    inputs_x = causal_conv(rim_x, pre_x, conv_x)
    taps_bc = lax.dynamic_slice_in_dim(conv_bc, spot * slice_bc, slice_bc, 1)
    conv_slice = causal_conv(rim_bc, proj_bc, taps_bc)
    conv_out = jnp.moveaxis(gather_heads(conv_slice), 0, 1).reshape(length, 2 * state_dim)
    block_count = length // BLOCK
    b_blocks = conv_out[:, :state_dim].reshape(block_count, BLOCK, state_dim)
    c_blocks = conv_out[:, state_dim:].reshape(block_count, BLOCK, state_dim)
    gram_mat = jnp.einsum("kqn,ksn->kqs", c_blocks, b_blocks, preferred_element_type=jnp.float32)
    step_dt = jax.nn.softplus(dt_raw + dt_bias)
    cum_decay = jnp.cumsum((-step_dt * decay_rate).reshape(block_count, BLOCK, heads_here), axis=1)
    dt_blocks = step_dt.reshape(block_count, BLOCK, heads_here)
    x_blocks = inputs_x.reshape(block_count, BLOCK, heads_here, head_dim)
    positions = jnp.arange(BLOCK)
    causal = positions[:, None] >= positions[None, :]
    cum_heads = jnp.moveaxis(cum_decay, 2, 1)
    dt_heads = jnp.moveaxis(dt_blocks, 2, 1)
    spread = cum_heads[:, :, :, None] - cum_heads[:, :, None, :]
    weights = (
        gram_mat[:, None]
        * jnp.exp(jnp.where(causal[None, None], spread, -jnp.inf))
        * dt_heads[:, :, None, :]
    ).astype(jnp.bfloat16)
    inside = jnp.einsum("khqs,kshp->kqhp", weights, x_blocks, preferred_element_type=jnp.float32)
    to_end = jnp.exp(cum_decay[:, -1:, :] - cum_decay) * dt_blocks
    scaled = (x_blocks.astype(jnp.float32) * to_end[:, :, :, None]).astype(jnp.bfloat16)
    block_ends = jnp.einsum("kqhp,kqn->khpn", scaled, b_blocks, preferred_element_type=jnp.float32)
    block_decay = cum_decay[:, -1, :]

    starts_local = jnp.stack(
        [weighted_prefix(block_ends, block_decay, k) for k in range(block_count)]
    )
    local_end = weighted_prefix(block_ends, block_decay, block_count)
    device_decay = jnp.sum(block_decay, axis=0)
    incoming = carried_in(device_decay, local_end, "scan")
    prior_decay = jnp.concatenate(
        [jnp.zeros((1, heads_here), jnp.float32), jnp.cumsum(block_decay, axis=0)[:-1]], axis=0
    )
    starts = jnp.exp(prior_decay)[:, :, None, None] * incoming[None] + starts_local
    carried = jnp.einsum(
        "kqn,khpn->kqhp", c_blocks.astype(jnp.float32), starts, precision=lax.Precision.HIGHEST
    )
    mixed_out = inside + jnp.exp(cum_decay)[:, :, :, None] * carried
    gated_out = mixed_out.reshape(length, heads_here, head_dim) * jax.nn.silu(gate_vals)
    normed = (
        (gated_out * lax.rsqrt(jnp.mean(gated_out * gated_out, axis=2, keepdims=True) + EPSILON))
        .astype(jnp.bfloat16)
        .reshape(length, heads_here * head_dim)
    )
    summed_out = jnp.dot(
        jnp.moveaxis(gather_heads(normed), 0, 1).reshape(length, inner * normed.shape[1]),
        w_out,
        preferred_element_type=jnp.float32,
    )
    return (stream.astype(jnp.float32) + summed_out).astype(jnp.bfloat16)


def local(stream, w_xz, w_bc, w_dt, dt_bias, decay_rate, conv_x, conv_bc, w_out):
    xz_cols = w_xz.shape[2]
    first, second = regroup_shared(w_xz, w_dt)
    layer = lambda u, rim, l, weights: mix_layer(
        u, rim, weights, xz_cols, w_bc[l], dt_bias[l], decay_rate[l], conv_x[l], conv_bc[l], w_out[l]
    )
    taps = conv_x.shape[1]
    raster_out = layer(stream, from_behind(stream[stream.shape[0] - taps + 1 :], "scan", 1), 0, first)
    members = lax.axis_size("scan")
    length = raster_out.shape[0]
    columns = raster_out.shape[1]
    grouped = raster_out.reshape(members, length // members, 1, columns)
    exchanged = lax.all_to_all(grouped, "scan", split_axis=0, concat_axis=2, tiled=True)
    reordered = exchanged.reshape(length, columns)
    rim = from_behind(reordered[length - taps + 1 :], "scan", 1)
    return layer(reordered, rim, 1, second)


def solution(mesh):
    placed = (
        P("scan", "head"),
        P(None, None, "head"),
        P(),
        P(None, None, "head"),
        P(None, "head"),
        P(None, "head"),
        P(None, None, "head"),
        P(),
        P(None, None, "head"),
    )
    return jax.shard_map(
        local, mesh=mesh, in_specs=placed, out_specs=P("scan", "head"), check_vma=False
    )
```

```python
import jax
import jax.numpy as jnp
from jax import lax
from jax.sharding import PartitionSpec as P

BLOCK = 256


EPSILON = 1e-05


def from_behind(shard, axis, by):
    devices = lax.axis_size(axis)
    pairs = [(i, i + by) for i in range(devices) if 0 <= i + by < devices]
    return lax.ppermute(shard, axis, pairs)


def weighted_prefix(states, decays, place):
    order = jnp.arange(states.shape[0])
    between = (order[:, None] < order[None, :]) & (order[None, :] < place)
    span = jnp.sum(jnp.where(between[:, :, None], decays[None, :, :], 0.0), axis=1)
    scale = jnp.where((order < place)[:, None], jnp.exp(span), 0.0)
    return jnp.sum(scale[:, :, None, None] * states, axis=0)


def carried_in(decay, state, axis):
    members = lax.axis_size(axis)
    heads, rows, cols = state.shape
    decay_row = jnp.zeros((1, cols), jnp.float32).at[0, :heads].set(decay)
    packed = jnp.concatenate([state.reshape(heads * rows, cols), decay_row], axis=0)
    gathered = lax.all_gather(packed.astype(jnp.bfloat16), axis).astype(jnp.float32)
    states = gathered[:, : heads * rows].reshape(members, heads, rows, cols)
    decays = gathered[:, heads * rows, :heads]
    return weighted_prefix(states, decays, lax.axis_index(axis))


def causal_conv(rim_rows, pre_conv, kernel):
    padded = jnp.concatenate([rim_rows, pre_conv], axis=0).astype(jnp.float32)
    length = pre_conv.shape[0]
    summed = jnp.zeros(pre_conv.shape, jnp.float32)
    for offset in range(kernel.shape[0]):
        summed = summed + kernel[offset] * padded[offset : offset + length]
    return jax.nn.silu(summed).astype(jnp.bfloat16)


def split_pair(values):
    high = values.astype(jnp.bfloat16)
    low = (values - high.astype(jnp.float32)).astype(jnp.bfloat16)
    return high, low


def regroup(w_xz, w_dt):
    inner = lax.axis_size("head")
    layers, features, _ = w_xz.shape
    packed = jnp.concatenate([w_xz, w_dt], axis=2)
    split = packed.reshape(layers, inner, features // inner, packed.shape[2])
    return lax.all_to_all(split, "head", 1, 1)


def regroup_shared(w_xz, w_dt):
    members = lax.axis_size("scan")
    core = lax.axis_index("scan") % 2
    own = regroup(
        jnp.where(core == 0, w_xz[:1], w_xz[1:2]), jnp.where(core == 0, w_dt[:1], w_dt[1:2])
    )[0]
    pairs = [(i, i ^ 1) for i in range(members)]
    other = lax.ppermute(own, "scan", pairs)
    return jnp.where(core == 0, own, other), jnp.where(core == 0, other, own)


def gather_heads(values):
    inner = lax.axis_size("head")
    me = lax.axis_index("head")
    pieces = [values] + [
        lax.ppermute(values, "head", [(i, (i + shift) % inner) for i in range(inner)])
        for shift in range(1, inner)
    ]
    flipped = jnp.stack(pieces[::-1])
    doubled = jnp.concatenate([flipped, flipped], axis=0)
    return lax.dynamic_slice_in_dim(doubled, inner - 1 - me, inner, 0)


def mix_layer(stream, regrouped, xz_cols, w_bc, dt_bias, decay_rate, conv_x, conv_bc, w_out):
    length, piece = stream.shape
    inner = lax.axis_size("head")
    spot = lax.axis_index("head")
    feature_count = piece * inner
    heads_here = regrouped.shape[2] - xz_cols
    head_dim = xz_cols // (2 * heads_here)
    state_dim = w_bc.shape[1] // 2
    taps = conv_x.shape[0]
    rows_bc = lax.dynamic_slice_in_dim(w_bc, spot * piece, piece, 0)
    slice_bc = 2 * state_dim // inner
    combined = jnp.concatenate(
        [
            regrouped[:, :, :xz_cols],
            jnp.moveaxis(rows_bc.reshape(piece, inner, slice_bc), 1, 0),
            regrouped[:, :, xz_cols:],
        ],
        axis=2,
    )
    partial = jnp.einsum("tf,gfc->gtc", stream, combined, preferred_element_type=jnp.float32)
    wide_piece = stream.astype(jnp.float32)
    square_high, square_low = split_pair(jnp.sum(wide_piece * wide_piece, axis=1))
    squares = jnp.broadcast_to(
        jnp.stack([square_high, square_low], axis=1)[None], (inner, length, 2)
    )
    step_high, step_low = split_pair(partial[:, :, xz_cols + slice_bc :])
    outgoing = jnp.concatenate(
        [partial[:, :, : xz_cols + slice_bc].astype(jnp.bfloat16), step_high, step_low, squares],
        axis=2,
    )
    arrived = lax.all_to_all(outgoing, "head", 0, 0).astype(jnp.float32)
    summed = jnp.sum(arrived, axis=0)
    summed_xz = summed[:, :xz_cols]
    summed_bc = summed[:, xz_cols : xz_cols + slice_bc]
    at = xz_cols + slice_bc
    dt_sum = summed[:, at : at + heads_here] + summed[:, at + heads_here : at + 2 * heads_here]
    square_sum = summed[:, at + 2 * heads_here :].sum(axis=1, keepdims=True)
    row_scale = lax.rsqrt(square_sum / feature_count + EPSILON)
    proj_xz = (
        (summed_xz.astype(jnp.float32) * row_scale)
        .astype(jnp.bfloat16)
        .reshape(length, heads_here, 2, head_dim)
    )
    proj_bc = (summed_bc * row_scale).astype(jnp.bfloat16)
    dt_raw = dt_sum * row_scale
    pre_x = proj_xz[:, :, 0, :].reshape(length, heads_here * head_dim)
    gate_vals = proj_xz[:, :, 1, :].astype(jnp.float32)
    rim_x, rim_bc = from_behind(
        (pre_x[length - taps + 1 :], proj_bc[length - taps + 1 :]), "scan", 1
    )
    inputs_x = causal_conv(rim_x, pre_x, conv_x)
    taps_bc = lax.dynamic_slice_in_dim(conv_bc, spot * slice_bc, slice_bc, 1)
    conv_slice = causal_conv(rim_bc, proj_bc, taps_bc)
    conv_out = jnp.moveaxis(gather_heads(conv_slice), 0, 1).reshape(length, 2 * state_dim)
    block_count = length // BLOCK
    b_blocks = conv_out[:, :state_dim].reshape(block_count, BLOCK, state_dim)
    c_blocks = conv_out[:, state_dim:].reshape(block_count, BLOCK, state_dim)
    gram_mat = jnp.einsum("kqn,ksn->kqs", c_blocks, b_blocks, preferred_element_type=jnp.float32)
    step_dt = jax.nn.softplus(dt_raw + dt_bias)
    cum_decay = jnp.cumsum((-step_dt * decay_rate).reshape(block_count, BLOCK, heads_here), axis=1)
    dt_blocks = step_dt.reshape(block_count, BLOCK, heads_here)
    x_blocks = inputs_x.reshape(block_count, BLOCK, heads_here, head_dim)
    positions = jnp.arange(BLOCK)
    causal = positions[:, None] >= positions[None, :]
    cum_heads = jnp.moveaxis(cum_decay, 2, 1)
    dt_heads = jnp.moveaxis(dt_blocks, 2, 1)
    spread = cum_heads[:, :, :, None] - cum_heads[:, :, None, :]
    weights = (
        gram_mat[:, None]
        * jnp.exp(jnp.where(causal[None, None], spread, -jnp.inf))
        * dt_heads[:, :, None, :]
    ).astype(jnp.bfloat16)
    inside = jnp.einsum("khqs,kshp->kqhp", weights, x_blocks, preferred_element_type=jnp.float32)
    to_end = jnp.exp(cum_decay[:, -1:, :] - cum_decay) * dt_blocks
    scaled = (x_blocks.astype(jnp.float32) * to_end[:, :, :, None]).astype(jnp.bfloat16)
    block_ends = jnp.einsum("kqhp,kqn->khpn", scaled, b_blocks, preferred_element_type=jnp.float32)
    block_decay = cum_decay[:, -1, :]

    starts_local = jnp.stack(
        [weighted_prefix(block_ends, block_decay, k) for k in range(block_count)]
    )
    local_end = weighted_prefix(block_ends, block_decay, block_count)
    device_decay = jnp.sum(block_decay, axis=0)
    incoming = carried_in(device_decay, local_end, "scan")
    prior_decay = jnp.concatenate(
        [jnp.zeros((1, heads_here), jnp.float32), jnp.cumsum(block_decay, axis=0)[:-1]], axis=0
    )
    starts = jnp.exp(prior_decay)[:, :, None, None] * incoming[None] + starts_local
    carried = jnp.einsum(
        "kqn,khpn->kqhp", c_blocks.astype(jnp.float32), starts, precision=lax.Precision.HIGHEST
    )
    mixed_out = inside + jnp.exp(cum_decay)[:, :, :, None] * carried
    gated_out = mixed_out.reshape(length, heads_here, head_dim) * jax.nn.silu(gate_vals)
    normed = (
        (gated_out * lax.rsqrt(jnp.mean(gated_out * gated_out, axis=2, keepdims=True) + EPSILON))
        .astype(jnp.bfloat16)
        .reshape(length, heads_here * head_dim)
    )
    summed_out = jnp.dot(
        jnp.moveaxis(gather_heads(normed), 0, 1).reshape(length, inner * normed.shape[1]),
        w_out,
        preferred_element_type=jnp.float32,
    )
    return (stream.astype(jnp.float32) + summed_out).astype(jnp.bfloat16)


def local(stream, w_xz, w_bc, w_dt, dt_bias, decay_rate, conv_x, conv_bc, w_out):
    xz_cols = w_xz.shape[2]
    first, second = regroup_shared(w_xz, w_dt)
    layer = lambda u, l, weights: mix_layer(
        u, weights, xz_cols, w_bc[l], dt_bias[l], decay_rate[l], conv_x[l], conv_bc[l], w_out[l]
    )
    raster_out = layer(stream, 0, first)
    members = lax.axis_size("scan")
    length = raster_out.shape[0]
    columns = raster_out.shape[1]
    grouped = raster_out.reshape(members, length // members, 1, columns)
    exchanged = lax.all_to_all(grouped, "scan", split_axis=0, concat_axis=2, tiled=True)
    return layer(exchanged.reshape(length, columns), 1, second)


def solution(mesh):
    placed = (
        P("scan", "head"),
        P(None, None, "head"),
        P(),
        P(None, None, "head"),
        P(None, "head"),
        P(None, "head"),
        P(None, None, "head"),
        P(),
        P(None, None, "head"),
    )
    return jax.shard_map(
        local, mesh=mesh, in_specs=placed, out_specs=P("scan", "head"), check_vma=False
    )
```

```python
import jax
import jax.numpy as jnp
from jax import lax
from jax.sharding import PartitionSpec as P

BLOCK = 256


EPSILON = 1e-05


def from_behind(shard, axis, by):
    devices = lax.axis_size(axis)
    pairs = [(i, i + by) for i in range(devices) if 0 <= i + by < devices]
    return lax.ppermute(shard, axis, pairs)


def weighted_prefix(states, decays, place):
    order = jnp.arange(states.shape[0])
    between = (order[:, None] < order[None, :]) & (order[None, :] < place)
    span = jnp.sum(jnp.where(between[:, :, None], decays[None, :, :], 0.0), axis=1)
    scale = jnp.where((order < place)[:, None], jnp.exp(span), 0.0)
    return jnp.sum(scale[:, :, None, None] * states, axis=0)


def carried_in(decay, state, axis):
    members = lax.axis_size(axis)
    heads, rows, cols = state.shape
    decay_row = jnp.zeros((1, cols), jnp.float32).at[0, :heads].set(decay)
    packed = jnp.concatenate([state.reshape(heads * rows, cols), decay_row], axis=0)
    gathered = lax.all_gather(packed.astype(jnp.bfloat16), axis).astype(jnp.float32)
    states = gathered[:, : heads * rows].reshape(members, heads, rows, cols)
    decays = gathered[:, heads * rows, :heads]
    return weighted_prefix(states, decays, lax.axis_index(axis))


def causal_conv(rim_rows, pre_conv, kernel):
    padded = jnp.concatenate([rim_rows, pre_conv], axis=0).astype(jnp.float32)
    length = pre_conv.shape[0]
    summed = jnp.zeros(pre_conv.shape, jnp.float32)
    for offset in range(kernel.shape[0]):
        summed = summed + kernel[offset] * padded[offset : offset + length]
    return jax.nn.silu(summed).astype(jnp.bfloat16)


def split_pair(values):
    high = values.astype(jnp.bfloat16)
    low = (values - high.astype(jnp.float32)).astype(jnp.bfloat16)
    return high, low


def regroup(w_xz, w_dt):
    inner = lax.axis_size("head")
    layers, features, _ = w_xz.shape
    packed = jnp.concatenate([w_xz, w_dt], axis=2)
    split = packed.reshape(layers, inner, features // inner, packed.shape[2])
    return lax.all_to_all(split, "head", 1, 1)


def regroup_shared(w_xz, w_dt):
    members = lax.axis_size("scan")
    core = lax.axis_index("scan") % 2
    own = regroup(
        jnp.where(core == 0, w_xz[:1], w_xz[1:2]), jnp.where(core == 0, w_dt[:1], w_dt[1:2])
    )[0]
    pairs = [(i, i ^ 1) for i in range(members)]
    other = lax.ppermute(own, "scan", pairs)
    return jnp.where(core == 0, own, other), jnp.where(core == 0, other, own)


def gather_heads(values):
    inner = lax.axis_size("head")
    me = lax.axis_index("head")
    pieces = [values] + [
        lax.ppermute(values, "head", [(i, (i + shift) % inner) for i in range(inner)])
        for shift in range(1, inner)
    ]
    flipped = jnp.stack(pieces[::-1])
    doubled = jnp.concatenate([flipped, flipped], axis=0)
    return lax.dynamic_slice_in_dim(doubled, inner - 1 - me, inner, 0)


def mix_layer(stream, regrouped, xz_cols, w_bc, dt_bias, decay_rate, conv_x, conv_bc, w_out):
    length, piece = stream.shape
    inner = lax.axis_size("head")
    spot = lax.axis_index("head")
    feature_count = piece * inner
    heads_here = regrouped.shape[2] - xz_cols
    head_dim = xz_cols // (2 * heads_here)
    state_dim = w_bc.shape[1] // 2
    taps = conv_x.shape[0]
    rows_bc = lax.dynamic_slice_in_dim(w_bc, spot * piece, piece, 0)
    slice_bc = 2 * state_dim // inner
    combined = jnp.concatenate(
        [
            regrouped[:, :, :xz_cols],
            jnp.moveaxis(rows_bc.reshape(piece, inner, slice_bc), 1, 0),
            regrouped[:, :, xz_cols:],
        ],
        axis=2,
    )
    partial = jnp.einsum("tf,gfc->gtc", stream, combined, preferred_element_type=jnp.float32)
    wide_piece = stream.astype(jnp.float32)
    square_high, square_low = split_pair(jnp.sum(wide_piece * wide_piece, axis=1))
    squares = jnp.broadcast_to(
        jnp.stack([square_high, square_low], axis=1)[None], (inner, length, 2)
    )
    step_high, step_low = split_pair(partial[:, :, xz_cols + slice_bc :])
    outgoing = jnp.concatenate(
        [partial[:, :, : xz_cols + slice_bc].astype(jnp.bfloat16), step_high, step_low, squares],
        axis=2,
    )
    arrived = lax.all_to_all(outgoing, "head", 0, 0).astype(jnp.float32)
    summed = jnp.sum(arrived, axis=0)
    summed_xz = summed[:, :xz_cols]
    summed_bc = summed[:, xz_cols : xz_cols + slice_bc]
    at = xz_cols + slice_bc
    dt_sum = summed[:, at : at + heads_here] + summed[:, at + heads_here : at + 2 * heads_here]
    square_sum = summed[:, at + 2 * heads_here :].sum(axis=1, keepdims=True)
    row_scale = lax.rsqrt(square_sum / feature_count + EPSILON)
    proj_xz = (
        (summed_xz.astype(jnp.float32) * row_scale)
        .astype(jnp.bfloat16)
        .reshape(length, heads_here, 2, head_dim)
    )
    proj_bc = (summed_bc * row_scale).astype(jnp.bfloat16)
    dt_raw = dt_sum * row_scale
    pre_x = proj_xz[:, :, 0, :].reshape(length, heads_here * head_dim)
    gate_vals = proj_xz[:, :, 1, :].astype(jnp.float32)
    rims = from_behind(
        jnp.concatenate([pre_x[length - taps + 1 :], proj_bc[length - taps + 1 :]], axis=1),
        "scan",
        1,
    )
    rim_x, rim_bc = rims[:, : pre_x.shape[1]], rims[:, pre_x.shape[1] :]
    inputs_x = causal_conv(rim_x, pre_x, conv_x)
    taps_bc = lax.dynamic_slice_in_dim(conv_bc, spot * slice_bc, slice_bc, 1)
    conv_slice = causal_conv(rim_bc, proj_bc, taps_bc)
    conv_out = jnp.moveaxis(gather_heads(conv_slice), 0, 1).reshape(length, 2 * state_dim)
    block_count = length // BLOCK
    b_blocks = conv_out[:, :state_dim].reshape(block_count, BLOCK, state_dim)
    c_blocks = conv_out[:, state_dim:].reshape(block_count, BLOCK, state_dim)
    gram_mat = jnp.einsum("kqn,ksn->kqs", c_blocks, b_blocks, preferred_element_type=jnp.float32)
    step_dt = jax.nn.softplus(dt_raw + dt_bias)
    cum_decay = jnp.cumsum((-step_dt * decay_rate).reshape(block_count, BLOCK, heads_here), axis=1)
    dt_blocks = step_dt.reshape(block_count, BLOCK, heads_here)
    x_blocks = inputs_x.reshape(block_count, BLOCK, heads_here, head_dim)
    positions = jnp.arange(BLOCK)
    causal = positions[:, None] >= positions[None, :]
    cum_heads = jnp.moveaxis(cum_decay, 2, 1)
    dt_heads = jnp.moveaxis(dt_blocks, 2, 1)
    spread = cum_heads[:, :, :, None] - cum_heads[:, :, None, :]
    weights = (
        gram_mat[:, None]
        * jnp.exp(jnp.where(causal[None, None], spread, -jnp.inf))
        * dt_heads[:, :, None, :]
    ).astype(jnp.bfloat16)
    inside = jnp.einsum("khqs,kshp->kqhp", weights, x_blocks, preferred_element_type=jnp.float32)
    to_end = jnp.exp(cum_decay[:, -1:, :] - cum_decay) * dt_blocks
    scaled = (x_blocks.astype(jnp.float32) * to_end[:, :, :, None]).astype(jnp.bfloat16)
    block_ends = jnp.einsum("kqhp,kqn->khpn", scaled, b_blocks, preferred_element_type=jnp.float32)
    block_decay = cum_decay[:, -1, :]

    starts_local = jnp.stack(
        [weighted_prefix(block_ends, block_decay, k) for k in range(block_count)]
    )
    local_end = weighted_prefix(block_ends, block_decay, block_count)
    device_decay = jnp.sum(block_decay, axis=0)
    incoming = carried_in(device_decay, local_end, "scan")
    prior_decay = jnp.concatenate(
        [jnp.zeros((1, heads_here), jnp.float32), jnp.cumsum(block_decay, axis=0)[:-1]], axis=0
    )
    starts = jnp.exp(prior_decay)[:, :, None, None] * incoming[None] + starts_local
    carried = jnp.einsum(
        "kqn,khpn->kqhp", c_blocks.astype(jnp.float32), starts, precision=lax.Precision.HIGHEST
    )
    mixed_out = inside + jnp.exp(cum_decay)[:, :, :, None] * carried
    gated_out = mixed_out.reshape(length, heads_here, head_dim) * jax.nn.silu(gate_vals)
    normed = (
        (gated_out * lax.rsqrt(jnp.mean(gated_out * gated_out, axis=2, keepdims=True) + EPSILON))
        .astype(jnp.bfloat16)
        .reshape(length, heads_here * head_dim)
    )
    summed_out = jnp.dot(
        jnp.moveaxis(gather_heads(normed), 0, 1).reshape(length, inner * normed.shape[1]),
        w_out,
        preferred_element_type=jnp.float32,
    )
    return (stream.astype(jnp.float32) + summed_out).astype(jnp.bfloat16)


def local(stream, w_xz, w_bc, w_dt, dt_bias, decay_rate, conv_x, conv_bc, w_out):
    xz_cols = w_xz.shape[2]
    first, second = regroup_shared(w_xz, w_dt)
    layer = lambda u, l, weights: mix_layer(
        u, weights, xz_cols, w_bc[l], dt_bias[l], decay_rate[l], conv_x[l], conv_bc[l], w_out[l]
    )
    raster_out = layer(stream, 0, first)
    members = lax.axis_size("scan")
    length = raster_out.shape[0]
    columns = raster_out.shape[1]
    grouped = raster_out.reshape(members, length // members, 1, columns)
    exchanged = lax.all_to_all(grouped, "scan", split_axis=0, concat_axis=2, tiled=True)
    return layer(exchanged.reshape(length, columns), 1, second)


def solution(mesh):
    placed = (
        P("scan", "head"),
        P(None, None, "head"),
        P(),
        P(None, None, "head"),
        P(None, "head"),
        P(None, "head"),
        P(None, None, "head"),
        P(),
        P(None, None, "head"),
    )
    return jax.shard_map(
        local, mesh=mesh, in_specs=placed, out_specs=P("scan", "head"), check_vma=False
    )
```

```python
import jax
import jax.numpy as jnp
from jax import lax
from jax.sharding import PartitionSpec as P

BLOCK = 256


EPSILON = 1e-05


def from_behind(shard, axis, by):
    devices = lax.axis_size(axis)
    pairs = [(i, i + by) for i in range(devices) if 0 <= i + by < devices]
    return lax.ppermute(shard, axis, pairs)


def weighted_prefix(states, decays, place):
    order = jnp.arange(states.shape[0])
    between = (order[:, None] < order[None, :]) & (order[None, :] < place)
    span = jnp.sum(jnp.where(between[:, :, None], decays[None, :, :], 0.0), axis=1)
    scale = jnp.where((order < place)[:, None], jnp.exp(span), 0.0)
    return jnp.sum(scale[:, :, None, None] * states, axis=0)


def carried_in(decay, state, axis):
    members = lax.axis_size(axis)
    heads, rows, cols = state.shape
    decay_row = jnp.zeros((1, cols), jnp.float32).at[0, :heads].set(decay)
    packed = jnp.concatenate([state.reshape(heads * rows, cols), decay_row], axis=0)
    gathered = lax.all_gather(packed.astype(jnp.bfloat16), axis).astype(jnp.float32)
    states = gathered[:, : heads * rows].reshape(members, heads, rows, cols)
    decays = gathered[:, heads * rows, :heads]
    return weighted_prefix(states, decays, lax.axis_index(axis))


def causal_conv(rim_rows, pre_conv, kernel):
    padded = jnp.concatenate([rim_rows, pre_conv], axis=0).astype(jnp.float32)
    length = pre_conv.shape[0]
    summed = jnp.zeros(pre_conv.shape, jnp.float32)
    for offset in range(kernel.shape[0]):
        summed = summed + kernel[offset] * padded[offset : offset + length]
    return jax.nn.silu(summed).astype(jnp.bfloat16)


def split_pair(values):
    high = values.astype(jnp.bfloat16)
    low = (values - high.astype(jnp.float32)).astype(jnp.bfloat16)
    return high, low


def regroup(w_xz, w_dt):
    inner = lax.axis_size("head")
    layers, features, _ = w_xz.shape
    packed = jnp.concatenate([w_xz, w_dt], axis=2)
    split = packed.reshape(layers, inner, features // inner, packed.shape[2])
    return lax.all_to_all(jnp.swapaxes(split, 2, 3), "head", 1, 1)


def regroup_shared(w_xz, w_dt):
    members = lax.axis_size("scan")
    core = lax.axis_index("scan") % 2
    own = regroup(
        jnp.where(core == 0, w_xz[:1], w_xz[1:2]), jnp.where(core == 0, w_dt[:1], w_dt[1:2])
    )[0]
    pairs = [(i, i ^ 1) for i in range(members)]
    other = lax.ppermute(own, "scan", pairs)
    return jnp.where(core == 0, own, other), jnp.where(core == 0, other, own)


def gather_heads(values):
    inner = lax.axis_size("head")
    me = lax.axis_index("head")
    pieces = [values] + [
        lax.ppermute(values, "head", [(i, (i + shift) % inner) for i in range(inner)])
        for shift in range(1, inner)
    ]
    flipped = jnp.stack(pieces[::-1])
    doubled = jnp.concatenate([flipped, flipped], axis=0)
    return lax.dynamic_slice_in_dim(doubled, inner - 1 - me, inner, 0)


def mix_layer(stream, regrouped, xz_cols, w_bc, dt_bias, decay_rate, conv_x, conv_bc, w_out):
    length, piece = stream.shape
    inner = lax.axis_size("head")
    spot = lax.axis_index("head")
    feature_count = piece * inner
    heads_here = regrouped.shape[1] - xz_cols
    head_dim = xz_cols // (2 * heads_here)
    state_dim = w_bc.shape[1] // 2
    taps = conv_x.shape[0]
    rows_bc = lax.dynamic_slice_in_dim(w_bc, spot * piece, piece, 0)
    slice_bc = 2 * state_dim // inner
    combined = jnp.concatenate(
        [
            regrouped[:, :xz_cols],
            jnp.transpose(rows_bc.reshape(piece, inner, slice_bc), (1, 2, 0)),
            regrouped[:, xz_cols:],
        ],
        axis=1,
    )
    partial = jnp.einsum("tf,gcf->gtc", stream, combined, preferred_element_type=jnp.float32)
    wide_piece = stream.astype(jnp.float32)
    square_high, square_low = split_pair(jnp.sum(wide_piece * wide_piece, axis=1))
    squares = jnp.broadcast_to(
        jnp.stack([square_high, square_low], axis=1)[None], (inner, length, 2)
    )
    step_high, step_low = split_pair(partial[:, :, xz_cols + slice_bc :])
    outgoing = jnp.concatenate(
        [partial[:, :, : xz_cols + slice_bc].astype(jnp.bfloat16), step_high, step_low, squares],
        axis=2,
    )
    arrived = lax.all_to_all(outgoing, "head", 0, 0).astype(jnp.float32)
    summed = jnp.sum(arrived, axis=0)
    summed_xz = summed[:, :xz_cols]
    summed_bc = summed[:, xz_cols : xz_cols + slice_bc]
    at = xz_cols + slice_bc
    dt_sum = summed[:, at : at + heads_here] + summed[:, at + heads_here : at + 2 * heads_here]
    square_sum = summed[:, at + 2 * heads_here :].sum(axis=1, keepdims=True)
    row_scale = lax.rsqrt(square_sum / feature_count + EPSILON)
    proj_xz = (
        (summed_xz.astype(jnp.float32) * row_scale)
        .astype(jnp.bfloat16)
        .reshape(length, heads_here, 2, head_dim)
    )
    proj_bc = (summed_bc * row_scale).astype(jnp.bfloat16)
    dt_raw = dt_sum * row_scale
    pre_x = proj_xz[:, :, 0, :].reshape(length, heads_here * head_dim)
    gate_vals = proj_xz[:, :, 1, :].astype(jnp.float32)
    rims = from_behind(
        jnp.concatenate([pre_x[length - taps + 1 :], proj_bc[length - taps + 1 :]], axis=1),
        "scan",
        1,
    )
    rim_x, rim_bc = rims[:, : pre_x.shape[1]], rims[:, pre_x.shape[1] :]
    inputs_x = causal_conv(rim_x, pre_x, conv_x)
    taps_bc = lax.dynamic_slice_in_dim(conv_bc, spot * slice_bc, slice_bc, 1)
    conv_slice = causal_conv(rim_bc, proj_bc, taps_bc)
    conv_out = jnp.moveaxis(gather_heads(conv_slice), 0, 1).reshape(length, 2 * state_dim)
    block_count = length // BLOCK
    b_blocks = conv_out[:, :state_dim].reshape(block_count, BLOCK, state_dim)
    c_blocks = conv_out[:, state_dim:].reshape(block_count, BLOCK, state_dim)
    gram_mat = jnp.einsum("kqn,ksn->kqs", c_blocks, b_blocks, preferred_element_type=jnp.float32)
    step_dt = jax.nn.softplus(dt_raw + dt_bias)
    cum_decay = jnp.cumsum((-step_dt * decay_rate).reshape(block_count, BLOCK, heads_here), axis=1)
    dt_blocks = step_dt.reshape(block_count, BLOCK, heads_here)
    x_blocks = inputs_x.reshape(block_count, BLOCK, heads_here, head_dim)
    positions = jnp.arange(BLOCK)
    causal = positions[:, None] >= positions[None, :]
    cum_heads = jnp.moveaxis(cum_decay, 2, 1)
    dt_heads = jnp.moveaxis(dt_blocks, 2, 1)
    spread = cum_heads[:, :, :, None] - cum_heads[:, :, None, :]
    weights = (
        gram_mat[:, None]
        * jnp.exp(jnp.where(causal[None, None], spread, -jnp.inf))
        * dt_heads[:, :, None, :]
    ).astype(jnp.bfloat16)
    inside = jnp.einsum("khqs,kshp->kqhp", weights, x_blocks, preferred_element_type=jnp.float32)
    to_end = jnp.exp(cum_decay[:, -1:, :] - cum_decay) * dt_blocks
    scaled = (x_blocks.astype(jnp.float32) * to_end[:, :, :, None]).astype(jnp.bfloat16)
    block_ends = jnp.einsum("kqhp,kqn->khpn", scaled, b_blocks, preferred_element_type=jnp.float32)
    block_decay = cum_decay[:, -1, :]

    starts_local = jnp.stack(
        [weighted_prefix(block_ends, block_decay, k) for k in range(block_count)]
    )
    local_end = weighted_prefix(block_ends, block_decay, block_count)
    device_decay = jnp.sum(block_decay, axis=0)
    incoming = carried_in(device_decay, local_end, "scan")
    prior_decay = jnp.concatenate(
        [jnp.zeros((1, heads_here), jnp.float32), jnp.cumsum(block_decay, axis=0)[:-1]], axis=0
    )
    starts = jnp.exp(prior_decay)[:, :, None, None] * incoming[None] + starts_local
    carried = jnp.einsum(
        "kqn,khpn->kqhp", c_blocks.astype(jnp.float32), starts, precision=lax.Precision.HIGHEST
    )
    mixed_out = inside + jnp.exp(cum_decay)[:, :, :, None] * carried
    gated_out = mixed_out.reshape(length, heads_here, head_dim) * jax.nn.silu(gate_vals)
    normed = (
        (gated_out * lax.rsqrt(jnp.mean(gated_out * gated_out, axis=2, keepdims=True) + EPSILON))
        .astype(jnp.bfloat16)
        .reshape(length, heads_here * head_dim)
    )
    summed_out = jnp.dot(
        jnp.moveaxis(gather_heads(normed), 0, 1).reshape(length, inner * normed.shape[1]),
        w_out,
        preferred_element_type=jnp.float32,
    )
    return (stream.astype(jnp.float32) + summed_out).astype(jnp.bfloat16)


def local(stream, w_xz, w_bc, w_dt, dt_bias, decay_rate, conv_x, conv_bc, w_out):
    xz_cols = w_xz.shape[2]
    first, second = regroup_shared(w_xz, w_dt)
    layer = lambda u, l, weights: mix_layer(
        u, weights, xz_cols, w_bc[l], dt_bias[l], decay_rate[l], conv_x[l], conv_bc[l], w_out[l]
    )
    raster_out = layer(stream, 0, first)
    members = lax.axis_size("scan")
    length = raster_out.shape[0]
    columns = raster_out.shape[1]
    grouped = raster_out.reshape(members, length // members, 1, columns)
    exchanged = lax.all_to_all(grouped, "scan", split_axis=0, concat_axis=2, tiled=True)
    return layer(exchanged.reshape(length, columns), 1, second)


def solution(mesh):
    placed = (
        P("scan", "head"),
        P(None, None, "head"),
        P(),
        P(None, None, "head"),
        P(None, "head"),
        P(None, "head"),
        P(None, None, "head"),
        P(),
        P(None, None, "head"),
    )
    return jax.shard_map(
        local, mesh=mesh, in_specs=placed, out_specs=P("scan", "head"), check_vma=False
    )
```

```python
import jax
import jax.numpy as jnp
from jax import lax
from jax.sharding import PartitionSpec as P

BLOCK = 256


EPSILON = 1e-05


def from_behind(shard, axis, by):
    devices = lax.axis_size(axis)
    pairs = [(i, i + by) for i in range(devices) if 0 <= i + by < devices]
    return lax.ppermute(shard, axis, pairs)


def weighted_prefix(states, decays, place):
    order = jnp.arange(states.shape[0])
    between = (order[:, None] < order[None, :]) & (order[None, :] < place)
    span = jnp.sum(jnp.where(between[:, :, None], decays[None, :, :], 0.0), axis=1)
    scale = jnp.where((order < place)[:, None], jnp.exp(span), 0.0)
    return jnp.sum(scale[:, :, None, None] * states, axis=0)


def carried_in(decay, state, axis):
    members = lax.axis_size(axis)
    heads, rows, cols = state.shape
    decay_row = jnp.zeros((1, cols), jnp.float32).at[0, :heads].set(decay)
    packed = jnp.concatenate([state.reshape(heads * rows, cols), decay_row], axis=0)
    gathered = lax.all_gather(packed.astype(jnp.bfloat16), axis).astype(jnp.float32)
    states = gathered[:, : heads * rows].reshape(members, heads, rows, cols)
    decays = gathered[:, heads * rows, :heads]
    return weighted_prefix(states, decays, lax.axis_index(axis))


def causal_conv(rim_rows, pre_conv, kernel):
    padded = jnp.concatenate([rim_rows, pre_conv], axis=0).astype(jnp.float32)
    length = pre_conv.shape[0]
    summed = jnp.zeros(pre_conv.shape, jnp.float32)
    for offset in range(kernel.shape[0]):
        summed = summed + kernel[offset] * padded[offset : offset + length]
    return jax.nn.silu(summed).astype(jnp.bfloat16)


def split_pair(values):
    high = values.astype(jnp.bfloat16)
    low = (values - high.astype(jnp.float32)).astype(jnp.bfloat16)
    return high, low


def regroup(w_xz, w_dt):
    inner = lax.axis_size("head")
    layers, features, _ = w_xz.shape
    packed = jnp.concatenate([w_xz, w_dt], axis=2)
    split = packed.reshape(layers, inner, features // inner, packed.shape[2])
    return lax.all_to_all(split, "head", 1, 1)


def regroup_shared(w_xz, w_dt):
    members = lax.axis_size("scan")
    core = lax.axis_index("scan") % 2
    own = regroup(
        jnp.where(core == 0, w_xz[:1], w_xz[1:2]), jnp.where(core == 0, w_dt[:1], w_dt[1:2])
    )[0]
    pairs = [(i, i ^ 1) for i in range(members)]
    other = lax.ppermute(own, "scan", pairs)
    return jnp.where(core == 0, own, other), jnp.where(core == 0, other, own)


def gather_heads(values):
    inner = lax.axis_size("head")
    me = lax.axis_index("head")
    pieces = [values] + [
        lax.ppermute(values, "head", [(i, (i + shift) % inner) for i in range(inner)])
        for shift in range(1, inner)
    ]
    flipped = jnp.stack(pieces[::-1])
    doubled = jnp.concatenate([flipped, flipped], axis=0)
    return lax.dynamic_slice_in_dim(doubled, inner - 1 - me, inner, 0)


def mix_layer(stream, regrouped, xz_cols, w_bc, dt_bias, decay_rate, conv_x, conv_bc, w_out):
    length, piece = stream.shape
    inner = lax.axis_size("head")
    spot = lax.axis_index("head")
    feature_count = piece * inner
    heads_here = regrouped.shape[2] - xz_cols
    head_dim = xz_cols // (2 * heads_here)
    state_dim = w_bc.shape[1] // 2
    taps = conv_x.shape[0]
    rows_bc = lax.dynamic_slice_in_dim(w_bc, spot * piece, piece, 0)
    slice_bc = 2 * state_dim // inner
    combined = jnp.concatenate(
        [
            regrouped[:, :, :xz_cols],
            jnp.moveaxis(rows_bc.reshape(piece, inner, slice_bc), 1, 0),
            regrouped[:, :, xz_cols:],
        ],
        axis=2,
    )
    partial = jnp.einsum("tf,gfc->gtc", stream, combined, preferred_element_type=jnp.float32)
    wide_piece = stream.astype(jnp.float32)
    square_high, square_low = split_pair(jnp.sum(wide_piece * wide_piece, axis=1))
    squares = jnp.broadcast_to(
        jnp.stack([square_high, square_low], axis=1)[None], (inner, length, 2)
    )
    step_high, step_low = split_pair(partial[:, :, xz_cols + slice_bc :])
    outgoing = jnp.concatenate(
        [partial[:, :, : xz_cols + slice_bc].astype(jnp.bfloat16), step_high, step_low, squares],
        axis=2,
    )
    arrived = lax.all_to_all(outgoing, "head", 0, 0).astype(jnp.float32)
    summed = jnp.sum(arrived, axis=0)
    summed_xz = summed[:, :xz_cols]
    summed_bc = summed[:, xz_cols : xz_cols + slice_bc]
    at = xz_cols + slice_bc
    dt_sum = summed[:, at : at + heads_here] + summed[:, at + heads_here : at + 2 * heads_here]
    square_sum = summed[:, at + 2 * heads_here :].sum(axis=1, keepdims=True)
    row_scale = lax.rsqrt(square_sum / feature_count + EPSILON)
    proj_xz = (
        (summed_xz.astype(jnp.float32) * row_scale)
        .astype(jnp.bfloat16)
        .reshape(length, heads_here, 2, head_dim)
    )
    proj_bc = (summed_bc * row_scale).astype(jnp.bfloat16)
    dt_raw = dt_sum * row_scale
    pre_x = proj_xz[:, :, 0, :].reshape(length, heads_here * head_dim)
    gate_vals = proj_xz[:, :, 1, :].astype(jnp.float32)
    rims = from_behind(
        jnp.concatenate([pre_x[length - taps + 1 :], proj_bc[length - taps + 1 :]], axis=1),
        "scan",
        1,
    )
    rim_x, rim_bc = rims[:, : pre_x.shape[1]], rims[:, pre_x.shape[1] :]
    inputs_x = causal_conv(rim_x, pre_x, conv_x)
    taps_bc = lax.dynamic_slice_in_dim(conv_bc, spot * slice_bc, slice_bc, 1)
    conv_slice = causal_conv(rim_bc, proj_bc, taps_bc)
    conv_out = jnp.moveaxis(gather_heads(conv_slice), 0, 1).reshape(length, 2 * state_dim)
    block_count = length // BLOCK
    b_blocks = conv_out[:, :state_dim].reshape(block_count, BLOCK, state_dim)
    c_blocks = conv_out[:, state_dim:].reshape(block_count, BLOCK, state_dim)
    gram_mat = jnp.einsum("kqn,ksn->kqs", c_blocks, b_blocks, preferred_element_type=jnp.float32)
    step_dt = jax.nn.softplus(dt_raw + dt_bias)
    cum_decay = jnp.cumsum((-step_dt * decay_rate).reshape(block_count, BLOCK, heads_here), axis=1)
    dt_blocks = step_dt.reshape(block_count, BLOCK, heads_here)
    x_blocks = inputs_x.reshape(block_count, BLOCK, heads_here, head_dim)
    positions = jnp.arange(BLOCK)
    causal = positions[:, None] >= positions[None, :]
    cum_heads = jnp.moveaxis(cum_decay, 2, 1)
    dt_heads = jnp.moveaxis(dt_blocks, 2, 1)
    spread = cum_heads[:, :, :, None] - cum_heads[:, :, None, :]
    weights = (
        gram_mat[:, None]
        * jnp.exp(jnp.where(causal[None, None], spread, -jnp.inf))
        * dt_heads[:, :, None, :]
    ).astype(jnp.bfloat16)
    inside = jnp.einsum("khqs,kshp->kqhp", weights, x_blocks, preferred_element_type=jnp.float32)
    to_end = jnp.exp(cum_decay[:, -1:, :] - cum_decay) * dt_blocks
    scaled = (x_blocks.astype(jnp.float32) * to_end[:, :, :, None]).astype(jnp.bfloat16)
    block_ends = jnp.einsum("kqhp,kqn->khpn", scaled, b_blocks, preferred_element_type=jnp.float32)
    block_decay = cum_decay[:, -1, :]

    starts_local = jnp.stack(
        [weighted_prefix(block_ends, block_decay, k) for k in range(block_count)]
    )
    local_end = weighted_prefix(block_ends, block_decay, block_count)
    device_decay = jnp.sum(block_decay, axis=0)
    incoming = carried_in(device_decay, local_end, "scan")
    prior_decay = jnp.concatenate(
        [jnp.zeros((1, heads_here), jnp.float32), jnp.cumsum(block_decay, axis=0)[:-1]], axis=0
    )
    starts = jnp.exp(prior_decay)[:, :, None, None] * incoming[None] + starts_local
    carried = jnp.einsum(
        "kqn,khpn->kqhp", c_blocks.astype(jnp.float32), starts, precision=lax.Precision.HIGHEST
    )
    mixed_out = inside + jnp.exp(cum_decay)[:, :, :, None] * carried
    gated_out = mixed_out.reshape(length, heads_here, head_dim) * jax.nn.silu(gate_vals)
    normed = (
        (gated_out * lax.rsqrt(jnp.mean(gated_out * gated_out, axis=2, keepdims=True) + EPSILON))
        .astype(jnp.bfloat16)
        .reshape(length, heads_here * head_dim)
    )
    summed_out = jnp.dot(
        jnp.moveaxis(gather_heads(normed), 0, 1).reshape(length, inner * normed.shape[1]),
        w_out,
        preferred_element_type=jnp.float32,
    )
    return (stream.astype(jnp.float32) + summed_out).astype(jnp.bfloat16)


def local(stream, w_xz, w_bc, w_dt, dt_bias, decay_rate, conv_x, conv_bc, w_out):
    xz_cols = w_xz.shape[2]
    first, second = regroup_shared(w_xz, w_dt)
    layer = lambda u, l, weights: mix_layer(
        u, weights, xz_cols, w_bc[l], dt_bias[l], decay_rate[l], conv_x[l], conv_bc[l], w_out[l]
    )
    raster_out = layer(stream, 0, first)
    members = lax.axis_size("scan")
    length = raster_out.shape[0]
    columns = raster_out.shape[1]
    grouped = raster_out.reshape(members, length // members, columns)
    exchanged = jnp.moveaxis(lax.all_to_all(grouped, "scan", 0, 0), 0, 1)
    return layer(exchanged.reshape(length, columns), 1, second)


def solution(mesh):
    placed = (
        P("scan", "head"),
        P(None, None, "head"),
        P(),
        P(None, None, "head"),
        P(None, "head"),
        P(None, "head"),
        P(None, None, "head"),
        P(),
        P(None, None, "head"),
    )
    return jax.shard_map(
        local, mesh=mesh, in_specs=placed, out_specs=P("scan", "head"), check_vma=False
    )
```

```python
import jax
import jax.numpy as jnp
from jax import lax
from jax.sharding import PartitionSpec as P

BLOCK = 256


EPSILON = 1e-05


def from_behind(shard, axis, by):
    devices = lax.axis_size(axis)
    pairs = [(i, i + by) for i in range(devices) if 0 <= i + by < devices]
    return lax.ppermute(shard, axis, pairs)


def weighted_prefix(states, decays, place):
    order = jnp.arange(states.shape[0])
    between = (order[:, None] < order[None, :]) & (order[None, :] < place)
    span = jnp.sum(jnp.where(between[:, :, None], decays[None, :, :], 0.0), axis=1)
    scale = jnp.where((order < place)[:, None], jnp.exp(span), 0.0)
    return jnp.sum(scale[:, :, None, None] * states, axis=0)


def carried_in(decay, state, axis):
    members = lax.axis_size(axis)
    heads, rows, cols = state.shape
    decay_row = jnp.zeros((1, cols), jnp.float32).at[0, :heads].set(decay)
    packed = jnp.concatenate([state.reshape(heads * rows, cols), decay_row], axis=0)
    gathered = lax.all_gather(packed.astype(jnp.bfloat16), axis).astype(jnp.float32)
    states = gathered[:, : heads * rows].reshape(members, heads, rows, cols)
    decays = gathered[:, heads * rows, :heads]
    return weighted_prefix(states, decays, lax.axis_index(axis))


def causal_conv(rim_rows, pre_conv, kernel):
    padded = jnp.concatenate([rim_rows, pre_conv], axis=0).astype(jnp.float32)
    length = pre_conv.shape[0]
    summed = jnp.zeros(pre_conv.shape, jnp.float32)
    for offset in range(kernel.shape[0]):
        summed = summed + kernel[offset] * padded[offset : offset + length]
    return jax.nn.silu(summed).astype(jnp.bfloat16)


def split_pair(values):
    high = values.astype(jnp.bfloat16)
    low = (values - high.astype(jnp.float32)).astype(jnp.bfloat16)
    return high, low


def regroup(w_xz, w_dt):
    inner = lax.axis_size("head")
    layers, features, _ = w_xz.shape
    packed = jnp.concatenate([w_xz, w_dt], axis=2)
    split = packed.reshape(layers, inner, features // inner, packed.shape[2])
    return lax.all_to_all(split, "head", 1, 1)


def regroup_shared(w_xz, w_dt):
    members = lax.axis_size("scan")
    core = lax.axis_index("scan") % 2
    own = regroup(
        lax.dynamic_slice_in_dim(w_xz, core, 1, 0), lax.dynamic_slice_in_dim(w_dt, core, 1, 0)
    )[0]
    pairs = [(i, i ^ 1) for i in range(members)]
    other = lax.ppermute(own, "scan", pairs)
    return jnp.where(core == 0, own, other), jnp.where(core == 0, other, own)


def gather_heads(values):
    inner = lax.axis_size("head")
    me = lax.axis_index("head")
    pieces = [values] + [
        lax.ppermute(values, "head", [(i, (i + shift) % inner) for i in range(inner)])
        for shift in range(1, inner)
    ]
    flipped = jnp.stack(pieces[::-1])
    doubled = jnp.concatenate([flipped, flipped], axis=0)
    return lax.dynamic_slice_in_dim(doubled, inner - 1 - me, inner, 0)


def mix_layer(stream, regrouped, xz_cols, w_bc, dt_bias, decay_rate, conv_x, conv_bc, w_out):
    length, piece = stream.shape
    inner = lax.axis_size("head")
    spot = lax.axis_index("head")
    feature_count = piece * inner
    heads_here = regrouped.shape[2] - xz_cols
    head_dim = xz_cols // (2 * heads_here)
    state_dim = w_bc.shape[1] // 2
    taps = conv_x.shape[0]
    rows_bc = lax.dynamic_slice_in_dim(w_bc, spot * piece, piece, 0)
    slice_bc = 2 * state_dim // inner
    combined = jnp.concatenate(
        [
            regrouped[:, :, :xz_cols],
            jnp.moveaxis(rows_bc.reshape(piece, inner, slice_bc), 1, 0),
            regrouped[:, :, xz_cols:],
        ],
        axis=2,
    )
    partial = jnp.einsum("tf,gfc->gtc", stream, combined, preferred_element_type=jnp.float32)
    wide_piece = stream.astype(jnp.float32)
    square_high, square_low = split_pair(jnp.sum(wide_piece * wide_piece, axis=1))
    squares = jnp.broadcast_to(
        jnp.stack([square_high, square_low], axis=1)[None], (inner, length, 2)
    )
    step_high, step_low = split_pair(partial[:, :, xz_cols + slice_bc :])
    outgoing = jnp.concatenate(
        [partial[:, :, : xz_cols + slice_bc].astype(jnp.bfloat16), step_high, step_low, squares],
        axis=2,
    )
    arrived = lax.all_to_all(outgoing, "head", 0, 0).astype(jnp.float32)
    summed = jnp.sum(arrived, axis=0)
    summed_xz = summed[:, :xz_cols]
    summed_bc = summed[:, xz_cols : xz_cols + slice_bc]
    at = xz_cols + slice_bc
    dt_sum = summed[:, at : at + heads_here] + summed[:, at + heads_here : at + 2 * heads_here]
    square_sum = summed[:, at + 2 * heads_here :].sum(axis=1, keepdims=True)
    row_scale = lax.rsqrt(square_sum / feature_count + EPSILON)
    proj_xz = (
        (summed_xz.astype(jnp.float32) * row_scale)
        .astype(jnp.bfloat16)
        .reshape(length, heads_here, 2, head_dim)
    )
    proj_bc = (summed_bc * row_scale).astype(jnp.bfloat16)
    dt_raw = dt_sum * row_scale
    pre_x = proj_xz[:, :, 0, :].reshape(length, heads_here * head_dim)
    gate_vals = proj_xz[:, :, 1, :].astype(jnp.float32)
    rims = from_behind(
        jnp.concatenate([pre_x[length - taps + 1 :], proj_bc[length - taps + 1 :]], axis=1),
        "scan",
        1,
    )
    rim_x, rim_bc = rims[:, : pre_x.shape[1]], rims[:, pre_x.shape[1] :]
    inputs_x = causal_conv(rim_x, pre_x, conv_x)
    taps_bc = lax.dynamic_slice_in_dim(conv_bc, spot * slice_bc, slice_bc, 1)
    conv_slice = causal_conv(rim_bc, proj_bc, taps_bc)
    conv_out = jnp.moveaxis(gather_heads(conv_slice), 0, 1).reshape(length, 2 * state_dim)
    block_count = length // BLOCK
    b_blocks = conv_out[:, :state_dim].reshape(block_count, BLOCK, state_dim)
    c_blocks = conv_out[:, state_dim:].reshape(block_count, BLOCK, state_dim)
    gram_mat = jnp.einsum("kqn,ksn->kqs", c_blocks, b_blocks, preferred_element_type=jnp.float32)
    step_dt = jax.nn.softplus(dt_raw + dt_bias)
    cum_decay = jnp.cumsum((-step_dt * decay_rate).reshape(block_count, BLOCK, heads_here), axis=1)
    dt_blocks = step_dt.reshape(block_count, BLOCK, heads_here)
    x_blocks = inputs_x.reshape(block_count, BLOCK, heads_here, head_dim)
    positions = jnp.arange(BLOCK)
    causal = positions[:, None] >= positions[None, :]
    cum_heads = jnp.moveaxis(cum_decay, 2, 1)
    dt_heads = jnp.moveaxis(dt_blocks, 2, 1)
    spread = cum_heads[:, :, :, None] - cum_heads[:, :, None, :]
    weights = (
        gram_mat[:, None]
        * jnp.exp(jnp.where(causal[None, None], spread, -jnp.inf))
        * dt_heads[:, :, None, :]
    ).astype(jnp.bfloat16)
    inside = jnp.einsum("khqs,kshp->kqhp", weights, x_blocks, preferred_element_type=jnp.float32)
    to_end = jnp.exp(cum_decay[:, -1:, :] - cum_decay) * dt_blocks
    scaled = (x_blocks.astype(jnp.float32) * to_end[:, :, :, None]).astype(jnp.bfloat16)
    block_ends = jnp.einsum("kqhp,kqn->khpn", scaled, b_blocks, preferred_element_type=jnp.float32)
    block_decay = cum_decay[:, -1, :]

    starts_local = jnp.stack(
        [weighted_prefix(block_ends, block_decay, k) for k in range(block_count)]
    )
    local_end = weighted_prefix(block_ends, block_decay, block_count)
    device_decay = jnp.sum(block_decay, axis=0)
    incoming = carried_in(device_decay, local_end, "scan")
    prior_decay = jnp.concatenate(
        [jnp.zeros((1, heads_here), jnp.float32), jnp.cumsum(block_decay, axis=0)[:-1]], axis=0
    )
    starts = jnp.exp(prior_decay)[:, :, None, None] * incoming[None] + starts_local
    carried = jnp.einsum(
        "kqn,khpn->kqhp", c_blocks.astype(jnp.float32), starts, precision=lax.Precision.HIGHEST
    )
    mixed_out = inside + jnp.exp(cum_decay)[:, :, :, None] * carried
    gated_out = mixed_out.reshape(length, heads_here, head_dim) * jax.nn.silu(gate_vals)
    normed = (
        (gated_out * lax.rsqrt(jnp.mean(gated_out * gated_out, axis=2, keepdims=True) + EPSILON))
        .astype(jnp.bfloat16)
        .reshape(length, heads_here * head_dim)
    )
    summed_out = jnp.dot(
        jnp.moveaxis(gather_heads(normed), 0, 1).reshape(length, inner * normed.shape[1]),
        w_out,
        preferred_element_type=jnp.float32,
    )
    return (stream.astype(jnp.float32) + summed_out).astype(jnp.bfloat16)


def local(stream, w_xz, w_bc, w_dt, dt_bias, decay_rate, conv_x, conv_bc, w_out):
    xz_cols = w_xz.shape[2]
    first, second = regroup_shared(w_xz, w_dt)
    layer = lambda u, l, weights: mix_layer(
        u, weights, xz_cols, w_bc[l], dt_bias[l], decay_rate[l], conv_x[l], conv_bc[l], w_out[l]
    )
    raster_out = layer(stream, 0, first)
    members = lax.axis_size("scan")
    length = raster_out.shape[0]
    columns = raster_out.shape[1]
    grouped = raster_out.reshape(members, length // members, 1, columns)
    exchanged = lax.all_to_all(grouped, "scan", split_axis=0, concat_axis=2, tiled=True)
    return layer(exchanged.reshape(length, columns), 1, second)


def solution(mesh):
    placed = (
        P("scan", "head"),
        P(None, None, "head"),
        P(),
        P(None, None, "head"),
        P(None, "head"),
        P(None, "head"),
        P(None, None, "head"),
        P(),
        P(None, None, "head"),
    )
    return jax.shard_map(
        local, mesh=mesh, in_specs=placed, out_specs=P("scan", "head"), check_vma=False
    )
```

```python
import jax
import jax.numpy as jnp
from jax import lax
from jax.sharding import PartitionSpec as P

BLOCK = 256


EPSILON = 1e-05


def from_behind(shard, axis, by):
    devices = lax.axis_size(axis)
    pairs = [(i, i + by) for i in range(devices) if 0 <= i + by < devices]
    return lax.ppermute(shard, axis, pairs)


def weighted_prefix(states, decays, place):
    order = jnp.arange(states.shape[0])
    between = (order[:, None] < order[None, :]) & (order[None, :] < place)
    span = jnp.sum(jnp.where(between[:, :, None], decays[None, :, :], 0.0), axis=1)
    scale = jnp.where((order < place)[:, None], jnp.exp(span), 0.0)
    return jnp.sum(scale[:, :, None, None] * states, axis=0)


def carried_in(decay, state, axis):
    members = lax.axis_size(axis)
    heads, rows, cols = state.shape
    decay_row = jnp.zeros((1, cols), jnp.float32).at[0, :heads].set(decay)
    packed = jnp.concatenate([state.reshape(heads * rows, cols), decay_row], axis=0)
    gathered = lax.all_gather(packed.astype(jnp.bfloat16), axis).astype(jnp.float32)
    states = gathered[:, : heads * rows].reshape(members, heads, rows, cols)
    decays = gathered[:, heads * rows, :heads]
    return weighted_prefix(states, decays, lax.axis_index(axis))


def causal_conv(rim_rows, pre_conv, kernel):
    padded = jnp.concatenate([rim_rows, pre_conv], axis=0).astype(jnp.float32)
    length = pre_conv.shape[0]
    summed = jnp.zeros(pre_conv.shape, jnp.float32)
    for offset in range(kernel.shape[0]):
        summed = summed + kernel[offset] * padded[offset : offset + length]
    return jax.nn.silu(summed).astype(jnp.bfloat16)


def split_pair(values):
    high = values.astype(jnp.bfloat16)
    low = (values - high.astype(jnp.float32)).astype(jnp.bfloat16)
    return high, low


def regroup(w_xz, w_dt):
    inner = lax.axis_size("head")
    layers, features, _ = w_xz.shape
    packed = jnp.concatenate([w_xz, w_dt], axis=2)
    split = packed.reshape(layers, inner, features // inner, packed.shape[2])
    return lax.all_to_all(split, "head", 1, 1)


def regroup_shared(w_xz, w_dt):
    members = lax.axis_size("scan")
    core = lax.axis_index("scan") % 2
    own = regroup(
        jnp.where(core == 0, w_xz[:1], w_xz[1:2]), jnp.where(core == 0, w_dt[:1], w_dt[1:2])
    )[0]
    pairs = [(i, i ^ 1) for i in range(members)]
    other = lax.ppermute(own, "scan", pairs)
    return jnp.where(core == 0, own, other), jnp.where(core == 0, other, own)


def gather_heads(values):
    inner = lax.axis_size("head")
    me = lax.axis_index("head")
    pieces = [values] + [
        lax.ppermute(values, "head", [(i, (i + shift) % inner) for i in range(inner)])
        for shift in range(1, inner)
    ]
    return jnp.concatenate(
        [lax.select_n((me - source) % inner, *pieces) for source in range(inner)], axis=1
    )


def mix_layer(stream, regrouped, xz_cols, w_bc, dt_bias, decay_rate, conv_x, conv_bc, w_out):
    length, piece = stream.shape
    inner = lax.axis_size("head")
    spot = lax.axis_index("head")
    feature_count = piece * inner
    heads_here = regrouped.shape[2] - xz_cols
    head_dim = xz_cols // (2 * heads_here)
    state_dim = w_bc.shape[1] // 2
    taps = conv_x.shape[0]
    rows_bc = lax.dynamic_slice_in_dim(w_bc, spot * piece, piece, 0)
    slice_bc = 2 * state_dim // inner
    combined = jnp.concatenate(
        [
            regrouped[:, :, :xz_cols],
            jnp.moveaxis(rows_bc.reshape(piece, inner, slice_bc), 1, 0),
            regrouped[:, :, xz_cols:],
        ],
        axis=2,
    )
    partial = jnp.einsum("tf,gfc->gtc", stream, combined, preferred_element_type=jnp.float32)
    wide_piece = stream.astype(jnp.float32)
    square_high, square_low = split_pair(jnp.sum(wide_piece * wide_piece, axis=1))
    squares = jnp.broadcast_to(
        jnp.stack([square_high, square_low], axis=1)[None], (inner, length, 2)
    )
    step_high, step_low = split_pair(partial[:, :, xz_cols + slice_bc :])
    outgoing = jnp.concatenate(
        [partial[:, :, : xz_cols + slice_bc].astype(jnp.bfloat16), step_high, step_low, squares],
        axis=2,
    )
    arrived = lax.all_to_all(outgoing, "head", 0, 0).astype(jnp.float32)
    summed = jnp.sum(arrived, axis=0)
    summed_xz = summed[:, :xz_cols]
    summed_bc = summed[:, xz_cols : xz_cols + slice_bc]
    at = xz_cols + slice_bc
    dt_sum = summed[:, at : at + heads_here] + summed[:, at + heads_here : at + 2 * heads_here]
    square_sum = summed[:, at + 2 * heads_here :].sum(axis=1, keepdims=True)
    row_scale = lax.rsqrt(square_sum / feature_count + EPSILON)
    proj_xz = (
        (summed_xz.astype(jnp.float32) * row_scale)
        .astype(jnp.bfloat16)
        .reshape(length, heads_here, 2, head_dim)
    )
    proj_bc = (summed_bc * row_scale).astype(jnp.bfloat16)
    dt_raw = dt_sum * row_scale
    pre_x = proj_xz[:, :, 0, :].reshape(length, heads_here * head_dim)
    gate_vals = proj_xz[:, :, 1, :].astype(jnp.float32)
    rims = from_behind(
        jnp.concatenate([pre_x[length - taps + 1 :], proj_bc[length - taps + 1 :]], axis=1),
        "scan",
        1,
    )
    rim_x, rim_bc = rims[:, : pre_x.shape[1]], rims[:, pre_x.shape[1] :]
    inputs_x = causal_conv(rim_x, pre_x, conv_x)
    taps_bc = lax.dynamic_slice_in_dim(conv_bc, spot * slice_bc, slice_bc, 1)
    conv_slice = causal_conv(rim_bc, proj_bc, taps_bc)
    conv_out = gather_heads(conv_slice)
    block_count = length // BLOCK
    b_blocks = conv_out[:, :state_dim].reshape(block_count, BLOCK, state_dim)
    c_blocks = conv_out[:, state_dim:].reshape(block_count, BLOCK, state_dim)
    gram_mat = jnp.einsum("kqn,ksn->kqs", c_blocks, b_blocks, preferred_element_type=jnp.float32)
    step_dt = jax.nn.softplus(dt_raw + dt_bias)
    cum_decay = jnp.cumsum((-step_dt * decay_rate).reshape(block_count, BLOCK, heads_here), axis=1)
    dt_blocks = step_dt.reshape(block_count, BLOCK, heads_here)
    x_blocks = inputs_x.reshape(block_count, BLOCK, heads_here, head_dim)
    positions = jnp.arange(BLOCK)
    causal = positions[:, None] >= positions[None, :]
    cum_heads = jnp.moveaxis(cum_decay, 2, 1)
    dt_heads = jnp.moveaxis(dt_blocks, 2, 1)
    spread = cum_heads[:, :, :, None] - cum_heads[:, :, None, :]
    weights = (
        gram_mat[:, None]
        * jnp.exp(jnp.where(causal[None, None], spread, -jnp.inf))
        * dt_heads[:, :, None, :]
    ).astype(jnp.bfloat16)
    inside = jnp.einsum("khqs,kshp->kqhp", weights, x_blocks, preferred_element_type=jnp.float32)
    to_end = jnp.exp(cum_decay[:, -1:, :] - cum_decay) * dt_blocks
    scaled = (x_blocks.astype(jnp.float32) * to_end[:, :, :, None]).astype(jnp.bfloat16)
    block_ends = jnp.einsum("kqhp,kqn->khpn", scaled, b_blocks, preferred_element_type=jnp.float32)
    block_decay = cum_decay[:, -1, :]

    starts_local = jnp.stack(
        [weighted_prefix(block_ends, block_decay, k) for k in range(block_count)]
    )
    local_end = weighted_prefix(block_ends, block_decay, block_count)
    device_decay = jnp.sum(block_decay, axis=0)
    incoming = carried_in(device_decay, local_end, "scan")
    prior_decay = jnp.concatenate(
        [jnp.zeros((1, heads_here), jnp.float32), jnp.cumsum(block_decay, axis=0)[:-1]], axis=0
    )
    starts = jnp.exp(prior_decay)[:, :, None, None] * incoming[None] + starts_local
    carried = jnp.einsum(
        "kqn,khpn->kqhp", c_blocks.astype(jnp.float32), starts, precision=lax.Precision.HIGHEST
    )
    mixed_out = inside + jnp.exp(cum_decay)[:, :, :, None] * carried
    gated_out = mixed_out.reshape(length, heads_here, head_dim) * jax.nn.silu(gate_vals)
    normed = (
        (gated_out * lax.rsqrt(jnp.mean(gated_out * gated_out, axis=2, keepdims=True) + EPSILON))
        .astype(jnp.bfloat16)
        .reshape(length, heads_here * head_dim)
    )
    summed_out = jnp.dot(
        gather_heads(normed),
        w_out,
        preferred_element_type=jnp.float32,
    )
    return (stream.astype(jnp.float32) + summed_out).astype(jnp.bfloat16)


def local(stream, w_xz, w_bc, w_dt, dt_bias, decay_rate, conv_x, conv_bc, w_out):
    xz_cols = w_xz.shape[2]
    first, second = regroup_shared(w_xz, w_dt)
    layer = lambda u, l, weights: mix_layer(
        u, weights, xz_cols, w_bc[l], dt_bias[l], decay_rate[l], conv_x[l], conv_bc[l], w_out[l]
    )
    raster_out = layer(stream, 0, first)
    members = lax.axis_size("scan")
    length = raster_out.shape[0]
    columns = raster_out.shape[1]
    grouped = raster_out.reshape(members, length // members, 1, columns)
    exchanged = lax.all_to_all(grouped, "scan", split_axis=0, concat_axis=2, tiled=True)
    return layer(exchanged.reshape(length, columns), 1, second)


def solution(mesh):
    placed = (
        P("scan", "head"),
        P(None, None, "head"),
        P(),
        P(None, None, "head"),
        P(None, "head"),
        P(None, "head"),
        P(None, None, "head"),
        P(),
        P(None, None, "head"),
    )
    return jax.shard_map(
        local, mesh=mesh, in_specs=placed, out_specs=P("scan", "head"), check_vma=False
    )
```
